128 devices in a mesh: row: 8 (over z, core), col: 16 (over y, x).
Axes of the slice: x: 4, y: 4, z: 4, core: 2. Of those that a mesh axis runs over, the one named last changes fastest.
Arguments:
- coeffs: float32 [2048, 3, 64, 128], P(('row', 'col')), may hold values from -0.18 to 0.18
- degree: int32 [2048], P(('row', 'col')), may hold values from 16 to 63
- material: float32 [2048, 2], P(('row', 'col')), may hold values from 0.2 to 2
- split_coeffs: float32 [512, 3, 64, 64], P(('row', 'col')), may hold values from -0.18 to 0.18
- split_material: float32 [256, 2], replicated, may hold values from 0.2 to 2
- separation: float32 [3, 2048, 8], P(None, ('row', 'col')), may hold values from -2.6 to 2.6, as said below
- reader_dev: int32 [2048, 8], P(('row', 'col')), may hold values from 0 to 127, all different within a row; in each aligned block of 16 rows (0 to 15, 16 to 31, ...) at most 2 rows name the same one
- reader_slot: int32 [2048, 8], P(('row', 'col')), may hold values from 0 to 15
Outputs:
- traction_coeffs: float32 [2048, 64, 128], P(('row', 'col'))
- split_traction: float32 [512, 64, 64], P(('row', 'col'))
- near_velocity: float32 [3, 8192], P(None, ('row', 'col'))
The draws below stay inside these ranges and needn't reach their ends.
Inputs may be any that keep to these rules, and one draw needn't show every extreme that they name: `reader_dev`: each ordinary drop names 8 different devices; among the drops of one device at most 2 name the same device, and some device is named exactly 2 times. Each entry's separation vector has a length between 1.9 and 2.6.
All inputs are finite; a program needn't handle non-finite values.
Results may differ from the reference program's by a relative error of at most 0.019.
Values may be sent and summed in bfloat16 or wider, within the bound.
No kernel may reach another device: no remote copies, remote signals or barrier semaphores. Data moves between devices by JAX's collectives and lax.ppermute only.
A program may use at most 128 MiB of HBM per device.

```python
import math
import jax
import jax.numpy as jnp
import numpy as np
from jax import lax

L = 64
MH = 32
NLAT = 64
NLON = 128
TPTS = 4
DROPS_DEV = 16
SPLIT_DEV = 4
READERS = 8
CAP = 2
DROPS = 2048
SPLIT_HALVES = 512
SPLIT_PAIRS = 256
N_ROW = 8
N_COL = 16
DEVICES = 128


def draw_separation(key, part):
    key_polar = jax.random.fold_in(key, 11)
    key_azimuth = jax.random.fold_in(key, 23)
    key_length = jax.random.fold_in(key, 37)
    cosine = jax.random.uniform(key_polar, (DROPS, READERS), jnp.float32, -1.0, 1.0)
    azimuth = jax.random.uniform(key_azimuth, (DROPS, READERS), jnp.float32, 0.0, 2.0 * math.pi)
    unit = jax.random.uniform(key_length, (DROPS, READERS), jnp.float32, 0.0, 1.0)
    length = 2.0 + 0.6 * unit
    planar = jnp.sqrt(jnp.maximum(1.0 - cosine * cosine, 0.0))
    return jnp.stack([length * planar * jnp.cos(azimuth), length * planar * jnp.sin(azimuth), length * cosine], axis=0)


def set_ends(values, stream_key, smallest, largest):
    dims = values.shape
    place = [jax.random.randint(jax.random.fold_in(stream_key, axis), (), 0, dims[axis]) for axis in range(len(dims))]
    values = values.at[tuple(place)].set(smallest)
    longest = dims.index(max(dims))
    place[longest] = (place[longest] + 1) % dims[longest]
    return values.at[tuple(place)].set(largest)


def level_of(own_key, shape, pieces, smallest, high):
    def one(dim, shards_of):
        draws = jax.random.uniform(jax.random.fold_in(jax.random.fold_in(own_key, 6), dim), (shards_of,), jnp.float32, smallest / len(pieces), high / len(pieces))
        return jnp.repeat(jnp.exp(draws), shape[dim] // shards_of).reshape((-1,) + (1,) * (len(shape) - dim - 1))

    factor_of = one(*pieces[0])
    for cut in pieces[1:]:
        factor_of = factor_of * one(*cut)
    return factor_of


def assign_block(key, own, number, rows, count, top, bound, lean):
    sequence = jax.random.permutation(key, count)
    crowded, usual = shares(count, rows * top, bound, lean, True), shares(count, rows * top, bound, lean, False)
    places = jnp.arange(count)

    def named(sizes, rotation):
        used = int((sizes > 0).sum())
        fixed = max(1, used // 4)
        moved = fixed + (places - fixed + rotation * (used - fixed)) % max(1, count - fixed)
        return jnp.zeros((count,), jnp.int32).at[sequence[jnp.where(places < fixed, places, moved)]].set(jnp.asarray(sizes, jnp.int32))

    sizes = jnp.where(number % 4 == 0, named(crowded, number // 4), named(usual, number - number // 4 - 1))
    mixed = jax.random.permutation(jax.random.fold_in(own, 3), count)
    donor, sink = mixed[0:count // 2 * 2:2], mixed[1:count // 2 * 2:2]
    slack = jnp.minimum(sizes[donor] - 1, bound - sizes[sink]) // 2
    slack = jnp.where((donor == sequence[0]) | (sink == sequence[0]) | (sizes[sink] == 0), 0, jnp.maximum(slack, 0))
    moved = jax.random.randint(jax.random.fold_in(own, 4), (count // 2,), 0, 1 << 20) % (slack + 1)
    sizes = sizes.at[donor].add(-moved).at[sink].add(moved)
    items = jnp.searchsorted(jnp.cumsum(sizes), jnp.arange(rows * top), side="right").astype(jnp.int32)
    listing = items.reshape(top, rows).T
    listing = listing[jax.random.permutation(jax.random.fold_in(own, 1), rows)]
    rotation = jax.random.randint(jax.random.fold_in(own, 2), (rows, 1), 0, top)
    return jnp.take_along_axis(listing, (jnp.arange(top)[None, :] + rotation) % top, axis=1)


def shares(amount, total, most, skew, full):
    weights = [(1 << 20) // math.isqrt(grade ** skew) + 1 for grade in range(1, amount + 1)]
    largest = most if full else min(most, max(-(-total // amount), total * weights[0] // sum(weights)))
    least = 1 if total - largest >= amount - 1 else 0
    holding, spare = [largest] + [least] * (amount - 1), total - largest - least * (amount - 1)
    while spare > 0:
        movable = [i for i in range(1, amount) if holding[i] < largest] or [i for i in range(1, amount) if holding[i] < most]
        mass, budget = sum([weights[i] for i in movable]), spare
        for i in movable:
            addition = min(most - holding[i], max(1, budget * weights[i] // mass), spare)
            holding[i] = holding[i] + addition
            spare = spare - addition
    return np.array(holding)


def centred(own_key, extent, spread, limit, split=(), kind=jnp.bfloat16):
    values = jax.random.normal(own_key, extent, jnp.float32) * spread
    if len(split) > 0:
        values = level_of(own_key, extent, split, -0.22, 0.18) * values
    return jnp.clip(values, min=-limit, max=limit).astype(kind)


def setup_inputs(seed: int = 0) -> dict:
    arg_keys = jax.random.split(jax.random.key(seed), 9)
    coeffs = centred(arg_keys[0], (DROPS, 3, L, 2 * L), 0.03, 0.18, ((0, 128),), jnp.float32)
    degree = set_ends(jax.random.randint(arg_keys[1], (DROPS,), L // 4, L), jax.random.fold_in(arg_keys[1], 1), L // 4, L - 1).astype(jnp.int32)
    material = jnp.clip(jnp.exp(math.log(2.0) - 2.3025851 * jax.random.uniform(arg_keys[2], (DROPS, 2), jnp.float32) ** level_of(arg_keys[2], (DROPS, 2), ((0, 128),), -0.2, 0.2)), 0.2, 2.0)
    split_coeffs = centred(arg_keys[3], (SPLIT_HALVES, 3, L, L), 0.03, 0.18, ((0, 128),), jnp.float32)
    split_material = jnp.clip(jnp.exp(jax.random.uniform(arg_keys[4], (SPLIT_PAIRS, 2), jnp.float32, math.log(0.2), math.log(2.0))), 0.2, 2.0)
    separation = draw_separation(jax.random.fold_in(arg_keys[8], 71), 0)
    reader_dev_keys = jax.random.split(jax.random.fold_in(arg_keys[6], 1), DROPS // DROPS_DEV)
    reader_dev_turns = jax.random.permutation(jax.random.fold_in(arg_keys[6], 3), DROPS // DROPS_DEV)
    reader_dev = jax.vmap(lambda own, number: assign_block(jax.random.fold_in(arg_keys[6], 2), own, number, DROPS_DEV, DEVICES, READERS, CAP, 2))(reader_dev_keys, reader_dev_turns).reshape((DROPS, READERS))
    reader_slot = set_ends(jax.random.randint(arg_keys[7], (DROPS, READERS), 0, DROPS_DEV), jax.random.fold_in(arg_keys[7], 1), 0, DROPS_DEV - 1).astype(jnp.int32)
    return {"coeffs": coeffs, "degree": degree, "material": material, "split_coeffs": split_coeffs, "split_material": split_material, "separation": separation, "reader_dev": reader_dev, "reader_slot": reader_slot}


HIGH = lax.Precision.HIGHEST
SOFTENING = 0.04

def spectral_tables(degrees):
    nlat = degrees
    nlon = 2 * degrees
    theta_lat = (np.arange(nlat) + 0.5) * (math.pi / nlat)
    cosine = np.cos(theta_lat)
    sine_theta = np.sin(theta_lat)
    legendre = np.zeros((degrees, nlat, degrees))
    for order in range(degrees):
        log_total = 0.0
        for step_index in range(1, order + 1):
            log_total = log_total + math.log((2.0 * step_index + 1.0) / (2.0 * step_index))
        diag_value = np.exp(0.5 * log_total + order * np.log(sine_theta)) / math.sqrt(4.0 * math.pi)
        legendre[order, :, order] = diag_value
        prev_two = diag_value
        if order + 1 < degrees:
            prev_one = math.sqrt(2.0 * order + 3.0) * cosine * diag_value
            legendre[order, :, order + 1] = prev_one
            for level in range(order + 2, degrees):
                alpha_term = math.sqrt((4.0 * level * level - 1.0) / (level * level - order * order))
                beta_term = math.sqrt(((level - 1.0) ** 2 - order * order) / (4.0 * (level - 1.0) ** 2 - 1.0))
                current = alpha_term * (cosine * prev_one - beta_term * prev_two)
                legendre[order, :, level] = current
                prev_two = prev_one
                prev_one = current
    order_index = np.arange(degrees)
    lon_index = np.arange(nlon)
    phase_angle = order_index[:, None] * lon_index[None, :] % nlon * (2.0 * math.pi / nlon)
    fourier = np.concatenate([np.cos(phase_angle), np.sin(phase_angle)], axis=0)
    quad_weight = sine_theta * (math.pi / nlat) * (2.0 * math.pi / nlon)
    longitude = lon_index * (2.0 * math.pi / nlon)
    normals = np.stack([sine_theta[:, None] * np.cos(longitude)[None, :], sine_theta[:, None] * np.sin(longitude)[None, :], cosine[:, None] * np.ones((1, nlon))], axis=0)
    return (jnp.asarray(legendre, dtype=jnp.float32), jnp.asarray(fourier, dtype=jnp.float32), jnp.asarray(quad_weight, dtype=jnp.float32), jnp.asarray(normals, dtype=jnp.float32))

def legendre_synth(coeff, legendre):
    batch_size, degrees, coef_width = coeff.shape
    orders = legendre.shape[0]
    parted = coeff.reshape(batch_size, degrees, 2, orders)
    return jnp.einsum('mjl,nlcm->njcm', legendre, parted, precision=HIGH)

def fourier_synth(partial_legendre, fourier_rows):
    batch_size, nlat, two, orders = partial_legendre.shape
    return jnp.einsum('njw,wk->njk', partial_legendre.reshape(batch_size, nlat, two * orders), fourier_rows, precision=HIGH)

def analysis_fourier(traction_grid, fourier, quad_weight):
    batch_size, nlat, nlon = traction_grid.shape
    projected = jnp.einsum('bjk,wk->bjw', traction_grid, fourier, precision=HIGH) * quad_weight[None, :, None]
    return projected.reshape(batch_size, nlat, 2, fourier.shape[0] // 2)

def analysis_legendre(coef_grid, legendre):
    batch_size = coef_grid.shape[0]
    result = jnp.einsum('mjl,bjcm->blcm', legendre, coef_grid, precision=HIGH)
    return result.reshape(batch_size, legendre.shape[2], 2 * legendre.shape[0])

def prepare(coeffs, keep_mask):
    degrees = coeffs.shape[2]
    degree_value = jnp.arange(degrees, dtype=jnp.float32)
    shape_part = coeffs[:, 0] * keep_mask
    curvature = shape_part * (degree_value * (degree_value + 1.0) / (degrees * degrees))[None, :, None]
    electric = 3.0 * coeffs[:, 1] * keep_mask
    viscous = 3.0 * coeffs[:, 2] * keep_mask * ((degree_value + 2.0) / degrees)[None, :, None]
    return jnp.stack([shape_part, curvature, electric, viscous], axis=1)

def traction(surface, material):
    radius = jnp.exp(surface[:, 0])
    traction_grid = material[:, 0, None, None] * surface[:, 1] + 0.5 * surface[:, 2] * surface[:, 2] + 2.0 * material[:, 1, None, None] * surface[:, 3]
    return (radius, traction_grid)

def drop_work(coeffs, keep_mask, material, legendre, fourier, quad_weight):
    batch_size, fields, degrees, coef_width = coeffs.shape
    prepared = prepare(coeffs, keep_mask)
    partial_legendre = legendre_synth(prepared.reshape(batch_size * 4, degrees, coef_width), legendre)
    surface = fourier_synth(partial_legendre, fourier)
    surface = surface.reshape(batch_size, 4, surface.shape[1], surface.shape[2])
    radius, traction_grid = traction(surface, material)
    result = analysis_legendre(analysis_fourier(traction_grid, fourier, quad_weight), legendre) * keep_mask
    return (result, radius, traction_grid)

def velocity_terms(radius, traction_grid, spacing, target_radius, cell_weight, cell_normal, target_normal):
    load_grid = traction_grid * radius * radius * cell_weight[None, :]
    target_point = spacing[:, :, None] + target_radius[None] * target_normal[:, None, :]
    surface_point = radius[None] * cell_normal[:, None, :]
    offset = target_point[:, :, :, None] - surface_point[:, :, None, :]
    distance_sq = lax.optimization_barrier(jnp.sum(offset * offset, axis=0))
    softened = distance_sq + SOFTENING
    weight = load_grid[:, None, :] / (softened * jnp.sqrt(softened))
    normal_dot = lax.optimization_barrier(jnp.sum(offset * cell_normal[:, None, None, :], axis=0))
    stokeslet = weight[None] * (cell_normal[:, None, None, :] * (distance_sq + 2.0 * SOFTENING)[None] + offset * normal_dot[None])
    return lax.optimization_barrier(jnp.sum(stokeslet, axis=3)) / (8.0 * math.pi)

def reference(coeffs, degree, material, split_coeffs, split_material, separation, reader_dev, reader_slot):
    legendre, fourier, quad_weight, normals = spectral_tables(L)
    degree_index = jnp.arange(L, dtype=jnp.int32)
    order_full = jnp.arange(2 * L, dtype=jnp.int32) % L
    order_mask = (degree_index[:, None] >= order_full[None, :]).astype(jnp.float32)

    def drop_block(block_args):
        block_coeffs, block_degree, block_material = block_args
        keep_mask = order_mask[None] * (degree_index[None, :, None] <= block_degree[:, None, None]).astype(jnp.float32)
        return drop_work(block_coeffs, keep_mask, block_material, legendre, fourier, quad_weight)
    result, radius, traction_grid = lax.map(drop_block, (coeffs.reshape(DEVICES, DROPS_DEV, 3, L, 2 * L), degree.reshape(DEVICES, DROPS_DEV), material.reshape(DEVICES, DROPS_DEV, 2)))
    traction_coeffs = result.reshape(DROPS, L, 2 * L)
    pair_view = split_coeffs.reshape(N_ROW // 2, 2, N_COL, SPLIT_DEV, 3, L, 2, MH)
    split_full = jnp.transpose(pair_view, (0, 2, 3, 4, 5, 6, 1, 7)).reshape(SPLIT_PAIRS, 3, L, 2 * L)
    split_result, split_radius, split_grid = drop_work(split_full, order_mask[None], split_material, legendre, fourier, quad_weight)
    split_back = split_result.reshape(N_ROW // 2, N_COL, SPLIT_DEV, L, 2, 2, MH)
    split_traction = jnp.transpose(split_back, (0, 5, 1, 2, 3, 4, 6)).reshape(SPLIT_HALVES, L, L)
    cell_count = NLAT * NLON
    cell_weight = jnp.broadcast_to(quad_weight[:, None], (NLAT, NLON)).reshape(cell_count)
    cell_normal = normals.reshape(3, cell_count)
    near_grid = jnp.stack([radius.reshape(DROPS, NLAT, NLON), traction_grid.reshape(DROPS, NLAT, NLON)], axis=1).astype(jnp.bfloat16)
    target_radius = near_grid[:, 0, NLAT // 4::NLAT // 2, ::NLON // 2].reshape(DROPS, TPTS)
    target_normal = normals[:, NLAT // 4::NLAT // 2, ::NLON // 2].reshape(3, TPTS)
    flat_grid = near_grid.reshape(DROPS, 2 * cell_count)
    sources = jnp.repeat(jnp.arange(DROPS, dtype=jnp.int32), READERS)
    targets = (reader_dev * DROPS_DEV + reader_slot).reshape(-1).astype(jnp.int32)
    pair_count = DROPS * READERS
    block_size = math.gcd(pair_count, 16)
    block_total = pair_count // block_size
    spacing_blocks = jnp.transpose(separation.reshape(3, block_total, block_size), (1, 0, 2))

    def near_block(block_args):
        block_source, block_target, block_spacing = block_args
        source_grid = flat_grid[block_source].astype(jnp.float32).reshape(block_size, 2, cell_count)
        return velocity_terms(source_grid[:, 0], source_grid[:, 1], block_spacing, target_radius[block_target].astype(jnp.float32), cell_weight, cell_normal, target_normal)
    velocity = lax.map(near_block, (sources.reshape(block_total, block_size), targets.reshape(block_total, block_size), spacing_blocks))
    velocity = jnp.transpose(velocity, (1, 0, 2, 3)).reshape(3, pair_count, TPTS)
    near_velocity = jnp.zeros((3, DROPS, TPTS), jnp.float32).at[:, targets].add(velocity).reshape(3, DROPS * TPTS)
    return (traction_coeffs, split_traction, near_velocity)
```

```python
import math

import jax
import jax.numpy as jnp
import numpy as np
from jax import lax
from jax.experimental import pallas as pl
from jax.experimental.pallas import tpu as pltpu
from jax.sharding import PartitionSpec as P

HIGH = lax.Precision.HIGHEST
SOFTENING = 0.04


def from_partner(block, axis, stride):
    count = lax.axis_size(axis)
    route = []
    for low in range(count):
        high = low | 1 << stride
        if high != low and high < count:
            route += [(low, high), (high, low)]
    return lax.ppermute(block, axis, route)


def spectral_tables(degrees):
    nlon = 2 * degrees
    theta_lat = (np.arange(degrees) + 0.5) * (math.pi / degrees)
    cosine = np.cos(theta_lat)
    sine_theta = np.sin(theta_lat)
    legendre = np.zeros((degrees, degrees, degrees))
    for order in range(degrees):
        log_total = 0.0
        for step_index in range(1, order + 1):
            log_total = log_total + math.log((2.0 * step_index + 1.0) / (2.0 * step_index))
        diag_value = np.exp(0.5 * log_total + order * np.log(sine_theta)) / math.sqrt(4.0 * math.pi)
        legendre[order, :, order] = diag_value
        prev_two = diag_value
        if order + 1 < degrees:
            prev_one = math.sqrt(2.0 * order + 3.0) * cosine * diag_value
            legendre[order, :, order + 1] = prev_one
            for level in range(order + 2, degrees):
                alpha_term = math.sqrt(
                    (4.0 * level * level - 1.0) / (level * level - order * order)
                )
                beta_term = math.sqrt(
                    ((level - 1.0) ** 2 - order * order) / (4.0 * (level - 1.0) ** 2 - 1.0)
                )
                current = alpha_term * (cosine * prev_one - beta_term * prev_two)
                legendre[order, :, level] = current
                prev_two = prev_one
                prev_one = current
    order_index = np.arange(degrees)
    lon_index = np.arange(nlon)
    phase_angle = order_index[:, None] * lon_index[None, :] % nlon * (2.0 * math.pi / nlon)
    fourier = np.concatenate([np.cos(phase_angle), np.sin(phase_angle)], axis=0)
    quad_weight = sine_theta * (math.pi / degrees) * (2.0 * math.pi / nlon)
    longitude = lon_index * (2.0 * math.pi / nlon)
    normals = np.stack(
        [
            sine_theta[:, None] * np.cos(longitude)[None, :],
            sine_theta[:, None] * np.sin(longitude)[None, :],
            cosine[:, None] * np.ones((1, nlon)),
        ],
        axis=0,
    )
    return (
        jnp.asarray(legendre, dtype=jnp.float32),
        jnp.asarray(fourier, dtype=jnp.float32),
        jnp.asarray(quad_weight, dtype=jnp.float32),
        jnp.asarray(normals, dtype=jnp.float32),
    )


def legendre_synth(coeff, legendre):
    batch_size, degrees, coef_width = coeff.shape
    orders = legendre.shape[0]
    parted = coeff.reshape(batch_size, degrees, 2, orders)
    return jnp.einsum("mjl,nlcm->njcm", legendre, parted, precision=HIGH)


def fourier_synth(partial_legendre, fourier_rows):
    batch_size, nlat, two, orders = partial_legendre.shape
    return jnp.einsum(
        "njw,wk->njk",
        partial_legendre.reshape(batch_size, nlat, two * orders),
        fourier_rows,
        precision=HIGH,
    )


def analysis_fourier(traction_grid, fourier, quad_weight):
    batch_size, nlat, nlon = traction_grid.shape
    projected = (
        jnp.einsum("bjk,wk->bjw", traction_grid, fourier, precision=HIGH)
        * quad_weight[None, :, None]
    )
    return projected.reshape(batch_size, nlat, 2, fourier.shape[0] // 2)


def analysis_legendre(coef_grid, legendre):
    batch_size = coef_grid.shape[0]
    result = jnp.einsum("mjl,bjcm->blcm", legendre, coef_grid, precision=HIGH)
    return result.reshape(batch_size, legendre.shape[2], 2 * legendre.shape[0])


def prepare(coeffs, keep_mask):
    degrees = coeffs.shape[2]
    degree_value = jnp.arange(degrees, dtype=jnp.float32)
    shape_part = coeffs[:, 0] * keep_mask
    curvature = (
        shape_part * (degree_value * (degree_value + 1.0) / (degrees * degrees))[None, :, None]
    )
    electric = 3.0 * coeffs[:, 1] * keep_mask
    viscous = 3.0 * coeffs[:, 2] * keep_mask * ((degree_value + 2.0) / degrees)[None, :, None]
    return jnp.stack([shape_part, curvature, electric, viscous], axis=1)


def traction(surface, material):
    radius = jnp.exp(surface[:, 0])
    traction_grid = (
        material[:, 0, None, None] * surface[:, 1]
        + 0.5 * surface[:, 2] * surface[:, 2]
        + 2.0 * material[:, 1, None, None] * surface[:, 3]
    )
    return (radius, traction_grid)


def velocity_terms(
    radius, traction_grid, spacing, target_radius, cell_weight, cell_normal, target_normal
):
    load_grid = traction_grid * radius * radius * cell_weight[None, :]
    target_point = spacing[:, :, None] + target_radius[None] * target_normal[:, None, :]
    surface_point = radius[None] * cell_normal[:, None, :]
    offset = target_point[:, :, :, None] - surface_point[:, :, None, :]
    distance_sq = jnp.sum(offset * offset, axis=0)
    softened = distance_sq + SOFTENING
    weight = load_grid[:, None, :] / (softened * jnp.sqrt(softened))
    normal_dot = jnp.sum(offset * cell_normal[:, None, None, :], axis=0)
    stokeslet = weight[None] * (
        cell_normal[:, None, None, :] * (distance_sq + 2.0 * SOFTENING)[None]
        + offset * normal_dot[None]
    )
    return jnp.sum(stokeslet, axis=3) / (8.0 * math.pi)


def per_device(
    coeffs, degree, material, split_coeffs, split_material, separation, reader_dev, reader_slot
):
    drop_count, fields, degrees, coef_width = coeffs.shape
    legendre, fourier, quad_weight, normals = spectral_tables(degrees)
    nlat = legendre.shape[1]
    nlon = fourier.shape[1]
    degree_index = jnp.arange(degrees, dtype=jnp.int32)
    order_full = jnp.arange(coef_width, dtype=jnp.int32) % degrees
    order_mask = (degree_index[:, None] >= order_full[None, :]).astype(jnp.float32)
    keep_mask = order_mask[None] * (degree_index[None, :, None] <= degree[:, None, None]).astype(
        jnp.float32
    )
    prepared = prepare(coeffs, keep_mask)
    partial_legendre = legendre_synth(
        prepared.reshape(drop_count * 4, degrees, coef_width), legendre
    )
    surface = fourier_synth(partial_legendre, fourier).reshape(drop_count, 4, nlat, nlon)
    radius, traction_grid = traction(surface, material)
    traction_coeffs = (
        analysis_legendre(analysis_fourier(traction_grid, fourier, quad_weight), legendre)
        * keep_mask
    )
    split_count = split_coeffs.shape[0]
    half_width = split_coeffs.shape[3]
    half_orders = half_width // 2
    half_index = lax.axis_index("row") % 2
    pair_start = (
        lax.axis_index("row") // 2 * lax.axis_size("col") + lax.axis_index("col")
    ) * split_count
    own_material = lax.dynamic_slice_in_dim(split_material, pair_start, split_count, 0)
    own_order = half_index * half_orders + jnp.arange(half_width, dtype=jnp.int32) % half_orders
    keep_half = (degree_index[:, None] >= own_order[None, :]).astype(jnp.float32)
    own_legendre = lax.dynamic_slice_in_dim(legendre, half_index * half_orders, half_orders, 0)
    own_fourier = lax.dynamic_slice_in_dim(
        fourier.reshape(2, degrees, nlon), half_index * half_orders, half_orders, 1
    ).reshape(half_width, nlon)
    split_prepared = prepare(split_coeffs, keep_half[None])
    split_legendre = legendre_synth(
        split_prepared.reshape(split_count * 4, degrees, half_width), own_legendre
    )
    partial_surface = fourier_synth(split_legendre, own_fourier)
    split_surface = partial_surface + from_partner(
        partial_surface.astype(jnp.bfloat16), "row", 0
    ).astype(partial_surface.dtype)
    split_radius, split_grid = traction(
        split_surface.reshape(split_count, 4, nlat, nlon), own_material
    )
    coef_grid = analysis_fourier(split_grid, fourier, quad_weight)
    own_grid = lax.dynamic_slice_in_dim(coef_grid, half_index * half_orders, half_orders, 3)
    split_traction = analysis_legendre(own_grid, own_legendre) * keep_half[None]
    near_grid = jnp.stack([radius, traction_grid], axis=1).astype(jnp.bfloat16)
    point_grid = near_grid[:, 0, nlat // 4 :: nlat // 2, :: nlon // 2]
    point_count = point_grid.shape[1] * point_grid.shape[2]
    own_points = point_grid.reshape(drop_count, point_count)
    target_normal = normals[:, nlat // 4 :: nlat // 2, :: nlon // 2].reshape(3, point_count)
    all_points = lax.all_gather(own_points, ("row", "col"), axis=0, tiled=True)
    total_drops = all_points.shape[0]
    readers = reader_dev.shape[1]
    target = (reader_dev * drop_count + reader_slot).reshape(-1)
    pick = (target[:, None] == jnp.arange(total_drops, dtype=jnp.int32)[None, :]).astype(
        jnp.float32
    )
    target_radius = jnp.dot(pick, all_points.astype(jnp.float32), precision=HIGH)
    target_point = separation.reshape(3, drop_count * readers)[:, :, None] + (
        target_radius[None] * target_normal[:, None, :]
    )
    target_point = jnp.transpose(
        target_point.reshape(3, drop_count, readers * point_count), (1, 2, 0)
    ).reshape(-1)
    source_radius = near_grid[:, 0].astype(jnp.float32)
    source_traction = near_grid[:, 1].astype(jnp.float32)
    cell_weight = jnp.broadcast_to(quad_weight[:, None], (nlat, nlon))
    partial = near_field(target_point, source_radius, source_traction, normals, cell_weight)
    contribution = jnp.sum(partial, axis=3) / (8.0 * math.pi)
    contribution = jnp.transpose(
        contribution.reshape(drop_count, 3, readers, point_count), (0, 2, 1, 3)
    ).reshape(drop_count * readers, 3 * point_count)
    dense = jnp.dot(jnp.transpose(pick), contribution, precision=HIGH)
    mine = lax.psum_scatter(dense, ("row", "col"), scatter_dimension=0, tiled=True)
    near_velocity = jnp.transpose(mine.reshape(drop_count, 3, point_count), (1, 0, 2))
    return (traction_coeffs, split_traction, near_velocity.reshape(3, drop_count * point_count))


def near_kernel(t_ref, r_ref, q_ref, n_ref, w_ref, o_ref, s_ref):
    drop = pl.program_id(0)
    targets = o_ref.shape[2]
    chunks = r_ref.shape[1] // 8
    r = r_ref[0]
    s_ref[0] = r * n_ref[0]
    s_ref[1] = r * n_ref[1]
    s_ref[2] = r * n_ref[2]
    s_ref[3] = q_ref[0] * r * r * w_ref[...]

    def body(t, carry):
        base = (drop * targets + t) * 3
        tx = t_ref[base]
        ty = t_ref[base + 1]
        tz = t_ref[base + 2]
        ax = jnp.zeros((8, 128), jnp.float32)
        ay = jnp.zeros((8, 128), jnp.float32)
        az = jnp.zeros((8, 128), jnp.float32)
        for c in range(chunks):
            rows = pl.ds(c * 8, 8)
            nx = n_ref[0, rows, :]
            ny = n_ref[1, rows, :]
            nz = n_ref[2, rows, :]
            dx = tx - s_ref[0, rows, :]
            dy = ty - s_ref[1, rows, :]
            dz = tz - s_ref[2, rows, :]
            dd = dx * dx + dy * dy + dz * dz
            inv = lax.rsqrt(dd + SOFTENING)
            w = s_ref[3, rows, :] * (inv * inv * inv)
            dn = dx * nx + dy * ny + dz * nz
            a = dd + 2.0 * SOFTENING
            ax = ax + w * (nx * a + dx * dn)
            ay = ay + w * (ny * a + dy * dn)
            az = az + w * (nz * a + dz * dn)
        o_ref[0, 0, pl.ds(t, 1), :] = jnp.sum(ax, axis=0, keepdims=True)
        o_ref[0, 1, pl.ds(t, 1), :] = jnp.sum(ay, axis=0, keepdims=True)
        o_ref[0, 2, pl.ds(t, 1), :] = jnp.sum(az, axis=0, keepdims=True)
        return carry

    lax.fori_loop(0, targets, body, 0)


def near_field(target_point, source_radius, source_traction, normals, cell_weight):
    drops, nlat, nlon = source_radius.shape
    targets = target_point.shape[0] // (3 * drops)
    cells = drops * targets * nlat * nlon
    return pl.pallas_call(
        near_kernel,
        grid=(drops,),
        in_specs=[
            pl.BlockSpec(memory_space=pltpu.SMEM),
            pl.BlockSpec((1, nlat, nlon), lambda s: (s, 0, 0)),
            pl.BlockSpec((1, nlat, nlon), lambda s: (s, 0, 0)),
            pl.BlockSpec((3, nlat, nlon), lambda s: (0, 0, 0)),
            pl.BlockSpec((nlat, nlon), lambda s: (0, 0)),
        ],
        out_specs=pl.BlockSpec((1, 3, targets, nlon), lambda s: (s, 0, 0, 0)),
        out_shape=jax.ShapeDtypeStruct((drops, 3, targets, nlon), jnp.float32),
        scratch_shapes=[pltpu.VMEM((4, nlat, nlon), jnp.float32)],
        cost_estimate=pl.CostEstimate(
            flops=36 * cells, transcendentals=cells, bytes_accessed=4 * drops * nlat * nlon * 2
        ),
    )(target_point, source_radius, source_traction, normals, cell_weight)


def solution(mesh):
    in_specs = (
        P(("row", "col"), None, None, None),
        P(("row", "col")),
        P(("row", "col"), None),
        P(("row", "col"), None, None, None),
        P(),
        P(None, ("row", "col"), None),
        P(("row", "col"), None),
        P(("row", "col"), None),
    )
    out_specs = (
        P(("row", "col"), None, None),
        P(("row", "col"), None, None),
        P(None, ("row", "col")),
    )
    return jax.shard_map(
        per_device, mesh=mesh, in_specs=in_specs, out_specs=out_specs, check_vma=False
    )
```

```python
import math

import jax
import jax.numpy as jnp
import numpy as np
from jax import lax
from jax.experimental import pallas as pl
from jax.experimental.pallas import tpu as pltpu
from jax.sharding import PartitionSpec as P

HIGH = lax.Precision.HIGHEST
SOFTENING = 0.04


def from_partner(block, axis, stride):
    count = lax.axis_size(axis)
    route = []
    for low in range(count):
        high = low | 1 << stride
        if high != low and high < count:
            route += [(low, high), (high, low)]
    return lax.ppermute(block, axis, route)


def spectral_tables(degrees):
    nlon = 2 * degrees
    theta_lat = (np.arange(degrees) + 0.5) * (math.pi / degrees)
    cosine = np.cos(theta_lat)
    sine_theta = np.sin(theta_lat)
    legendre = np.zeros((degrees, degrees, degrees))
    for order in range(degrees):
        log_total = 0.0
        for step_index in range(1, order + 1):
            log_total = log_total + math.log((2.0 * step_index + 1.0) / (2.0 * step_index))
        diag_value = np.exp(0.5 * log_total + order * np.log(sine_theta)) / math.sqrt(4.0 * math.pi)
        legendre[order, :, order] = diag_value
        prev_two = diag_value
        if order + 1 < degrees:
            prev_one = math.sqrt(2.0 * order + 3.0) * cosine * diag_value
            legendre[order, :, order + 1] = prev_one
            for level in range(order + 2, degrees):
                alpha_term = math.sqrt(
                    (4.0 * level * level - 1.0) / (level * level - order * order)
                )
                beta_term = math.sqrt(
                    ((level - 1.0) ** 2 - order * order) / (4.0 * (level - 1.0) ** 2 - 1.0)
                )
                current = alpha_term * (cosine * prev_one - beta_term * prev_two)
                legendre[order, :, level] = current
                prev_two = prev_one
                prev_one = current
    order_index = np.arange(degrees)
    lon_index = np.arange(nlon)
    phase_angle = order_index[:, None] * lon_index[None, :] % nlon * (2.0 * math.pi / nlon)
    fourier = np.concatenate([np.cos(phase_angle), np.sin(phase_angle)], axis=0)
    quad_weight = sine_theta * (math.pi / degrees) * (2.0 * math.pi / nlon)
    longitude = lon_index * (2.0 * math.pi / nlon)
    normals = np.stack(
        [
            sine_theta[:, None] * np.cos(longitude)[None, :],
            sine_theta[:, None] * np.sin(longitude)[None, :],
            cosine[:, None] * np.ones((1, nlon)),
        ],
        axis=0,
    )
    return (
        jnp.asarray(legendre, dtype=jnp.float32),
        jnp.asarray(fourier, dtype=jnp.float32),
        jnp.asarray(quad_weight, dtype=jnp.float32),
        jnp.asarray(normals, dtype=jnp.float32),
    )


def legendre_synth(coeff, legendre):
    batch_size, degrees, coef_width = coeff.shape
    orders = legendre.shape[0]
    parted = coeff.reshape(batch_size, degrees, 2, orders)
    return jnp.einsum("mjl,nlcm->njcm", legendre, parted, precision=HIGH)


def fourier_synth(partial_legendre, fourier_rows):
    batch_size, nlat, two, orders = partial_legendre.shape
    return jnp.einsum(
        "njw,wk->njk",
        partial_legendre.reshape(batch_size, nlat, two * orders),
        fourier_rows,
        precision=HIGH,
    )


def analysis_fourier(traction_grid, fourier, quad_weight):
    batch_size, nlat, nlon = traction_grid.shape
    projected = (
        jnp.einsum("bjk,wk->bjw", traction_grid, fourier, precision=HIGH)
        * quad_weight[None, :, None]
    )
    return projected.reshape(batch_size, nlat, 2, fourier.shape[0] // 2)


def analysis_legendre(coef_grid, legendre):
    batch_size = coef_grid.shape[0]
    result = jnp.einsum("mjl,bjcm->blcm", legendre, coef_grid, precision=HIGH)
    return result.reshape(batch_size, legendre.shape[2], 2 * legendre.shape[0])


def prepare(coeffs, keep_mask):
    degrees = coeffs.shape[2]
    degree_value = jnp.arange(degrees, dtype=jnp.float32)
    shape_part = coeffs[:, 0] * keep_mask
    curvature = (
        shape_part * (degree_value * (degree_value + 1.0) / (degrees * degrees))[None, :, None]
    )
    electric = 3.0 * coeffs[:, 1] * keep_mask
    viscous = 3.0 * coeffs[:, 2] * keep_mask * ((degree_value + 2.0) / degrees)[None, :, None]
    return jnp.stack([shape_part, curvature, electric, viscous], axis=1)


def traction(surface, material):
    radius = jnp.exp(surface[:, 0])
    traction_grid = (
        material[:, 0, None, None] * surface[:, 1]
        + 0.5 * surface[:, 2] * surface[:, 2]
        + 2.0 * material[:, 1, None, None] * surface[:, 3]
    )
    return (radius, traction_grid)


def velocity_terms(
    radius, traction_grid, spacing, target_radius, cell_weight, cell_normal, target_normal
):
    load_grid = traction_grid * radius * radius * cell_weight[None, :]
    target_point = spacing[:, :, None] + target_radius[None] * target_normal[:, None, :]
    surface_point = radius[None] * cell_normal[:, None, :]
    offset = target_point[:, :, :, None] - surface_point[:, :, None, :]
    distance_sq = jnp.sum(offset * offset, axis=0)
    softened = distance_sq + SOFTENING
    weight = load_grid[:, None, :] / (softened * jnp.sqrt(softened))
    normal_dot = jnp.sum(offset * cell_normal[:, None, None, :], axis=0)
    stokeslet = weight[None] * (
        cell_normal[:, None, None, :] * (distance_sq + 2.0 * SOFTENING)[None]
        + offset * normal_dot[None]
    )
    return jnp.sum(stokeslet, axis=3) / (8.0 * math.pi)


def per_device(
    coeffs, degree, material, split_coeffs, split_material, separation, reader_dev, reader_slot
):
    drop_count, fields, degrees, coef_width = coeffs.shape
    legendre, fourier, quad_weight, normals = spectral_tables(degrees)
    nlat = legendre.shape[1]
    nlon = fourier.shape[1]
    degree_index = jnp.arange(degrees, dtype=jnp.int32)
    order_full = jnp.arange(coef_width, dtype=jnp.int32) % degrees
    order_mask = (degree_index[:, None] >= order_full[None, :]).astype(jnp.float32)
    keep_mask = order_mask[None] * (degree_index[None, :, None] <= degree[:, None, None]).astype(
        jnp.float32
    )
    prepared = prepare(coeffs, keep_mask)
    partial_legendre = legendre_synth(
        prepared.reshape(drop_count * 4, degrees, coef_width), legendre
    )
    surface = fourier_synth(partial_legendre, fourier).reshape(drop_count, 4, nlat, nlon)
    radius, traction_grid = traction(surface, material)
    traction_coeffs = (
        analysis_legendre(analysis_fourier(traction_grid, fourier, quad_weight), legendre)
        * keep_mask
    )
    split_count = split_coeffs.shape[0]
    half_width = split_coeffs.shape[3]
    half_orders = half_width // 2
    half_index = lax.axis_index("row") % 2
    pair_start = (
        lax.axis_index("row") // 2 * lax.axis_size("col") + lax.axis_index("col")
    ) * split_count
    own_material = lax.dynamic_slice_in_dim(split_material, pair_start, split_count, 0)
    own_order = half_index * half_orders + jnp.arange(half_width, dtype=jnp.int32) % half_orders
    keep_half = (degree_index[:, None] >= own_order[None, :]).astype(jnp.float32)
    own_legendre = lax.dynamic_slice_in_dim(legendre, half_index * half_orders, half_orders, 0)
    own_fourier = lax.dynamic_slice_in_dim(
        fourier.reshape(2, degrees, nlon), half_index * half_orders, half_orders, 1
    ).reshape(half_width, nlon)
    split_prepared = prepare(split_coeffs, keep_half[None])
    split_legendre = legendre_synth(
        split_prepared.reshape(split_count * 4, degrees, half_width), own_legendre
    )
    partial_surface = fourier_synth(split_legendre, own_fourier)
    split_surface = partial_surface + from_partner(
        partial_surface.astype(jnp.bfloat16), "row", 0
    ).astype(partial_surface.dtype)
    split_radius, split_grid = traction(
        split_surface.reshape(split_count, 4, nlat, nlon), own_material
    )
    coef_grid = analysis_fourier(split_grid, fourier, quad_weight)
    own_grid = lax.dynamic_slice_in_dim(coef_grid, half_index * half_orders, half_orders, 3)
    split_traction = analysis_legendre(own_grid, own_legendre) * keep_half[None]
    near_grid = jnp.stack([radius, traction_grid], axis=1).astype(jnp.bfloat16)
    point_grid = near_grid[:, 0, nlat // 4 :: nlat // 2, :: nlon // 2]
    point_count = point_grid.shape[1] * point_grid.shape[2]
    own_points = point_grid.reshape(drop_count, point_count)
    target_normal = normals[:, nlat // 4 :: nlat // 2, :: nlon // 2].reshape(3, point_count)
    devices = lax.axis_size("row") * lax.axis_size("col")
    all_points = lax.all_to_all(
        jnp.broadcast_to(own_points.reshape(1, -1), (devices, drop_count * point_count)),
        ("row", "col"),
        split_axis=0,
        concat_axis=0,
        tiled=True,
    ).reshape(devices * drop_count, point_count)
    total_drops = all_points.shape[0]
    readers = reader_dev.shape[1]
    target = (reader_dev * drop_count + reader_slot).reshape(-1)
    pick = (target[:, None] == jnp.arange(total_drops, dtype=jnp.int32)[None, :]).astype(
        jnp.float32
    )
    target_radius = jnp.dot(pick, all_points.astype(jnp.float32), precision=HIGH)
    target_point = separation.reshape(3, drop_count * readers)[:, :, None] + (
        target_radius[None] * target_normal[:, None, :]
    )
    target_point = jnp.transpose(
        target_point.reshape(3, drop_count, readers * point_count), (1, 2, 0)
    ).reshape(-1)
    source_radius = near_grid[:, 0].astype(jnp.float32)
    source_traction = near_grid[:, 1].astype(jnp.float32)
    cell_weight = jnp.broadcast_to(quad_weight[:, None], (nlat, nlon))
    partial = near_field(target_point, source_radius, source_traction, normals, cell_weight)
    contribution = jnp.sum(partial, axis=3) / (8.0 * math.pi)
    contribution = jnp.transpose(
        contribution.reshape(drop_count, 3, readers, point_count), (0, 2, 1, 3)
    ).reshape(drop_count * readers, 3 * point_count)
    destination = reader_dev.reshape(-1)
    capacity = 2
    onehot = (destination[:, None] == jnp.arange(devices, dtype=jnp.int32)[None, :]).astype(
        jnp.int32
    )
    rank = jnp.sum((jnp.cumsum(onehot, axis=0) - onehot) * onehot, axis=1)
    position = destination * capacity + rank
    place = (position[:, None] == jnp.arange(devices * capacity, dtype=jnp.int32)[None, :]).astype(
        jnp.float32
    )
    record = jnp.concatenate(
        [contribution, reader_slot.reshape(-1, 1).astype(jnp.float32)], axis=1
    )
    outgoing = jnp.dot(jnp.transpose(place), record, precision=HIGH)
    incoming = lax.all_to_all(
        outgoing.reshape(devices, capacity, record.shape[1]),
        ("row", "col"),
        split_axis=0,
        concat_axis=0,
        tiled=True,
    ).reshape(devices * capacity, record.shape[1])
    slot_pick = (
        incoming[:, -1:] == jnp.arange(drop_count, dtype=jnp.float32)[None, :]
    ).astype(jnp.float32)
    mine = jnp.dot(jnp.transpose(slot_pick), incoming[:, :-1], precision=HIGH)
    near_velocity = jnp.transpose(mine.reshape(drop_count, 3, point_count), (1, 0, 2))
    return (traction_coeffs, split_traction, near_velocity.reshape(3, drop_count * point_count))


def near_kernel(t_ref, r_ref, q_ref, n_ref, w_ref, o_ref, s_ref):
    drop = pl.program_id(0)
    targets = o_ref.shape[2]
    chunks = r_ref.shape[1] // 8
    r = r_ref[0]
    s_ref[0] = r * n_ref[0]
    s_ref[1] = r * n_ref[1]
    s_ref[2] = r * n_ref[2]
    s_ref[3] = q_ref[0] * r * r * w_ref[...]

    def body(t, carry):
        base = (drop * targets + t) * 3
        tx = t_ref[base]
        ty = t_ref[base + 1]
        tz = t_ref[base + 2]
        ax = jnp.zeros((8, 128), jnp.float32)
        ay = jnp.zeros((8, 128), jnp.float32)
        az = jnp.zeros((8, 128), jnp.float32)
        for c in range(chunks):
            rows = pl.ds(c * 8, 8)
            nx = n_ref[0, rows, :]
            ny = n_ref[1, rows, :]
            nz = n_ref[2, rows, :]
            dx = tx - s_ref[0, rows, :]
            dy = ty - s_ref[1, rows, :]
            dz = tz - s_ref[2, rows, :]
            dd = dx * dx + dy * dy + dz * dz
            inv = lax.rsqrt(dd + SOFTENING)
            w = s_ref[3, rows, :] * (inv * inv * inv)
            dn = dx * nx + dy * ny + dz * nz
            a = dd + 2.0 * SOFTENING
            ax = ax + w * (nx * a + dx * dn)
            ay = ay + w * (ny * a + dy * dn)
            az = az + w * (nz * a + dz * dn)
        o_ref[0, 0, pl.ds(t, 1), :] = jnp.sum(ax, axis=0, keepdims=True)
        o_ref[0, 1, pl.ds(t, 1), :] = jnp.sum(ay, axis=0, keepdims=True)
        o_ref[0, 2, pl.ds(t, 1), :] = jnp.sum(az, axis=0, keepdims=True)
        return carry

    lax.fori_loop(0, targets, body, 0)


def near_field(target_point, source_radius, source_traction, normals, cell_weight):
    drops, nlat, nlon = source_radius.shape
    targets = target_point.shape[0] // (3 * drops)
    cells = drops * targets * nlat * nlon
    return pl.pallas_call(
        near_kernel,
        grid=(drops,),
        in_specs=[
            pl.BlockSpec(memory_space=pltpu.SMEM),
            pl.BlockSpec((1, nlat, nlon), lambda s: (s, 0, 0)),
            pl.BlockSpec((1, nlat, nlon), lambda s: (s, 0, 0)),
            pl.BlockSpec((3, nlat, nlon), lambda s: (0, 0, 0)),
            pl.BlockSpec((nlat, nlon), lambda s: (0, 0)),
        ],
        out_specs=pl.BlockSpec((1, 3, targets, nlon), lambda s: (s, 0, 0, 0)),
        out_shape=jax.ShapeDtypeStruct((drops, 3, targets, nlon), jnp.float32),
        scratch_shapes=[pltpu.VMEM((4, nlat, nlon), jnp.float32)],
        cost_estimate=pl.CostEstimate(
            flops=36 * cells, transcendentals=cells, bytes_accessed=4 * drops * nlat * nlon * 2
        ),
    )(target_point, source_radius, source_traction, normals, cell_weight)


def solution(mesh):
    in_specs = (
        P(("row", "col"), None, None, None),
        P(("row", "col")),
        P(("row", "col"), None),
        P(("row", "col"), None, None, None),
        P(),
        P(None, ("row", "col"), None),
        P(("row", "col"), None),
        P(("row", "col"), None),
    )
    out_specs = (
        P(("row", "col"), None, None),
        P(("row", "col"), None, None),
        P(None, ("row", "col")),
    )
    return jax.shard_map(
        per_device, mesh=mesh, in_specs=in_specs, out_specs=out_specs, check_vma=False
    )
```

```python
import math

import jax
import jax.numpy as jnp
import numpy as np
from jax import lax
from jax.experimental import pallas as pl
from jax.experimental.pallas import tpu as pltpu
from jax.sharding import PartitionSpec as P

HIGH = lax.Precision.HIGHEST
SPECTRAL = lax.Precision.DEFAULT
SOFTENING = 0.04


def from_partner(block, axis, stride):
    count = lax.axis_size(axis)
    route = []
    for low in range(count):
        high = low | 1 << stride
        if high != low and high < count:
            route += [(low, high), (high, low)]
    return lax.ppermute(block, axis, route)


def spectral_tables(degrees):
    nlon = 2 * degrees
    theta_lat = (np.arange(degrees) + 0.5) * (math.pi / degrees)
    cosine = np.cos(theta_lat)
    sine_theta = np.sin(theta_lat)
    legendre = np.zeros((degrees, degrees, degrees))
    for order in range(degrees):
        log_total = 0.0
        for step_index in range(1, order + 1):
            log_total = log_total + math.log((2.0 * step_index + 1.0) / (2.0 * step_index))
        diag_value = np.exp(0.5 * log_total + order * np.log(sine_theta)) / math.sqrt(4.0 * math.pi)
        legendre[order, :, order] = diag_value
        prev_two = diag_value
        if order + 1 < degrees:
            prev_one = math.sqrt(2.0 * order + 3.0) * cosine * diag_value
            legendre[order, :, order + 1] = prev_one
            for level in range(order + 2, degrees):
                alpha_term = math.sqrt(
                    (4.0 * level * level - 1.0) / (level * level - order * order)
                )
                beta_term = math.sqrt(
                    ((level - 1.0) ** 2 - order * order) / (4.0 * (level - 1.0) ** 2 - 1.0)
                )
                current = alpha_term * (cosine * prev_one - beta_term * prev_two)
                legendre[order, :, level] = current
                prev_two = prev_one
                prev_one = current
    order_index = np.arange(degrees)
    lon_index = np.arange(nlon)
    phase_angle = order_index[:, None] * lon_index[None, :] % nlon * (2.0 * math.pi / nlon)
    fourier = np.concatenate([np.cos(phase_angle), np.sin(phase_angle)], axis=0)
    quad_weight = sine_theta * (math.pi / degrees) * (2.0 * math.pi / nlon)
    longitude = lon_index * (2.0 * math.pi / nlon)
    normals = np.stack(
        [
            sine_theta[:, None] * np.cos(longitude)[None, :],
            sine_theta[:, None] * np.sin(longitude)[None, :],
            cosine[:, None] * np.ones((1, nlon)),
        ],
        axis=0,
    )
    return (
        jnp.asarray(legendre, dtype=jnp.float32),
        jnp.asarray(fourier, dtype=jnp.float32),
        jnp.asarray(quad_weight, dtype=jnp.float32),
        jnp.asarray(normals, dtype=jnp.float32),
    )


def legendre_synth(coeff, legendre):
    batch_size, degrees, coef_width = coeff.shape
    orders = legendre.shape[0]
    parted = coeff.reshape(batch_size, degrees, 2, orders)
    return jnp.einsum("mjl,nlcm->njcm", legendre, parted, precision=SPECTRAL)


def fourier_synth(partial_legendre, fourier_rows):
    batch_size, nlat, two, orders = partial_legendre.shape
    return jnp.einsum(
        "njw,wk->njk",
        partial_legendre.reshape(batch_size, nlat, two * orders),
        fourier_rows,
        precision=SPECTRAL,
    )


def analysis_fourier(traction_grid, fourier, quad_weight):
    batch_size, nlat, nlon = traction_grid.shape
    projected = (
        jnp.einsum("bjk,wk->bjw", traction_grid, fourier, precision=SPECTRAL)
        * quad_weight[None, :, None]
    )
    return projected.reshape(batch_size, nlat, 2, fourier.shape[0] // 2)


def analysis_legendre(coef_grid, legendre):
    batch_size = coef_grid.shape[0]
    result = jnp.einsum("mjl,bjcm->blcm", legendre, coef_grid, precision=SPECTRAL)
    return result.reshape(batch_size, legendre.shape[2], 2 * legendre.shape[0])


def prepare(coeffs, keep_mask):
    degrees = coeffs.shape[2]
    degree_value = jnp.arange(degrees, dtype=jnp.float32)
    shape_part = coeffs[:, 0] * keep_mask
    curvature = (
        shape_part * (degree_value * (degree_value + 1.0) / (degrees * degrees))[None, :, None]
    )
    electric = 3.0 * coeffs[:, 1] * keep_mask
    viscous = 3.0 * coeffs[:, 2] * keep_mask * ((degree_value + 2.0) / degrees)[None, :, None]
    return jnp.stack([shape_part, curvature, electric, viscous], axis=1)


def traction(surface, material):
    radius = jnp.exp(surface[:, 0])
    traction_grid = (
        material[:, 0, None, None] * surface[:, 1]
        + 0.5 * surface[:, 2] * surface[:, 2]
        + 2.0 * material[:, 1, None, None] * surface[:, 3]
    )
    return (radius, traction_grid)


def velocity_terms(
    radius, traction_grid, spacing, target_radius, cell_weight, cell_normal, target_normal
):
    load_grid = traction_grid * radius * radius * cell_weight[None, :]
    target_point = spacing[:, :, None] + target_radius[None] * target_normal[:, None, :]
    surface_point = radius[None] * cell_normal[:, None, :]
    offset = target_point[:, :, :, None] - surface_point[:, :, None, :]
    distance_sq = jnp.sum(offset * offset, axis=0)
    softened = distance_sq + SOFTENING
    weight = load_grid[:, None, :] / (softened * jnp.sqrt(softened))
    normal_dot = jnp.sum(offset * cell_normal[:, None, None, :], axis=0)
    stokeslet = weight[None] * (
        cell_normal[:, None, None, :] * (distance_sq + 2.0 * SOFTENING)[None]
        + offset * normal_dot[None]
    )
    return jnp.sum(stokeslet, axis=3) / (8.0 * math.pi)


def per_device(
    coeffs, degree, material, split_coeffs, split_material, separation, reader_dev, reader_slot
):
    drop_count, fields, degrees, coef_width = coeffs.shape
    legendre, fourier, quad_weight, normals = spectral_tables(degrees)
    nlat = legendre.shape[1]
    nlon = fourier.shape[1]
    degree_index = jnp.arange(degrees, dtype=jnp.int32)
    order_full = jnp.arange(coef_width, dtype=jnp.int32) % degrees
    order_mask = (degree_index[:, None] >= order_full[None, :]).astype(jnp.float32)
    keep_mask = order_mask[None] * (degree_index[None, :, None] <= degree[:, None, None]).astype(
        jnp.float32
    )
    prepared = prepare(coeffs, keep_mask)
    partial_legendre = legendre_synth(
        prepared.reshape(drop_count * 4, degrees, coef_width), legendre
    )
    surface = fourier_synth(partial_legendre, fourier).reshape(drop_count, 4, nlat, nlon)
    radius, traction_grid = traction(surface, material)
    traction_coeffs = (
        analysis_legendre(analysis_fourier(traction_grid, fourier, quad_weight), legendre)
        * keep_mask
    )
    split_count = split_coeffs.shape[0]
    half_width = split_coeffs.shape[3]
    half_orders = half_width // 2
    half_index = lax.axis_index("row") % 2
    pair_start = (
        lax.axis_index("row") // 2 * lax.axis_size("col") + lax.axis_index("col")
    ) * split_count
    own_material = lax.dynamic_slice_in_dim(split_material, pair_start, split_count, 0)
    own_order = half_index * half_orders + jnp.arange(half_width, dtype=jnp.int32) % half_orders
    keep_half = (degree_index[:, None] >= own_order[None, :]).astype(jnp.float32)
    own_legendre = lax.dynamic_slice_in_dim(legendre, half_index * half_orders, half_orders, 0)
    own_fourier = lax.dynamic_slice_in_dim(
        fourier.reshape(2, degrees, nlon), half_index * half_orders, half_orders, 1
    ).reshape(half_width, nlon)
    split_prepared = prepare(split_coeffs, keep_half[None])
    split_legendre = legendre_synth(
        split_prepared.reshape(split_count * 4, degrees, half_width), own_legendre
    )
    partial_surface = fourier_synth(split_legendre, own_fourier)
    split_surface = partial_surface + from_partner(
        partial_surface.astype(jnp.bfloat16), "row", 0
    ).astype(partial_surface.dtype)
    split_radius, split_grid = traction(
        split_surface.reshape(split_count, 4, nlat, nlon), own_material
    )
    coef_grid = analysis_fourier(split_grid, fourier, quad_weight)
    own_grid = lax.dynamic_slice_in_dim(coef_grid, half_index * half_orders, half_orders, 3)
    split_traction = analysis_legendre(own_grid, own_legendre) * keep_half[None]
    near_grid = jnp.stack([radius, traction_grid], axis=1).astype(jnp.bfloat16)
    point_grid = near_grid[:, 0, nlat // 4 :: nlat // 2, :: nlon // 2]
    point_count = point_grid.shape[1] * point_grid.shape[2]
    own_points = point_grid.reshape(drop_count, point_count)
    target_normal = normals[:, nlat // 4 :: nlat // 2, :: nlon // 2].reshape(3, point_count)
    devices = lax.axis_size("row") * lax.axis_size("col")
    all_points = lax.all_to_all(
        jnp.broadcast_to(own_points.reshape(1, -1), (devices, drop_count * point_count)),
        ("row", "col"),
        split_axis=0,
        concat_axis=0,
        tiled=True,
    ).reshape(devices * drop_count, point_count)
    total_drops = all_points.shape[0]
    readers = reader_dev.shape[1]
    target = (reader_dev * drop_count + reader_slot).reshape(-1)
    pick = (target[:, None] == jnp.arange(total_drops, dtype=jnp.int32)[None, :]).astype(
        jnp.float32
    )
    target_radius = jnp.dot(pick, all_points.astype(jnp.float32), precision=HIGH)
    target_point = separation.reshape(3, drop_count * readers)[:, :, None] + (
        target_radius[None] * target_normal[:, None, :]
    )
    target_point = jnp.transpose(
        target_point.reshape(3, drop_count, readers * point_count), (1, 2, 0)
    ).reshape(-1)
    source_radius = near_grid[:, 0].astype(jnp.float32)
    source_traction = near_grid[:, 1].astype(jnp.float32)
    cell_weight = jnp.broadcast_to(quad_weight[:, None], (nlat, nlon))
    partial = near_field(target_point, source_radius, source_traction, normals, cell_weight)
    contribution = jnp.sum(partial, axis=3) / (8.0 * math.pi)
    contribution = jnp.transpose(
        contribution.reshape(drop_count, 3, readers, point_count), (0, 2, 1, 3)
    ).reshape(drop_count * readers, 3 * point_count)
    destination = reader_dev.reshape(-1)
    capacity = 2
    onehot = (destination[:, None] == jnp.arange(devices, dtype=jnp.int32)[None, :]).astype(
        jnp.int32
    )
    rank = jnp.sum((jnp.cumsum(onehot, axis=0) - onehot) * onehot, axis=1)
    position = destination * capacity + rank
    place = (position[:, None] == jnp.arange(devices * capacity, dtype=jnp.int32)[None, :]).astype(
        jnp.float32
    )
    record = jnp.concatenate(
        [contribution, reader_slot.reshape(-1, 1).astype(jnp.float32)], axis=1
    )
    outgoing = jnp.dot(jnp.transpose(place), record, precision=HIGH)
    incoming = lax.all_to_all(
        outgoing.reshape(devices, capacity, record.shape[1]),
        ("row", "col"),
        split_axis=0,
        concat_axis=0,
        tiled=True,
    ).reshape(devices * capacity, record.shape[1])
    slot_pick = (
        incoming[:, -1:] == jnp.arange(drop_count, dtype=jnp.float32)[None, :]
    ).astype(jnp.float32)
    mine = jnp.dot(jnp.transpose(slot_pick), incoming[:, :-1], precision=HIGH)
    near_velocity = jnp.transpose(mine.reshape(drop_count, 3, point_count), (1, 0, 2))
    return (traction_coeffs, split_traction, near_velocity.reshape(3, drop_count * point_count))


def near_kernel(t_ref, r_ref, q_ref, n_ref, w_ref, o_ref, s_ref):
    drop = pl.program_id(0)
    targets = o_ref.shape[2]
    chunks = r_ref.shape[1] // 8
    r = r_ref[0]
    s_ref[0] = r * n_ref[0]
    s_ref[1] = r * n_ref[1]
    s_ref[2] = r * n_ref[2]
    s_ref[3] = q_ref[0] * r * r * w_ref[...]

    def body(t, carry):
        base = (drop * targets + t) * 3
        tx = t_ref[base]
        ty = t_ref[base + 1]
        tz = t_ref[base + 2]
        ax = jnp.zeros((8, 128), jnp.float32)
        ay = jnp.zeros((8, 128), jnp.float32)
        az = jnp.zeros((8, 128), jnp.float32)
        for c in range(chunks):
            rows = pl.ds(c * 8, 8)
            nx = n_ref[0, rows, :]
            ny = n_ref[1, rows, :]
            nz = n_ref[2, rows, :]
            dx = tx - s_ref[0, rows, :]
            dy = ty - s_ref[1, rows, :]
            dz = tz - s_ref[2, rows, :]
            dd = dx * dx + dy * dy + dz * dz
            inv = lax.rsqrt(dd + SOFTENING)
            w = s_ref[3, rows, :] * (inv * inv * inv)
            dn = dx * nx + dy * ny + dz * nz
            a = dd + 2.0 * SOFTENING
            ax = ax + w * (nx * a + dx * dn)
            ay = ay + w * (ny * a + dy * dn)
            az = az + w * (nz * a + dz * dn)
        o_ref[0, 0, pl.ds(t, 1), :] = jnp.sum(ax, axis=0, keepdims=True)
        o_ref[0, 1, pl.ds(t, 1), :] = jnp.sum(ay, axis=0, keepdims=True)
        o_ref[0, 2, pl.ds(t, 1), :] = jnp.sum(az, axis=0, keepdims=True)
        return carry

    lax.fori_loop(0, targets, body, 0)


def near_field(target_point, source_radius, source_traction, normals, cell_weight):
    drops, nlat, nlon = source_radius.shape
    targets = target_point.shape[0] // (3 * drops)
    cells = drops * targets * nlat * nlon
    return pl.pallas_call(
        near_kernel,
        grid=(drops,),
        in_specs=[
            pl.BlockSpec(memory_space=pltpu.SMEM),
            pl.BlockSpec((1, nlat, nlon), lambda s: (s, 0, 0)),
            pl.BlockSpec((1, nlat, nlon), lambda s: (s, 0, 0)),
            pl.BlockSpec((3, nlat, nlon), lambda s: (0, 0, 0)),
            pl.BlockSpec((nlat, nlon), lambda s: (0, 0)),
        ],
        out_specs=pl.BlockSpec((1, 3, targets, nlon), lambda s: (s, 0, 0, 0)),
        out_shape=jax.ShapeDtypeStruct((drops, 3, targets, nlon), jnp.float32),
        scratch_shapes=[pltpu.VMEM((4, nlat, nlon), jnp.float32)],
        cost_estimate=pl.CostEstimate(
            flops=36 * cells, transcendentals=cells, bytes_accessed=4 * drops * nlat * nlon * 2
        ),
    )(target_point, source_radius, source_traction, normals, cell_weight)


def solution(mesh):
    in_specs = (
        P(("row", "col"), None, None, None),
        P(("row", "col")),
        P(("row", "col"), None),
        P(("row", "col"), None, None, None),
        P(),
        P(None, ("row", "col"), None),
        P(("row", "col"), None),
        P(("row", "col"), None),
    )
    out_specs = (
        P(("row", "col"), None, None),
        P(("row", "col"), None, None),
        P(None, ("row", "col")),
    )
    return jax.shard_map(
        per_device, mesh=mesh, in_specs=in_specs, out_specs=out_specs, check_vma=False
    )
```

```python
import math

import jax
import jax.numpy as jnp
import numpy as np
from jax import lax
from jax.experimental import pallas as pl
from jax.experimental.pallas import tpu as pltpu
from jax.sharding import PartitionSpec as P

HIGH = lax.Precision.HIGHEST
SPECTRAL = lax.Precision.DEFAULT
SOFTENING = 0.04


def from_partner(block, axis, stride):
    count = lax.axis_size(axis)
    route = []
    for low in range(count):
        high = low | 1 << stride
        if high != low and high < count:
            route += [(low, high), (high, low)]
    return lax.ppermute(block, axis, route)


def spectral_tables(degrees):
    nlon = 2 * degrees
    theta_lat = (np.arange(degrees) + 0.5) * (math.pi / degrees)
    cosine = np.cos(theta_lat)
    sine_theta = np.sin(theta_lat)
    legendre = np.zeros((degrees, degrees, degrees))
    for order in range(degrees):
        log_total = 0.0
        for step_index in range(1, order + 1):
            log_total = log_total + math.log((2.0 * step_index + 1.0) / (2.0 * step_index))
        diag_value = np.exp(0.5 * log_total + order * np.log(sine_theta)) / math.sqrt(4.0 * math.pi)
        legendre[order, :, order] = diag_value
        prev_two = diag_value
        if order + 1 < degrees:
            prev_one = math.sqrt(2.0 * order + 3.0) * cosine * diag_value
            legendre[order, :, order + 1] = prev_one
            for level in range(order + 2, degrees):
                alpha_term = math.sqrt(
                    (4.0 * level * level - 1.0) / (level * level - order * order)
                )
                beta_term = math.sqrt(
                    ((level - 1.0) ** 2 - order * order) / (4.0 * (level - 1.0) ** 2 - 1.0)
                )
                current = alpha_term * (cosine * prev_one - beta_term * prev_two)
                legendre[order, :, level] = current
                prev_two = prev_one
                prev_one = current
    order_index = np.arange(degrees)
    lon_index = np.arange(nlon)
    phase_angle = order_index[:, None] * lon_index[None, :] % nlon * (2.0 * math.pi / nlon)
    fourier = np.concatenate([np.cos(phase_angle), np.sin(phase_angle)], axis=0)
    quad_weight = sine_theta * (math.pi / degrees) * (2.0 * math.pi / nlon)
    longitude = lon_index * (2.0 * math.pi / nlon)
    normals = np.stack(
        [
            sine_theta[:, None] * np.cos(longitude)[None, :],
            sine_theta[:, None] * np.sin(longitude)[None, :],
            cosine[:, None] * np.ones((1, nlon)),
        ],
        axis=0,
    )
    return (
        jnp.asarray(legendre, dtype=jnp.float32),
        jnp.asarray(fourier, dtype=jnp.float32),
        jnp.asarray(quad_weight, dtype=jnp.float32),
        jnp.asarray(normals, dtype=jnp.float32),
    )


def legendre_synth(coeff, legendre):
    batch_size, degrees, coef_width = coeff.shape
    orders = legendre.shape[0]
    parted = coeff.reshape(batch_size, degrees, 2, orders)
    return jnp.einsum("mjl,nlcm->njcm", legendre, parted, precision=SPECTRAL)


def fourier_synth(partial_legendre, fourier_rows):
    batch_size, nlat, two, orders = partial_legendre.shape
    return jnp.einsum(
        "njw,wk->njk",
        partial_legendre.reshape(batch_size, nlat, two * orders),
        fourier_rows,
        precision=SPECTRAL,
    )


def analysis_fourier(traction_grid, fourier, quad_weight):
    batch_size, nlat, nlon = traction_grid.shape
    projected = (
        jnp.einsum("bjk,wk->bjw", traction_grid, fourier, precision=SPECTRAL)
        * quad_weight[None, :, None]
    )
    return projected.reshape(batch_size, nlat, 2, fourier.shape[0] // 2)


def analysis_legendre(coef_grid, legendre):
    batch_size = coef_grid.shape[0]
    result = jnp.einsum("mjl,bjcm->blcm", legendre, coef_grid, precision=SPECTRAL)
    return result.reshape(batch_size, legendre.shape[2], 2 * legendre.shape[0])


def prepare(coeffs, keep_mask):
    degrees = coeffs.shape[2]
    degree_value = jnp.arange(degrees, dtype=jnp.float32)
    shape_part = coeffs[:, 0] * keep_mask
    curvature = (
        shape_part * (degree_value * (degree_value + 1.0) / (degrees * degrees))[None, :, None]
    )
    electric = 3.0 * coeffs[:, 1] * keep_mask
    viscous = 3.0 * coeffs[:, 2] * keep_mask * ((degree_value + 2.0) / degrees)[None, :, None]
    return jnp.stack([shape_part, curvature, electric, viscous], axis=1)


def traction(surface, material):
    radius = jnp.exp(surface[:, 0])
    traction_grid = (
        material[:, 0, None, None] * surface[:, 1]
        + 0.5 * surface[:, 2] * surface[:, 2]
        + 2.0 * material[:, 1, None, None] * surface[:, 3]
    )
    return (radius, traction_grid)


def velocity_terms(
    radius, traction_grid, spacing, target_radius, cell_weight, cell_normal, target_normal
):
    load_grid = traction_grid * radius * radius * cell_weight[None, :]
    target_point = spacing[:, :, None] + target_radius[None] * target_normal[:, None, :]
    surface_point = radius[None] * cell_normal[:, None, :]
    offset = target_point[:, :, :, None] - surface_point[:, :, None, :]
    distance_sq = jnp.sum(offset * offset, axis=0)
    softened = distance_sq + SOFTENING
    weight = load_grid[:, None, :] / (softened * jnp.sqrt(softened))
    normal_dot = jnp.sum(offset * cell_normal[:, None, None, :], axis=0)
    stokeslet = weight[None] * (
        cell_normal[:, None, None, :] * (distance_sq + 2.0 * SOFTENING)[None]
        + offset * normal_dot[None]
    )
    return jnp.sum(stokeslet, axis=3) / (8.0 * math.pi)


def per_device(
    coeffs, degree, material, split_coeffs, split_material, separation, reader_dev, reader_slot
):
    drop_count, fields, degrees, coef_width = coeffs.shape
    legendre, fourier, quad_weight, normals = spectral_tables(degrees)
    nlat = legendre.shape[1]
    nlon = fourier.shape[1]
    degree_index = jnp.arange(degrees, dtype=jnp.int32)
    order_full = jnp.arange(coef_width, dtype=jnp.int32) % degrees
    order_mask = (degree_index[:, None] >= order_full[None, :]).astype(jnp.float32)
    keep_mask = order_mask[None] * (degree_index[None, :, None] <= degree[:, None, None]).astype(
        jnp.float32
    )
    prepared = prepare(coeffs, keep_mask)
    point_lat = np.arange(nlat // 4, nlat, nlat // 2)
    point_lon = np.arange(0, nlon, nlon // 2)
    point_legendre = legendre[:, point_lat, :]
    point_partial = jnp.einsum(
        "mjl,nlcm->njcm",
        point_legendre,
        prepared[:, 0].reshape(drop_count, degrees, 2, degrees),
        precision=HIGH,
    )
    point_surface = jnp.einsum(
        "njw,wk->njk",
        point_partial.reshape(drop_count, point_lat.size, coef_width),
        fourier[:, point_lon],
        precision=HIGH,
    )
    own_points = jnp.exp(point_surface).astype(jnp.bfloat16).reshape(drop_count, -1)
    partial_legendre = legendre_synth(
        prepared.reshape(drop_count * 4, degrees, coef_width), legendre
    )
    surface = fourier_synth(partial_legendre, fourier).reshape(drop_count, 4, nlat, nlon)
    radius, traction_grid = traction(surface, material)
    split_count = split_coeffs.shape[0]
    half_width = split_coeffs.shape[3]
    half_orders = half_width // 2
    half_index = lax.axis_index("row") % 2
    pair_start = (
        lax.axis_index("row") // 2 * lax.axis_size("col") + lax.axis_index("col")
    ) * split_count
    own_material = lax.dynamic_slice_in_dim(split_material, pair_start, split_count, 0)
    own_order = half_index * half_orders + jnp.arange(half_width, dtype=jnp.int32) % half_orders
    keep_half = (degree_index[:, None] >= own_order[None, :]).astype(jnp.float32)
    own_legendre = lax.dynamic_slice_in_dim(legendre, half_index * half_orders, half_orders, 0)
    own_fourier = lax.dynamic_slice_in_dim(
        fourier.reshape(2, degrees, nlon), half_index * half_orders, half_orders, 1
    ).reshape(half_width, nlon)
    split_prepared = prepare(split_coeffs, keep_half[None])
    split_legendre = legendre_synth(
        split_prepared.reshape(split_count * 4, degrees, half_width), own_legendre
    )
    partial_surface = fourier_synth(split_legendre, own_fourier)
    split_surface = partial_surface + from_partner(
        partial_surface.astype(jnp.bfloat16), "row", 0
    ).astype(partial_surface.dtype)
    split_radius, split_grid = traction(
        split_surface.reshape(split_count, 4, nlat, nlon), own_material
    )
    near_grid = jnp.stack([radius, traction_grid], axis=1).astype(jnp.bfloat16)
    point_lat = np.arange(nlat // 4, nlat, nlat // 2)
    point_lon = np.arange(0, nlon, nlon // 2)
    point_count = point_lat.size * point_lon.size
    target_normal = normals[:, nlat // 4 :: nlat // 2, :: nlon // 2].reshape(3, point_count)
    all_points = gather_all(own_points.reshape(-1)).reshape(-1, point_count)
    total_drops = all_points.shape[0]
    readers = reader_dev.shape[1]
    target = (reader_dev * drop_count + reader_slot).reshape(-1)
    pick = (target[:, None] == jnp.arange(total_drops, dtype=jnp.int32)[None, :]).astype(
        jnp.float32
    )
    target_radius = jnp.dot(pick, all_points.astype(jnp.float32), precision=HIGH)
    target_point = separation.reshape(3, drop_count * readers)[:, :, None] + (
        target_radius[None] * target_normal[:, None, :]
    )
    target_point = jnp.transpose(
        target_point.reshape(3, drop_count, readers * point_count), (1, 2, 0)
    ).reshape(-1)
    source_radius = near_grid[:, 0].astype(jnp.float32)
    source_traction = near_grid[:, 1].astype(jnp.float32)
    cell_weight = jnp.broadcast_to(quad_weight[:, None], (nlat, nlon))
    partial = near_field(target_point, source_radius, source_traction, normals, cell_weight)
    partial, traction_grid, split_grid = lax.optimization_barrier(
        (partial, traction_grid, split_grid)
    )
    contribution = jnp.sum(partial, axis=3) / (8.0 * math.pi)
    contribution = jnp.transpose(
        contribution.reshape(drop_count, 3, readers, point_count), (0, 2, 1, 3)
    ).reshape(drop_count * readers, 3 * point_count)
    dense = jnp.dot(jnp.transpose(pick), contribution, precision=HIGH)
    mine = reduce_to_owner(dense.reshape(-1, drop_count * 3 * point_count))
    near_velocity = jnp.transpose(mine.reshape(drop_count, 3, point_count), (1, 0, 2))
    traction_coeffs = (
        analysis_legendre(analysis_fourier(traction_grid, fourier, quad_weight), legendre)
        * keep_mask
    )
    coef_grid = analysis_fourier(split_grid, fourier, quad_weight)
    own_grid = lax.dynamic_slice_in_dim(coef_grid, half_index * half_orders, half_orders, 3)
    split_traction = analysis_legendre(own_grid, own_legendre) * keep_half[None]
    return (traction_coeffs, split_traction, near_velocity.reshape(3, drop_count * point_count))


def index_bits():
    bits = []
    for axis in ("row", "col"):
        size = lax.axis_size(axis)
        width = size.bit_length() - 1
        assert 1 << width == size
        bits += [(axis, k) for k in reversed(range(width))]
    return bits


def exchange_order(bits):
    return sorted(bits, key=lambda item: (item[0] != "row", item[1]))


def gather_all(own):
    bits = index_bits()
    done = []
    buf = own
    for axis, k in exchange_order(bits):
        other = from_partner(buf, axis, k)
        upper = (lax.axis_index(axis) >> k) & 1
        buf = jnp.where(upper == 1, jnp.stack([other, buf]), jnp.stack([buf, other]))
        done.insert(0, (axis, k))
    buf = jnp.transpose(buf, [done.index(item) for item in bits] + [len(bits)])
    return buf.reshape((-1,) + own.shape)


def reduce_to_owner(dense):
    bits = index_bits()
    left = list(bits)
    buf = dense.reshape((2,) * len(bits) + dense.shape[1:])
    for axis, k in exchange_order(bits):
        place = left.index((axis, k))
        lower = lax.index_in_dim(buf, 0, place, keepdims=False)
        upper_half = lax.index_in_dim(buf, 1, place, keepdims=False)
        upper = (lax.axis_index(axis) >> k) & 1
        keep = jnp.where(upper == 1, upper_half, lower)
        send = jnp.where(upper == 1, lower, upper_half)
        buf = keep + from_partner(send, axis, k)
        left.pop(place)
    return buf


def near_kernel(t_ref, r_ref, q_ref, n_ref, w_ref, o_ref, s_ref):
    drop = pl.program_id(0)
    targets = o_ref.shape[2]
    chunks = r_ref.shape[1] // 8
    r = r_ref[0]
    s_ref[0] = r * n_ref[0]
    s_ref[1] = r * n_ref[1]
    s_ref[2] = r * n_ref[2]
    s_ref[3] = q_ref[0] * r * r * w_ref[...]

    def body(t, carry):
        base = (drop * targets + t) * 3
        tx = t_ref[base]
        ty = t_ref[base + 1]
        tz = t_ref[base + 2]
        ax = jnp.zeros((8, 128), jnp.float32)
        ay = jnp.zeros((8, 128), jnp.float32)
        az = jnp.zeros((8, 128), jnp.float32)
        for c in range(chunks):
            rows = pl.ds(c * 8, 8)
            nx = n_ref[0, rows, :]
            ny = n_ref[1, rows, :]
            nz = n_ref[2, rows, :]
            dx = tx - s_ref[0, rows, :]
            dy = ty - s_ref[1, rows, :]
            dz = tz - s_ref[2, rows, :]
            dd = dx * dx + dy * dy + dz * dz
            inv = lax.rsqrt(dd + SOFTENING)
            w = s_ref[3, rows, :] * (inv * inv * inv)
            dn = dx * nx + dy * ny + dz * nz
            a = dd + 2.0 * SOFTENING
            ax = ax + w * (nx * a + dx * dn)
            ay = ay + w * (ny * a + dy * dn)
            az = az + w * (nz * a + dz * dn)
        o_ref[0, 0, pl.ds(t, 1), :] = jnp.sum(ax, axis=0, keepdims=True)
        o_ref[0, 1, pl.ds(t, 1), :] = jnp.sum(ay, axis=0, keepdims=True)
        o_ref[0, 2, pl.ds(t, 1), :] = jnp.sum(az, axis=0, keepdims=True)
        return carry

    lax.fori_loop(0, targets, body, 0)


def near_field(target_point, source_radius, source_traction, normals, cell_weight):
    drops, nlat, nlon = source_radius.shape
    targets = target_point.shape[0] // (3 * drops)
    cells = drops * targets * nlat * nlon
    return pl.pallas_call(
        near_kernel,
        grid=(drops,),
        in_specs=[
            pl.BlockSpec(memory_space=pltpu.SMEM),
            pl.BlockSpec((1, nlat, nlon), lambda s: (s, 0, 0)),
            pl.BlockSpec((1, nlat, nlon), lambda s: (s, 0, 0)),
            pl.BlockSpec((3, nlat, nlon), lambda s: (0, 0, 0)),
            pl.BlockSpec((nlat, nlon), lambda s: (0, 0)),
        ],
        out_specs=pl.BlockSpec((1, 3, targets, nlon), lambda s: (s, 0, 0, 0)),
        out_shape=jax.ShapeDtypeStruct((drops, 3, targets, nlon), jnp.float32),
        scratch_shapes=[pltpu.VMEM((4, nlat, nlon), jnp.float32)],
        cost_estimate=pl.CostEstimate(
            flops=36 * cells, transcendentals=cells, bytes_accessed=4 * drops * nlat * nlon * 2
        ),
    )(target_point, source_radius, source_traction, normals, cell_weight)


def solution(mesh):
    in_specs = (
        P(("row", "col"), None, None, None),
        P(("row", "col")),
        P(("row", "col"), None),
        P(("row", "col"), None, None, None),
        P(),
        P(None, ("row", "col"), None),
        P(("row", "col"), None),
        P(("row", "col"), None),
    )
    out_specs = (
        P(("row", "col"), None, None),
        P(("row", "col"), None, None),
        P(None, ("row", "col")),
    )
    return jax.shard_map(
        per_device, mesh=mesh, in_specs=in_specs, out_specs=out_specs, check_vma=False
    )
```

```python
import math

import jax
import jax.numpy as jnp
import numpy as np
from jax import lax
from jax.experimental import pallas as pl
from jax.experimental.pallas import tpu as pltpu
from jax.sharding import PartitionSpec as P

HIGH = lax.Precision.HIGHEST
SPECTRAL = lax.Precision.DEFAULT
SOFTENING = 0.04


def from_partner(block, axis, stride):
    count = lax.axis_size(axis)
    route = []
    for low in range(count):
        high = low | 1 << stride
        if high != low and high < count:
            route += [(low, high), (high, low)]
    return lax.ppermute(block, axis, route)


def spectral_tables(degrees):
    nlon = 2 * degrees
    theta_lat = (np.arange(degrees) + 0.5) * (math.pi / degrees)
    cosine = np.cos(theta_lat)
    sine_theta = np.sin(theta_lat)
    legendre = np.zeros((degrees, degrees, degrees))
    for order in range(degrees):
        log_total = 0.0
        for step_index in range(1, order + 1):
            log_total = log_total + math.log((2.0 * step_index + 1.0) / (2.0 * step_index))
        diag_value = np.exp(0.5 * log_total + order * np.log(sine_theta)) / math.sqrt(4.0 * math.pi)
        legendre[order, :, order] = diag_value
        prev_two = diag_value
        if order + 1 < degrees:
            prev_one = math.sqrt(2.0 * order + 3.0) * cosine * diag_value
            legendre[order, :, order + 1] = prev_one
            for level in range(order + 2, degrees):
                alpha_term = math.sqrt(
                    (4.0 * level * level - 1.0) / (level * level - order * order)
                )
                beta_term = math.sqrt(
                    ((level - 1.0) ** 2 - order * order) / (4.0 * (level - 1.0) ** 2 - 1.0)
                )
                current = alpha_term * (cosine * prev_one - beta_term * prev_two)
                legendre[order, :, level] = current
                prev_two = prev_one
                prev_one = current
    order_index = np.arange(degrees)
    lon_index = np.arange(nlon)
    phase_angle = order_index[:, None] * lon_index[None, :] % nlon * (2.0 * math.pi / nlon)
    fourier = np.concatenate([np.cos(phase_angle), np.sin(phase_angle)], axis=0)
    quad_weight = sine_theta * (math.pi / degrees) * (2.0 * math.pi / nlon)
    longitude = lon_index * (2.0 * math.pi / nlon)
    normals = np.stack(
        [
            sine_theta[:, None] * np.cos(longitude)[None, :],
            sine_theta[:, None] * np.sin(longitude)[None, :],
            cosine[:, None] * np.ones((1, nlon)),
        ],
        axis=0,
    )
    return (
        jnp.asarray(legendre, dtype=jnp.float32),
        jnp.asarray(fourier, dtype=jnp.float32),
        jnp.asarray(quad_weight, dtype=jnp.float32),
        jnp.asarray(normals, dtype=jnp.float32),
    )


def legendre_synth(coeff, legendre):
    batch_size, degrees, coef_width = coeff.shape
    orders = legendre.shape[0]
    parted = coeff.reshape(batch_size, degrees, 2, orders)
    return jnp.einsum("mjl,nlcm->njcm", legendre, parted, precision=SPECTRAL)


def fourier_synth(partial_legendre, fourier_rows):
    batch_size, nlat, two, orders = partial_legendre.shape
    return jnp.einsum(
        "njw,wk->njk",
        partial_legendre.reshape(batch_size, nlat, two * orders),
        fourier_rows,
        precision=SPECTRAL,
    )


def analysis_fourier(traction_grid, fourier, quad_weight):
    batch_size, nlat, nlon = traction_grid.shape
    projected = (
        jnp.einsum("bjk,wk->bjw", traction_grid, fourier, precision=SPECTRAL)
        * quad_weight[None, :, None]
    )
    return projected.reshape(batch_size, nlat, 2, fourier.shape[0] // 2)


def analysis_legendre(coef_grid, legendre):
    batch_size = coef_grid.shape[0]
    result = jnp.einsum("mjl,bjcm->blcm", legendre, coef_grid, precision=SPECTRAL)
    return result.reshape(batch_size, legendre.shape[2], 2 * legendre.shape[0])


def prepare(coeffs, keep_mask):
    degrees = coeffs.shape[2]
    degree_value = jnp.arange(degrees, dtype=jnp.float32)
    shape_part = coeffs[:, 0] * keep_mask
    curvature = (
        shape_part * (degree_value * (degree_value + 1.0) / (degrees * degrees))[None, :, None]
    )
    electric = 3.0 * coeffs[:, 1] * keep_mask
    viscous = 3.0 * coeffs[:, 2] * keep_mask * ((degree_value + 2.0) / degrees)[None, :, None]
    return jnp.stack([shape_part, curvature, electric, viscous], axis=1)


def traction(surface, material):
    radius = jnp.exp(surface[:, 0])
    traction_grid = (
        material[:, 0, None, None] * surface[:, 1]
        + 0.5 * surface[:, 2] * surface[:, 2]
        + 2.0 * material[:, 1, None, None] * surface[:, 3]
    )
    return (radius, traction_grid)


def velocity_terms(
    radius, traction_grid, spacing, target_radius, cell_weight, cell_normal, target_normal
):
    load_grid = traction_grid * radius * radius * cell_weight[None, :]
    target_point = spacing[:, :, None] + target_radius[None] * target_normal[:, None, :]
    surface_point = radius[None] * cell_normal[:, None, :]
    offset = target_point[:, :, :, None] - surface_point[:, :, None, :]
    distance_sq = jnp.sum(offset * offset, axis=0)
    softened = distance_sq + SOFTENING
    weight = load_grid[:, None, :] / (softened * jnp.sqrt(softened))
    normal_dot = jnp.sum(offset * cell_normal[:, None, None, :], axis=0)
    stokeslet = weight[None] * (
        cell_normal[:, None, None, :] * (distance_sq + 2.0 * SOFTENING)[None]
        + offset * normal_dot[None]
    )
    return jnp.sum(stokeslet, axis=3) / (8.0 * math.pi)


def per_device(
    coeffs, degree, material, split_coeffs, split_material, separation, reader_dev, reader_slot
):
    drop_count, fields, degrees, coef_width = coeffs.shape
    legendre, fourier, quad_weight, normals = spectral_tables(degrees)
    nlat = legendre.shape[1]
    nlon = fourier.shape[1]
    degree_index = jnp.arange(degrees, dtype=jnp.int32)
    order_full = jnp.arange(coef_width, dtype=jnp.int32) % degrees
    order_mask = (degree_index[:, None] >= order_full[None, :]).astype(jnp.float32)
    keep_mask = order_mask[None] * (degree_index[None, :, None] <= degree[:, None, None]).astype(
        jnp.float32
    )
    prepared = prepare(coeffs, keep_mask)
    partial_legendre = legendre_synth(
        prepared.reshape(drop_count * 4, degrees, coef_width), legendre
    )
    surface = fourier_synth(partial_legendre, fourier).reshape(drop_count, 4, nlat, nlon)
    radius, traction_grid = traction(surface, material)
    traction_coeffs = (
        analysis_legendre(analysis_fourier(traction_grid, fourier, quad_weight), legendre)
        * keep_mask
    )
    split_count = split_coeffs.shape[0]
    half_width = split_coeffs.shape[3]
    half_orders = half_width // 2
    half_index = lax.axis_index("row") % 2
    pair_start = (
        lax.axis_index("row") // 2 * lax.axis_size("col") + lax.axis_index("col")
    ) * split_count
    own_material = lax.dynamic_slice_in_dim(split_material, pair_start, split_count, 0)
    own_order = half_index * half_orders + jnp.arange(half_width, dtype=jnp.int32) % half_orders
    keep_half = (degree_index[:, None] >= own_order[None, :]).astype(jnp.float32)
    own_legendre = lax.dynamic_slice_in_dim(legendre, half_index * half_orders, half_orders, 0)
    own_fourier = lax.dynamic_slice_in_dim(
        fourier.reshape(2, degrees, nlon), half_index * half_orders, half_orders, 1
    ).reshape(half_width, nlon)
    split_prepared = prepare(split_coeffs, keep_half[None])
    split_legendre = legendre_synth(
        split_prepared.reshape(split_count * 4, degrees, half_width), own_legendre
    )
    partial_surface = fourier_synth(split_legendre, own_fourier)
    split_surface = partial_surface + from_partner(
        partial_surface.astype(jnp.bfloat16), "row", 0
    ).astype(partial_surface.dtype)
    split_radius, split_grid = traction(
        split_surface.reshape(split_count, 4, nlat, nlon), own_material
    )
    coef_grid = analysis_fourier(split_grid, fourier, quad_weight)
    own_grid = lax.dynamic_slice_in_dim(coef_grid, half_index * half_orders, half_orders, 3)
    split_traction = analysis_legendre(own_grid, own_legendre) * keep_half[None]
    near_grid = jnp.stack([radius, traction_grid], axis=1).astype(jnp.bfloat16)
    point_grid = near_grid[:, 0, nlat // 4 :: nlat // 2, :: nlon // 2]
    point_count = point_grid.shape[1] * point_grid.shape[2]
    own_points = point_grid.reshape(drop_count, point_count)
    target_normal = normals[:, nlat // 4 :: nlat // 2, :: nlon // 2].reshape(3, point_count)
    devices = lax.axis_size("row") * lax.axis_size("col")
    all_points = lax.all_to_all(
        jnp.broadcast_to(own_points.reshape(1, -1), (devices, drop_count * point_count)),
        ("row", "col"),
        split_axis=0,
        concat_axis=0,
        tiled=True,
    ).reshape(devices * drop_count, point_count)
    total_drops = all_points.shape[0]
    readers = reader_dev.shape[1]
    target = (reader_dev * drop_count + reader_slot).reshape(-1)
    pick = (target[:, None] == jnp.arange(total_drops, dtype=jnp.int32)[None, :]).astype(
        jnp.float32
    )
    target_radius = jnp.dot(pick, all_points.astype(jnp.float32), precision=HIGH)
    target_point = separation.reshape(3, drop_count * readers)[:, :, None] + (
        target_radius[None] * target_normal[:, None, :]
    )
    target_point = jnp.transpose(
        target_point.reshape(3, drop_count, readers * point_count), (1, 2, 0)
    )
    target_square = jnp.sum(target_point * target_point, axis=2, keepdims=True) + SOFTENING
    target_table = jnp.concatenate([target_point, target_square], axis=2).reshape(-1)
    source_radius = near_grid[:, 0].astype(jnp.float32)
    source_traction = near_grid[:, 1].astype(jnp.float32)
    cell_weight = jnp.broadcast_to(quad_weight[:, None], (nlat, nlon))
    partial = near_field(target_table, source_radius, source_traction, normals, cell_weight)
    sums = jnp.sum(partial, axis=3)
    contribution = (
        sums[:, :3] + jnp.transpose(target_point, (0, 2, 1)) * sums[:, 3:]
    ) / (8.0 * math.pi)
    contribution = jnp.transpose(
        contribution.reshape(drop_count, 3, readers, point_count), (0, 2, 1, 3)
    ).reshape(drop_count * readers, 3 * point_count)
    destination = reader_dev.reshape(-1)
    capacity = 2
    onehot = (destination[:, None] == jnp.arange(devices, dtype=jnp.int32)[None, :]).astype(
        jnp.int32
    )
    rank = jnp.sum((jnp.cumsum(onehot, axis=0) - onehot) * onehot, axis=1)
    position = destination * capacity + rank
    place = (position[:, None] == jnp.arange(devices * capacity, dtype=jnp.int32)[None, :]).astype(
        jnp.float32
    )
    record = jnp.concatenate(
        [contribution, reader_slot.reshape(-1, 1).astype(jnp.float32)], axis=1
    )
    outgoing = jnp.dot(jnp.transpose(place), record, precision=HIGH)
    incoming = lax.all_to_all(
        outgoing.reshape(devices, capacity, record.shape[1]),
        ("row", "col"),
        split_axis=0,
        concat_axis=0,
        tiled=True,
    ).reshape(devices * capacity, record.shape[1])
    slot_pick = (
        incoming[:, -1:] == jnp.arange(drop_count, dtype=jnp.float32)[None, :]
    ).astype(jnp.float32)
    mine = jnp.dot(jnp.transpose(slot_pick), incoming[:, :-1], precision=HIGH)
    near_velocity = jnp.transpose(mine.reshape(drop_count, 3, point_count), (1, 0, 2))
    return (traction_coeffs, split_traction, near_velocity.reshape(3, drop_count * point_count))


def near_kernel(t_ref, r_ref, q_ref, n_ref, w_ref, o_ref, s_ref):
    drop = pl.program_id(0)
    targets = o_ref.shape[2]
    chunks = r_ref.shape[1] // 8
    r = r_ref[0]
    s_ref[0] = r
    s_ref[1] = r * r
    s_ref[2] = r + r
    s_ref[3] = q_ref[0] * r * r * w_ref[...]

    def body(t, carry):
        base = (drop * targets + t) * 4
        tx = t_ref[base]
        ty = t_ref[base + 1]
        tz = t_ref[base + 2]
        tt = t_ref[base + 3]
        hx = jnp.zeros((8, 128), jnp.float32)
        hy = jnp.zeros((8, 128), jnp.float32)
        hz = jnp.zeros((8, 128), jnp.float32)
        sq = jnp.zeros((8, 128), jnp.float32)
        for c in range(chunks):
            rows = pl.ds(c * 8, 8)
            nx = n_ref[0, rows, :]
            ny = n_ref[1, rows, :]
            nz = n_ref[2, rows, :]
            rr = s_ref[0, rows, :]
            along = tx * nx + ty * ny + tz * nz
            soft = (tt + s_ref[1, rows, :]) - s_ref[2, rows, :] * along
            inv = lax.rsqrt(soft)
            w = s_ref[3, rows, :] * (inv * inv * inv)
            dn = along - rr
            h = w * ((soft + SOFTENING) - dn * rr)
            hx = hx + h * nx
            hy = hy + h * ny
            hz = hz + h * nz
            sq = sq + w * dn
        o_ref[0, 0, pl.ds(t, 1), :] = jnp.sum(hx, axis=0, keepdims=True)
        o_ref[0, 1, pl.ds(t, 1), :] = jnp.sum(hy, axis=0, keepdims=True)
        o_ref[0, 2, pl.ds(t, 1), :] = jnp.sum(hz, axis=0, keepdims=True)
        o_ref[0, 3, pl.ds(t, 1), :] = jnp.sum(sq, axis=0, keepdims=True)
        return carry

    lax.fori_loop(0, targets, body, 0)


def near_field(target_point, source_radius, source_traction, normals, cell_weight):
    drops, nlat, nlon = source_radius.shape
    targets = target_point.shape[0] // (4 * drops)
    cells = drops * targets * nlat * nlon
    return pl.pallas_call(
        near_kernel,
        grid=(drops,),
        in_specs=[
            pl.BlockSpec(memory_space=pltpu.SMEM),
            pl.BlockSpec((1, nlat, nlon), lambda s: (s, 0, 0)),
            pl.BlockSpec((1, nlat, nlon), lambda s: (s, 0, 0)),
            pl.BlockSpec((3, nlat, nlon), lambda s: (0, 0, 0)),
            pl.BlockSpec((nlat, nlon), lambda s: (0, 0)),
        ],
        out_specs=pl.BlockSpec((1, 4, targets, nlon), lambda s: (s, 0, 0, 0)),
        out_shape=jax.ShapeDtypeStruct((drops, 4, targets, nlon), jnp.float32),
        scratch_shapes=[pltpu.VMEM((4, nlat, nlon), jnp.float32)],
        cost_estimate=pl.CostEstimate(
            flops=26 * cells, transcendentals=cells, bytes_accessed=4 * drops * nlat * nlon * 2
        ),
    )(target_point, source_radius, source_traction, normals, cell_weight)


def solution(mesh):
    in_specs = (
        P(("row", "col"), None, None, None),
        P(("row", "col")),
        P(("row", "col"), None),
        P(("row", "col"), None, None, None),
        P(),
        P(None, ("row", "col"), None),
        P(("row", "col"), None),
        P(("row", "col"), None),
    )
    out_specs = (
        P(("row", "col"), None, None),
        P(("row", "col"), None, None),
        P(None, ("row", "col")),
    )
    return jax.shard_map(
        per_device, mesh=mesh, in_specs=in_specs, out_specs=out_specs, check_vma=False
    )
```

```python
import math

import jax
import jax.numpy as jnp
import numpy as np
from jax import lax
from jax.experimental import pallas as pl
from jax.experimental.pallas import tpu as pltpu
from jax.sharding import PartitionSpec as P

HIGH = lax.Precision.HIGHEST
SPECTRAL = lax.Precision.DEFAULT
SOFTENING = 0.04


def from_partner(block, axis, stride):
    count = lax.axis_size(axis)
    route = []
    for low in range(count):
        high = low | 1 << stride
        if high != low and high < count:
            route += [(low, high), (high, low)]
    return lax.ppermute(block, axis, route)


def spectral_tables(degrees):
    nlon = 2 * degrees
    theta_lat = (np.arange(degrees) + 0.5) * (math.pi / degrees)
    cosine = np.cos(theta_lat)
    sine_theta = np.sin(theta_lat)
    legendre = np.zeros((degrees, degrees, degrees))
    for order in range(degrees):
        log_total = 0.0
        for step_index in range(1, order + 1):
            log_total = log_total + math.log((2.0 * step_index + 1.0) / (2.0 * step_index))
        diag_value = np.exp(0.5 * log_total + order * np.log(sine_theta)) / math.sqrt(4.0 * math.pi)
        legendre[order, :, order] = diag_value
        prev_two = diag_value
        if order + 1 < degrees:
            prev_one = math.sqrt(2.0 * order + 3.0) * cosine * diag_value
            legendre[order, :, order + 1] = prev_one
            for level in range(order + 2, degrees):
                alpha_term = math.sqrt(
                    (4.0 * level * level - 1.0) / (level * level - order * order)
                )
                beta_term = math.sqrt(
                    ((level - 1.0) ** 2 - order * order) / (4.0 * (level - 1.0) ** 2 - 1.0)
                )
                current = alpha_term * (cosine * prev_one - beta_term * prev_two)
                legendre[order, :, level] = current
                prev_two = prev_one
                prev_one = current
    order_index = np.arange(degrees)
    lon_index = np.arange(nlon)
    phase_angle = order_index[:, None] * lon_index[None, :] % nlon * (2.0 * math.pi / nlon)
    fourier = np.concatenate([np.cos(phase_angle), np.sin(phase_angle)], axis=0)
    quad_weight = sine_theta * (math.pi / degrees) * (2.0 * math.pi / nlon)
    longitude = lon_index * (2.0 * math.pi / nlon)
    normals = np.stack(
        [
            sine_theta[:, None] * np.cos(longitude)[None, :],
            sine_theta[:, None] * np.sin(longitude)[None, :],
            cosine[:, None] * np.ones((1, nlon)),
        ],
        axis=0,
    )
    return (
        jnp.asarray(legendre, dtype=jnp.float32),
        jnp.asarray(fourier, dtype=jnp.float32),
        jnp.asarray(quad_weight, dtype=jnp.float32),
        jnp.asarray(normals, dtype=jnp.float32),
    )


def legendre_synth(coeff, legendre):
    batch_size, degrees, _ = coeff.shape
    orders = legendre.shape[0]
    parted = coeff.reshape(batch_size, degrees, 2, orders)
    return jnp.einsum("mjl,nlcm->njcm", legendre, parted, precision=SPECTRAL)


def fourier_synth(partial_legendre, fourier_rows):
    batch_size, nlat, two, orders = partial_legendre.shape
    return jnp.einsum(
        "njw,wk->njk",
        partial_legendre.reshape(batch_size, nlat, two * orders),
        fourier_rows,
        precision=SPECTRAL,
    )


def analysis_fourier(traction_grid, fourier, quad_weight):
    batch_size, nlat, _ = traction_grid.shape
    projected = (
        jnp.einsum("bjk,wk->bjw", traction_grid, fourier, precision=SPECTRAL)
        * quad_weight[None, :, None]
    )
    return projected.reshape(batch_size, nlat, 2, fourier.shape[0] // 2)


def analysis_legendre(coef_grid, legendre):
    batch_size = coef_grid.shape[0]
    result = jnp.einsum("mjl,bjcm->blcm", legendre, coef_grid, precision=SPECTRAL)
    return result.reshape(batch_size, legendre.shape[2], 2 * legendre.shape[0])


def prepare(coeffs, keep_mask):
    degrees = coeffs.shape[2]
    degree_value = jnp.arange(degrees, dtype=jnp.float32)
    shape_part = coeffs[:, 0] * keep_mask
    curvature = (
        shape_part * (degree_value * (degree_value + 1.0) / (degrees * degrees))[None, :, None]
    )
    electric = 3.0 * coeffs[:, 1] * keep_mask
    viscous = 3.0 * coeffs[:, 2] * keep_mask * ((degree_value + 2.0) / degrees)[None, :, None]
    return jnp.stack([shape_part, curvature, electric, viscous], axis=1)


def traction(surface, material):
    radius = jnp.exp(surface[:, 0])
    traction_grid = (
        material[:, 0, None, None] * surface[:, 1]
        + 0.5 * surface[:, 2] * surface[:, 2]
        + 2.0 * material[:, 1, None, None] * surface[:, 3]
    )
    return (radius, traction_grid)


def per_device(
    coeffs, degree, material, split_coeffs, split_material, separation, reader_dev, reader_slot
):
    drop_count, _, degrees, coef_width = coeffs.shape
    legendre, fourier, quad_weight, normals = spectral_tables(degrees)
    nlat = legendre.shape[1]
    nlon = fourier.shape[1]
    degree_index = jnp.arange(degrees, dtype=jnp.int32)
    order_full = jnp.arange(coef_width, dtype=jnp.int32) % degrees
    order_mask = (degree_index[:, None] >= order_full[None, :]).astype(jnp.float32)
    keep_mask = order_mask[None] * (degree_index[None, :, None] <= degree[:, None, None]).astype(
        jnp.float32
    )
    prepared = prepare(coeffs, keep_mask)
    partial_legendre = legendre_synth(
        prepared.reshape(drop_count * 4, degrees, coef_width), legendre
    )
    surface = fourier_synth(partial_legendre, fourier).reshape(drop_count, 4, nlat, nlon)
    radius, traction_grid = traction(surface, material)
    split_count = split_coeffs.shape[0]
    half_width = split_coeffs.shape[3]
    half_orders = half_width // 2
    half_index = lax.axis_index("row") % 2
    pair_start = (
        lax.axis_index("row") // 2 * lax.axis_size("col") + lax.axis_index("col")
    ) * split_count
    own_material = lax.dynamic_slice_in_dim(split_material, pair_start, split_count, 0)
    own_order = half_index * half_orders + jnp.arange(half_width, dtype=jnp.int32) % half_orders
    keep_half = (degree_index[:, None] >= own_order[None, :]).astype(jnp.float32)
    own_legendre = lax.dynamic_slice_in_dim(legendre, half_index * half_orders, half_orders, 0)
    own_fourier = lax.dynamic_slice_in_dim(
        fourier.reshape(2, degrees, nlon), half_index * half_orders, half_orders, 1
    ).reshape(half_width, nlon)
    split_prepared = prepare(split_coeffs, keep_half[None])
    split_legendre = legendre_synth(
        split_prepared.reshape(split_count * 4, degrees, half_width), own_legendre
    )
    partial_surface = fourier_synth(split_legendre, own_fourier)
    split_surface = partial_surface + from_partner(
        partial_surface.astype(jnp.bfloat16), "row", 0
    ).astype(partial_surface.dtype)
    _, split_grid = traction(split_surface.reshape(split_count, 4, nlat, nlon), own_material)
    near_grid = jnp.stack([radius, traction_grid], axis=1).astype(jnp.bfloat16)
    point_grid = near_grid[:, 0, nlat // 4 :: nlat // 2, :: nlon // 2]
    point_count = point_grid.shape[1] * point_grid.shape[2]
    own_points = point_grid.reshape(drop_count, point_count)
    target_normal = normals[:, nlat // 4 :: nlat // 2, :: nlon // 2].reshape(3, point_count)
    devices = lax.axis_size("row") * lax.axis_size("col")
    all_points = lax.all_to_all(
        jnp.broadcast_to(own_points.reshape(1, -1), (devices, drop_count * point_count)),
        ("row", "col"),
        split_axis=0,
        concat_axis=0,
        tiled=True,
    ).reshape(devices * drop_count, point_count)
    total_drops = all_points.shape[0]
    readers = reader_dev.shape[1]
    target = (reader_dev * drop_count + reader_slot).reshape(-1)
    pick = (target[:, None] == jnp.arange(total_drops, dtype=jnp.int32)[None, :]).astype(
        jnp.float32
    )
    target_radius = jnp.dot(pick, all_points.astype(jnp.float32), precision=HIGH)
    target_point = separation.reshape(3, drop_count * readers)[:, :, None] + (
        target_radius[None] * target_normal[:, None, :]
    )
    target_point = jnp.transpose(
        target_point.reshape(3, drop_count, readers * point_count), (1, 2, 0)
    )
    target_square = jnp.sum(target_point * target_point, axis=2, keepdims=True) + SOFTENING
    target_table = jnp.concatenate([target_point, target_square], axis=2).reshape(-1)
    source_radius = near_grid[:, 0].astype(jnp.float32)
    source_traction = near_grid[:, 1].astype(jnp.float32)
    cell_weight = jnp.broadcast_to(quad_weight[:, None], (nlat, nlon))
    partial = near_field(target_table, source_radius, source_traction, normals, cell_weight)
    partial, traction_grid, split_grid = lax.optimization_barrier(
        (partial, traction_grid, split_grid)
    )
    sums = jnp.sum(partial, axis=3)
    contribution = (
        sums[:, :3] + jnp.transpose(target_point, (0, 2, 1)) * sums[:, 3:]
    ) / (8.0 * math.pi)
    contribution = jnp.transpose(
        contribution.reshape(drop_count, 3, readers, point_count), (0, 2, 1, 3)
    ).reshape(drop_count * readers, 3 * point_count)
    destination = reader_dev.reshape(-1)
    capacity = 2
    onehot = (destination[:, None] == jnp.arange(devices, dtype=jnp.int32)[None, :]).astype(
        jnp.int32
    )
    rank = jnp.sum((jnp.cumsum(onehot, axis=0) - onehot) * onehot, axis=1)
    position = destination * capacity + rank
    place = (position[:, None] == jnp.arange(devices * capacity, dtype=jnp.int32)[None, :]).astype(
        jnp.float32
    )
    record = jnp.concatenate(
        [contribution, reader_slot.reshape(-1, 1).astype(jnp.float32)], axis=1
    )
    outgoing = jnp.dot(jnp.transpose(place), record, precision=HIGH)
    incoming = lax.all_to_all(
        outgoing.reshape(devices, capacity, record.shape[1]),
        ("row", "col"),
        split_axis=0,
        concat_axis=0,
        tiled=True,
    ).reshape(devices * capacity, record.shape[1])
    slot_pick = (
        incoming[:, -1:] == jnp.arange(drop_count, dtype=jnp.float32)[None, :]
    ).astype(jnp.float32)
    mine = jnp.dot(jnp.transpose(slot_pick), incoming[:, :-1], precision=HIGH)
    near_velocity = jnp.transpose(mine.reshape(drop_count, 3, point_count), (1, 0, 2))
    traction_coeffs = (
        analysis_legendre(analysis_fourier(traction_grid, fourier, quad_weight), legendre)
        * keep_mask
    )
    coef_grid = analysis_fourier(split_grid, fourier, quad_weight)
    own_grid = lax.dynamic_slice_in_dim(coef_grid, half_index * half_orders, half_orders, 3)
    split_traction = analysis_legendre(own_grid, own_legendre) * keep_half[None]
    return (traction_coeffs, split_traction, near_velocity.reshape(3, drop_count * point_count))


def near_kernel(t_ref, r_ref, q_ref, n_ref, w_ref, o_ref, s_ref):
    drop = pl.program_id(0)
    targets = o_ref.shape[2]
    chunks = r_ref.shape[1] // 8
    r = r_ref[0]
    s_ref[0] = r
    s_ref[1] = r * r
    s_ref[2] = r + r
    s_ref[3] = q_ref[0] * r * r * w_ref[...]

    def body(t, carry):
        base = (drop * targets + t) * 4
        tx = t_ref[base]
        ty = t_ref[base + 1]
        tz = t_ref[base + 2]
        tt = t_ref[base + 3]
        hx = jnp.zeros((8, 128), jnp.float32)
        hy = jnp.zeros((8, 128), jnp.float32)
        hz = jnp.zeros((8, 128), jnp.float32)
        sq = jnp.zeros((8, 128), jnp.float32)
        for c in range(chunks):
            rows = pl.ds(c * 8, 8)
            nx = n_ref[0, rows, :]
            ny = n_ref[1, rows, :]
            nz = n_ref[2, rows, :]
            rr = s_ref[0, rows, :]
            along = tx * nx + ty * ny + tz * nz
            soft = (tt + s_ref[1, rows, :]) - s_ref[2, rows, :] * along
            inv = lax.rsqrt(soft)
            w = s_ref[3, rows, :] * (inv * inv * inv)
            dn = along - rr
            h = w * ((soft + SOFTENING) - dn * rr)
            hx = hx + h * nx
            hy = hy + h * ny
            hz = hz + h * nz
            sq = sq + w * dn
        o_ref[0, 0, pl.ds(t, 1), :] = jnp.sum(hx, axis=0, keepdims=True)
        o_ref[0, 1, pl.ds(t, 1), :] = jnp.sum(hy, axis=0, keepdims=True)
        o_ref[0, 2, pl.ds(t, 1), :] = jnp.sum(hz, axis=0, keepdims=True)
        o_ref[0, 3, pl.ds(t, 1), :] = jnp.sum(sq, axis=0, keepdims=True)
        return carry

    lax.fori_loop(0, targets, body, 0)


def near_field(target_point, source_radius, source_traction, normals, cell_weight):
    drops, nlat, nlon = source_radius.shape
    targets = target_point.shape[0] // (4 * drops)
    cells = drops * targets * nlat * nlon
    return pl.pallas_call(
        near_kernel,
        grid=(drops,),
        in_specs=[
            pl.BlockSpec(memory_space=pltpu.SMEM),
            pl.BlockSpec((1, nlat, nlon), lambda s: (s, 0, 0)),
            pl.BlockSpec((1, nlat, nlon), lambda s: (s, 0, 0)),
            pl.BlockSpec((3, nlat, nlon), lambda s: (0, 0, 0)),
            pl.BlockSpec((nlat, nlon), lambda s: (0, 0)),
        ],
        out_specs=pl.BlockSpec((1, 4, targets, nlon), lambda s: (s, 0, 0, 0)),
        out_shape=jax.ShapeDtypeStruct((drops, 4, targets, nlon), jnp.float32),
        scratch_shapes=[pltpu.VMEM((4, nlat, nlon), jnp.float32)],
        cost_estimate=pl.CostEstimate(
            flops=26 * cells, transcendentals=cells, bytes_accessed=4 * drops * nlat * nlon * 2
        ),
    )(target_point, source_radius, source_traction, normals, cell_weight)


def solution(mesh):
    in_specs = (
        P(("row", "col"), None, None, None),
        P(("row", "col")),
        P(("row", "col"), None),
        P(("row", "col"), None, None, None),
        P(),
        P(None, ("row", "col"), None),
        P(("row", "col"), None),
        P(("row", "col"), None),
    )
    out_specs = (
        P(("row", "col"), None, None),
        P(("row", "col"), None, None),
        P(None, ("row", "col")),
    )
    return jax.shard_map(
        per_device, mesh=mesh, in_specs=in_specs, out_specs=out_specs, check_vma=False
    )
```

```python
import functools
import math

import jax
import jax.numpy as jnp
import numpy as np
from jax import lax
from jax.experimental import pallas as pl
from jax.experimental.pallas import tpu as pltpu
from jax.sharding import PartitionSpec as P

HIGH = lax.Precision.HIGHEST
SPECTRAL = lax.Precision.DEFAULT
SOFTENING = 0.04


def from_partner(block, axis, stride):
    count = lax.axis_size(axis)
    route = []
    for low in range(count):
        high = low | 1 << stride
        if high != low and high < count:
            route += [(low, high), (high, low)]
    return lax.ppermute(block, axis, route)


def spectral_tables(degrees):
    nlon = 2 * degrees
    theta_lat = (np.arange(degrees) + 0.5) * (math.pi / degrees)
    cosine = np.cos(theta_lat)
    sine_theta = np.sin(theta_lat)
    legendre = np.zeros((degrees, degrees, degrees))
    for order in range(degrees):
        log_total = 0.0
        for step_index in range(1, order + 1):
            log_total = log_total + math.log((2.0 * step_index + 1.0) / (2.0 * step_index))
        diag_value = np.exp(0.5 * log_total + order * np.log(sine_theta)) / math.sqrt(4.0 * math.pi)
        legendre[order, :, order] = diag_value
        prev_two = diag_value
        if order + 1 < degrees:
            prev_one = math.sqrt(2.0 * order + 3.0) * cosine * diag_value
            legendre[order, :, order + 1] = prev_one
            for level in range(order + 2, degrees):
                alpha_term = math.sqrt(
                    (4.0 * level * level - 1.0) / (level * level - order * order)
                )
                beta_term = math.sqrt(
                    ((level - 1.0) ** 2 - order * order) / (4.0 * (level - 1.0) ** 2 - 1.0)
                )
                current = alpha_term * (cosine * prev_one - beta_term * prev_two)
                legendre[order, :, level] = current
                prev_two = prev_one
                prev_one = current
    order_index = np.arange(degrees)
    lon_index = np.arange(nlon)
    phase_angle = order_index[:, None] * lon_index[None, :] % nlon * (2.0 * math.pi / nlon)
    fourier = np.concatenate([np.cos(phase_angle), np.sin(phase_angle)], axis=0)
    quad_weight = sine_theta * (math.pi / degrees) * (2.0 * math.pi / nlon)
    longitude = lon_index * (2.0 * math.pi / nlon)
    normals = np.stack(
        [
            sine_theta[:, None] * np.cos(longitude)[None, :],
            sine_theta[:, None] * np.sin(longitude)[None, :],
            cosine[:, None] * np.ones((1, nlon)),
        ],
        axis=0,
    )
    return (
        jnp.asarray(legendre, dtype=jnp.float32),
        jnp.asarray(fourier, dtype=jnp.float32),
        jnp.asarray(quad_weight, dtype=jnp.float32),
        jnp.asarray(normals, dtype=jnp.float32),
    )


def legendre_synth(coeff, legendre):
    batch_size, degrees, _ = coeff.shape
    orders = legendre.shape[0]
    parted = coeff.reshape(batch_size, degrees, 2, orders)
    return jnp.einsum("mjl,nlcm->njcm", legendre, parted, precision=SPECTRAL)


def fourier_synth(partial_legendre, fourier_rows):
    batch_size, nlat, two, orders = partial_legendre.shape
    return jnp.einsum(
        "njw,wk->njk",
        partial_legendre.reshape(batch_size, nlat, two * orders),
        fourier_rows,
        precision=SPECTRAL,
    )


def analysis_fourier(traction_grid, fourier, quad_weight):
    batch_size, nlat, _ = traction_grid.shape
    projected = (
        jnp.einsum("bjk,wk->bjw", traction_grid, fourier, precision=SPECTRAL)
        * quad_weight[None, :, None]
    )
    return projected.reshape(batch_size, nlat, 2, fourier.shape[0] // 2)


def analysis_legendre(coef_grid, legendre):
    batch_size = coef_grid.shape[0]
    result = jnp.einsum("mjl,bjcm->blcm", legendre, coef_grid, precision=SPECTRAL)
    return result.reshape(batch_size, legendre.shape[2], 2 * legendre.shape[0])


def prepare(coeffs, keep_mask):
    degrees = coeffs.shape[2]
    degree_value = jnp.arange(degrees, dtype=jnp.float32)
    shape_part = coeffs[:, 0] * keep_mask
    curvature = (
        shape_part * (degree_value * (degree_value + 1.0) / (degrees * degrees))[None, :, None]
    )
    electric = 3.0 * coeffs[:, 1] * keep_mask
    viscous = 3.0 * coeffs[:, 2] * keep_mask * ((degree_value + 2.0) / degrees)[None, :, None]
    return jnp.stack([shape_part, curvature, electric, viscous], axis=1)


def traction(surface, material):
    radius = jnp.exp(surface[:, 0])
    traction_grid = (
        material[:, 0, None, None] * surface[:, 1]
        + 0.5 * surface[:, 2] * surface[:, 2]
        + 2.0 * material[:, 1, None, None] * surface[:, 3]
    )
    return (radius, traction_grid)


def per_device(
    coeffs, degree, material, split_coeffs, split_material, separation, reader_dev, reader_slot
):
    drop_count, _, degrees, coef_width = coeffs.shape
    legendre, fourier, quad_weight, normals = spectral_tables(degrees)
    nlat = legendre.shape[1]
    nlon = fourier.shape[1]
    degree_index = jnp.arange(degrees, dtype=jnp.int32)
    order_full = jnp.arange(coef_width, dtype=jnp.int32) % degrees
    order_mask = (degree_index[:, None] >= order_full[None, :]).astype(jnp.float32)
    keep_mask = order_mask[None] * (degree_index[None, :, None] <= degree[:, None, None]).astype(
        jnp.float32
    )
    prepared = prepare(coeffs, keep_mask)
    partial_legendre = legendre_synth(
        prepared.reshape(drop_count * 4, degrees, coef_width), legendre
    )
    surface = fourier_synth(partial_legendre, fourier).reshape(drop_count, 4, nlat, nlon)
    radius, traction_grid = traction(surface, material)
    split_count = split_coeffs.shape[0]
    half_width = split_coeffs.shape[3]
    half_orders = half_width // 2
    half_index = lax.axis_index("row") % 2
    pair_start = (
        lax.axis_index("row") // 2 * lax.axis_size("col") + lax.axis_index("col")
    ) * split_count
    own_material = lax.dynamic_slice_in_dim(split_material, pair_start, split_count, 0)
    own_order = half_index * half_orders + jnp.arange(half_width, dtype=jnp.int32) % half_orders
    keep_half = (degree_index[:, None] >= own_order[None, :]).astype(jnp.float32)
    own_legendre = lax.dynamic_slice_in_dim(legendre, half_index * half_orders, half_orders, 0)
    own_fourier = lax.dynamic_slice_in_dim(
        fourier.reshape(2, degrees, nlon), half_index * half_orders, half_orders, 1
    ).reshape(half_width, nlon)
    split_prepared = prepare(split_coeffs, keep_half[None])
    split_legendre = legendre_synth(
        split_prepared.reshape(split_count * 4, degrees, half_width), own_legendre
    )
    partial_surface = fourier_synth(split_legendre, own_fourier)
    split_surface = partial_surface + from_partner(
        partial_surface.astype(jnp.bfloat16), "row", 0
    ).astype(partial_surface.dtype)
    _, split_grid = traction(split_surface.reshape(split_count, 4, nlat, nlon), own_material)
    near_grid = jnp.stack([radius, traction_grid], axis=1).astype(jnp.bfloat16)
    point_grid = radius[:, nlat // 4 :: nlat // 2, :: nlon // 2].astype(jnp.bfloat16)
    point_count = point_grid.shape[1] * point_grid.shape[2]
    own_points = point_grid.reshape(drop_count, point_count)
    target_normal = normals[:, nlat // 4 :: nlat // 2, :: nlon // 2].reshape(3, point_count)
    devices = lax.axis_size("row") * lax.axis_size("col")
    all_points = lax.all_to_all(
        jnp.broadcast_to(own_points.reshape(1, -1), (devices, drop_count * point_count)),
        ("row", "col"),
        split_axis=0,
        concat_axis=0,
        tiled=True,
    ).reshape(devices * drop_count, point_count)
    total_drops = all_points.shape[0]
    readers = reader_dev.shape[1]
    target = (reader_dev * drop_count + reader_slot).reshape(-1)
    pick = (target[:, None] == jnp.arange(total_drops, dtype=jnp.int32)[None, :]).astype(
        jnp.float32
    )
    target_radius = jnp.dot(pick, all_points.astype(jnp.float32), precision=HIGH)
    target_point = separation.reshape(3, drop_count * readers)[:, :, None] + (
        target_radius[None] * target_normal[:, None, :]
    )
    target_point = jnp.transpose(
        target_point.reshape(3, drop_count, readers * point_count), (1, 2, 0)
    )
    target_square = jnp.sum(target_point * target_point, axis=2) + SOFTENING
    entry_table = jnp.concatenate(
        [
            jnp.transpose(separation, (1, 2, 0)),
            target_radius.reshape(drop_count, readers, point_count),
            target_square.reshape(drop_count, readers, point_count),
        ],
        axis=2,
    ).reshape(-1)
    cell_table = cell_tables(nlat, nlon, point_count)
    partial = near_field(entry_table, near_grid, cell_table, readers, point_count)
    partial, traction_grid, split_grid = lax.optimization_barrier(
        (partial, traction_grid, split_grid)
    )
    sums = jnp.sum(partial, axis=3)
    contribution = (
        sums[:, :3] + jnp.transpose(target_point, (0, 2, 1)) * sums[:, 3:]
    ) / (8.0 * math.pi)
    contribution = jnp.transpose(
        contribution.reshape(drop_count, 3, readers, point_count), (0, 2, 1, 3)
    ).reshape(drop_count * readers, 3 * point_count)
    destination = reader_dev.reshape(-1)
    capacity = 2
    onehot = (destination[:, None] == jnp.arange(devices, dtype=jnp.int32)[None, :]).astype(
        jnp.int32
    )
    rank = jnp.sum((jnp.cumsum(onehot, axis=0) - onehot) * onehot, axis=1)
    position = destination * capacity + rank
    place = (position[:, None] == jnp.arange(devices * capacity, dtype=jnp.int32)[None, :]).astype(
        jnp.float32
    )
    record = jnp.concatenate(
        [contribution, reader_slot.reshape(-1, 1).astype(jnp.float32)], axis=1
    )
    outgoing = jnp.dot(jnp.transpose(place), record, precision=HIGH)
    incoming = lax.all_to_all(
        outgoing.reshape(devices, capacity, record.shape[1]),
        ("row", "col"),
        split_axis=0,
        concat_axis=0,
        tiled=True,
    ).reshape(devices * capacity, record.shape[1])
    slot_pick = (
        incoming[:, -1:] == jnp.arange(drop_count, dtype=jnp.float32)[None, :]
    ).astype(jnp.float32)
    mine = jnp.dot(jnp.transpose(slot_pick), incoming[:, :-1], precision=HIGH)
    near_velocity = jnp.transpose(mine.reshape(drop_count, 3, point_count), (1, 0, 2))
    traction_coeffs = (
        analysis_legendre(analysis_fourier(traction_grid, fourier, quad_weight), legendre)
        * keep_mask
    )
    coef_grid = analysis_fourier(split_grid, fourier, quad_weight)
    own_grid = lax.dynamic_slice_in_dim(coef_grid, half_index * half_orders, half_orders, 3)
    split_traction = analysis_legendre(own_grid, own_legendre) * keep_half[None]
    return (traction_coeffs, split_traction, near_velocity.reshape(3, drop_count * point_count))


def cell_tables(nlat, nlon, point_count):
    theta = (np.arange(nlat) + 0.5) * (math.pi / nlat)
    longitude = np.arange(nlon) * (2.0 * math.pi / nlon)
    quad_weight = (np.sin(theta) * (math.pi / nlat) * (2.0 * math.pi / nlon)).astype(np.float32)
    normals = np.stack(
        [
            np.sin(theta)[:, None] * np.cos(longitude)[None, :],
            np.sin(theta)[:, None] * np.sin(longitude)[None, :],
            np.cos(theta)[:, None] * np.ones((1, nlon)),
        ],
        axis=0,
    ).astype(np.float32)
    points = normals[:, nlat // 4 :: nlat // 2, :: nlon // 2].reshape(3, point_count)
    facing = np.einsum("dp,djk->pjk", points.astype(np.float64), normals.astype(np.float64))
    weight = np.broadcast_to(quad_weight[None, :, None], (1, nlat, nlon))
    table = np.concatenate([normals, facing.astype(np.float32), weight], axis=0)
    return jnp.asarray(table, dtype=jnp.float32)


def near_kernel(points, t_ref, g_ref, c_ref, o_ref, s_ref):
    drop = pl.program_id(0)
    entries = o_ref.shape[2] // points
    width = 3 + 2 * points
    chunks = g_ref.shape[2] // 8
    r = g_ref[0, 0].astype(jnp.float32)
    s_ref[0] = r
    s_ref[1] = r * r
    s_ref[2] = r + r
    s_ref[3] = g_ref[0, 1].astype(jnp.float32) * r * r * c_ref[3 + points]

    def body(e, carry):
        base = (drop * entries + e) * width
        sx = t_ref[base]
        sy = t_ref[base + 1]
        sz = t_ref[base + 2]
        lift = [t_ref[base + 3 + k] for k in range(points)]
        tt = [t_ref[base + 3 + points + k] for k in range(points)]
        acc = [[jnp.zeros((8, 128), jnp.float32) for _ in range(4)] for _ in range(points)]
        for c in range(chunks):
            rows = pl.ds(c * 8, 8)
            nx = c_ref[0, rows, :]
            ny = c_ref[1, rows, :]
            nz = c_ref[2, rows, :]
            rr = s_ref[0, rows, :]
            r2 = s_ref[1, rows, :]
            twice = s_ref[2, rows, :]
            load = s_ref[3, rows, :]
            shared = sx * nx + sy * ny + sz * nz
            for k in range(points):
                along = shared + lift[k] * c_ref[3 + k, rows, :]
                soft = (tt[k] + r2) - twice * along
                inv = lax.rsqrt(soft)
                w = load * (inv * inv * inv)
                dn = along - rr
                h = w * ((soft + SOFTENING) - dn * rr)
                hx, hy, hz, sq = acc[k]
                acc[k] = [hx + h * nx, hy + h * ny, hz + h * nz, sq + w * dn]
        for k in range(points):
            row = pl.ds(e * points + k, 1)
            for comp in range(4):
                o_ref[0, comp, row, :] = jnp.sum(acc[k][comp], axis=0, keepdims=True)
        return carry

    lax.fori_loop(0, entries, body, 0)


def near_field(entry_table, near_grid, cell_table, readers, points):
    drops, fields, nlat, nlon = near_grid.shape
    targets = readers * points
    cells = drops * targets * nlat * nlon
    return pl.pallas_call(
        functools.partial(near_kernel, points),
        grid=(drops,),
        in_specs=[
            pl.BlockSpec(memory_space=pltpu.SMEM),
            pl.BlockSpec((1, fields, nlat, nlon), lambda s: (s, 0, 0, 0)),
            pl.BlockSpec(cell_table.shape, lambda s: (0, 0, 0)),
        ],
        out_specs=pl.BlockSpec((1, 4, targets, nlon), lambda s: (s, 0, 0, 0)),
        out_shape=jax.ShapeDtypeStruct((drops, 4, targets, nlon), jnp.float32),
        scratch_shapes=[pltpu.VMEM((4, nlat, nlon), jnp.float32)],
        cost_estimate=pl.CostEstimate(
            flops=24 * cells, transcendentals=cells, bytes_accessed=2 * drops * fields * nlat * nlon
        ),
    )(entry_table, near_grid, cell_table)


def solution(mesh):
    in_specs = (
        P(("row", "col"), None, None, None),
        P(("row", "col")),
        P(("row", "col"), None),
        P(("row", "col"), None, None, None),
        P(),
        P(None, ("row", "col"), None),
        P(("row", "col"), None),
        P(("row", "col"), None),
    )
    out_specs = (
        P(("row", "col"), None, None),
        P(("row", "col"), None, None),
        P(None, ("row", "col")),
    )
    return jax.shard_map(
        per_device, mesh=mesh, in_specs=in_specs, out_specs=out_specs, check_vma=False
    )
```

```python
import functools
import math

import jax
import jax.numpy as jnp
import numpy as np
from jax import lax
from jax.experimental import pallas as pl
from jax.experimental.pallas import tpu as pltpu
from jax.sharding import PartitionSpec as P

HIGH = lax.Precision.HIGHEST
SPECTRAL = lax.Precision.DEFAULT
SOFTENING = 0.04


def from_partner(block, axis, stride):
    count = lax.axis_size(axis)
    route = []
    for low in range(count):
        high = low | 1 << stride
        if high != low and high < count:
            route += [(low, high), (high, low)]
    return lax.ppermute(block, axis, route)


def spectral_tables(degrees):
    nlon = 2 * degrees
    theta_lat = (np.arange(degrees) + 0.5) * (math.pi / degrees)
    cosine = np.cos(theta_lat)
    sine_theta = np.sin(theta_lat)
    legendre = np.zeros((degrees, degrees, degrees))
    for order in range(degrees):
        log_total = 0.0
        for step_index in range(1, order + 1):
            log_total = log_total + math.log((2.0 * step_index + 1.0) / (2.0 * step_index))
        diag_value = np.exp(0.5 * log_total + order * np.log(sine_theta)) / math.sqrt(4.0 * math.pi)
        legendre[order, :, order] = diag_value
        prev_two = diag_value
        if order + 1 < degrees:
            prev_one = math.sqrt(2.0 * order + 3.0) * cosine * diag_value
            legendre[order, :, order + 1] = prev_one
            for level in range(order + 2, degrees):
                alpha_term = math.sqrt(
                    (4.0 * level * level - 1.0) / (level * level - order * order)
                )
                beta_term = math.sqrt(
                    ((level - 1.0) ** 2 - order * order) / (4.0 * (level - 1.0) ** 2 - 1.0)
                )
                current = alpha_term * (cosine * prev_one - beta_term * prev_two)
                legendre[order, :, level] = current
                prev_two = prev_one
                prev_one = current
    order_index = np.arange(degrees)
    lon_index = np.arange(nlon)
    phase_angle = order_index[:, None] * lon_index[None, :] % nlon * (2.0 * math.pi / nlon)
    fourier = np.concatenate([np.cos(phase_angle), np.sin(phase_angle)], axis=0)
    quad_weight = sine_theta * (math.pi / degrees) * (2.0 * math.pi / nlon)
    longitude = lon_index * (2.0 * math.pi / nlon)
    normals = np.stack(
        [
            sine_theta[:, None] * np.cos(longitude)[None, :],
            sine_theta[:, None] * np.sin(longitude)[None, :],
            cosine[:, None] * np.ones((1, nlon)),
        ],
        axis=0,
    )
    return (
        jnp.asarray(legendre, dtype=jnp.float32),
        jnp.asarray(fourier, dtype=jnp.float32),
        jnp.asarray(quad_weight, dtype=jnp.float32),
        jnp.asarray(normals, dtype=jnp.float32),
    )


def spectral_tables_np(degrees):
    nlon = 2 * degrees
    theta_lat = (np.arange(degrees) + 0.5) * (math.pi / degrees)
    cosine = np.cos(theta_lat)
    sine_theta = np.sin(theta_lat)
    legendre = np.zeros((degrees, degrees, degrees))
    for order in range(degrees):
        log_total = 0.0
        for step_index in range(1, order + 1):
            log_total = log_total + math.log((2.0 * step_index + 1.0) / (2.0 * step_index))
        diag_value = np.exp(0.5 * log_total + order * np.log(sine_theta)) / math.sqrt(4.0 * math.pi)
        legendre[order, :, order] = diag_value
        prev_two = diag_value
        if order + 1 < degrees:
            prev_one = math.sqrt(2.0 * order + 3.0) * cosine * diag_value
            legendre[order, :, order + 1] = prev_one
            for level in range(order + 2, degrees):
                alpha_term = math.sqrt(
                    (4.0 * level * level - 1.0) / (level * level - order * order)
                )
                beta_term = math.sqrt(
                    ((level - 1.0) ** 2 - order * order) / (4.0 * (level - 1.0) ** 2 - 1.0)
                )
                current = alpha_term * (cosine * prev_one - beta_term * prev_two)
                legendre[order, :, level] = current
                prev_two = prev_one
                prev_one = current
    order_index = np.arange(degrees)
    lon_index = np.arange(nlon)
    phase_angle = order_index[:, None] * lon_index[None, :] % nlon * (2.0 * math.pi / nlon)
    fourier = np.concatenate([np.cos(phase_angle), np.sin(phase_angle)], axis=0)
    quad_weight = sine_theta * (math.pi / degrees) * (2.0 * math.pi / nlon)
    longitude = lon_index * (2.0 * math.pi / nlon)
    normals = np.stack(
        [
            sine_theta[:, None] * np.cos(longitude)[None, :],
            sine_theta[:, None] * np.sin(longitude)[None, :],
            cosine[:, None] * np.ones((1, nlon)),
        ],
        axis=0,
    )
    return (
        legendre.astype(np.float32),
        fourier.astype(np.float32),
        quad_weight.astype(np.float32),
        normals.astype(np.float32),
    )


def legendre_synth(coeff, legendre):
    batch_size, degrees, _ = coeff.shape
    orders = legendre.shape[0]
    parted = coeff.reshape(batch_size, degrees, 2, orders)
    return jnp.einsum("mjl,nlcm->njcm", legendre, parted, precision=SPECTRAL)


def fourier_synth(partial_legendre, fourier_rows):
    batch_size, nlat, two, orders = partial_legendre.shape
    return jnp.einsum(
        "njw,wk->njk",
        partial_legendre.reshape(batch_size, nlat, two * orders),
        fourier_rows,
        precision=SPECTRAL,
    )


def analysis_fourier(traction_grid, fourier, quad_weight):
    batch_size, nlat, _ = traction_grid.shape
    projected = (
        jnp.einsum("bjk,wk->bjw", traction_grid, fourier, precision=SPECTRAL)
        * quad_weight[None, :, None]
    )
    return projected.reshape(batch_size, nlat, 2, fourier.shape[0] // 2)


def analysis_legendre(coef_grid, legendre):
    batch_size = coef_grid.shape[0]
    result = jnp.einsum("mjl,bjcm->blcm", legendre, coef_grid, precision=SPECTRAL)
    return result.reshape(batch_size, legendre.shape[2], 2 * legendre.shape[0])


def prepare(coeffs, keep_mask):
    degrees = coeffs.shape[2]
    degree_value = jnp.arange(degrees, dtype=jnp.float32)
    shape_part = coeffs[:, 0] * keep_mask
    curvature = (
        shape_part * (degree_value * (degree_value + 1.0) / (degrees * degrees))[None, :, None]
    )
    electric = 3.0 * coeffs[:, 1] * keep_mask
    viscous = 3.0 * coeffs[:, 2] * keep_mask * ((degree_value + 2.0) / degrees)[None, :, None]
    return jnp.stack([shape_part, curvature, electric, viscous], axis=1)


def traction(surface, material):
    radius = jnp.exp(surface[:, 0])
    traction_grid = (
        material[:, 0, None, None] * surface[:, 1]
        + 0.5 * surface[:, 2] * surface[:, 2]
        + 2.0 * material[:, 1, None, None] * surface[:, 3]
    )
    return (radius, traction_grid)


def per_device(
    coeffs, degree, material, split_coeffs, split_material, separation, reader_dev, reader_slot
):
    drop_count, _, degrees, coef_width = coeffs.shape
    legendre, fourier, quad_weight, normals = spectral_tables(degrees)
    nlat = legendre.shape[1]
    nlon = fourier.shape[1]
    degree_index = jnp.arange(degrees, dtype=jnp.int32)
    order_full = jnp.arange(coef_width, dtype=jnp.int32) % degrees
    order_mask = (degree_index[:, None] >= order_full[None, :]).astype(jnp.float32)
    keep_mask = order_mask[None] * (degree_index[None, :, None] <= degree[:, None, None]).astype(
        jnp.float32
    )
    prepared = prepare(coeffs, keep_mask)
    point_weight = point_table(degrees)
    point_surface = jnp.dot(
        prepared[:, 0].reshape(drop_count, degrees * coef_width), point_weight, precision=HIGH
    )
    own_points = jnp.exp(point_surface).astype(jnp.bfloat16)
    partial_legendre = legendre_synth(
        prepared.reshape(drop_count * 4, degrees, coef_width), legendre
    )
    surface = fourier_synth(partial_legendre, fourier).reshape(drop_count, 4, nlat, nlon)
    radius, traction_grid = traction(surface, material)
    split_count = split_coeffs.shape[0]
    half_width = split_coeffs.shape[3]
    half_orders = half_width // 2
    half_index = lax.axis_index("row") % 2
    pair_start = (
        lax.axis_index("row") // 2 * lax.axis_size("col") + lax.axis_index("col")
    ) * split_count
    own_material = lax.dynamic_slice_in_dim(split_material, pair_start, split_count, 0)
    own_order = half_index * half_orders + jnp.arange(half_width, dtype=jnp.int32) % half_orders
    keep_half = (degree_index[:, None] >= own_order[None, :]).astype(jnp.float32)
    own_legendre = lax.dynamic_slice_in_dim(legendre, half_index * half_orders, half_orders, 0)
    own_fourier = lax.dynamic_slice_in_dim(
        fourier.reshape(2, degrees, nlon), half_index * half_orders, half_orders, 1
    ).reshape(half_width, nlon)
    split_prepared = prepare(split_coeffs, keep_half[None])
    split_legendre = legendre_synth(
        split_prepared.reshape(split_count * 4, degrees, half_width), own_legendre
    )
    partial_surface = fourier_synth(split_legendre, own_fourier)
    split_surface = partial_surface + from_partner(
        partial_surface.astype(jnp.bfloat16), "row", 0
    ).astype(partial_surface.dtype)
    _, split_grid = traction(split_surface.reshape(split_count, 4, nlat, nlon), own_material)
    near_grid = jnp.stack([radius, traction_grid], axis=1).astype(jnp.bfloat16)
    point_count = 4
    target_normal = normals[:, nlat // 4 :: nlat // 2, :: nlon // 2].reshape(3, point_count)
    devices = lax.axis_size("row") * lax.axis_size("col")
    all_points = lax.all_to_all(
        jnp.broadcast_to(own_points.reshape(1, -1), (devices, drop_count * point_count)),
        ("row", "col"),
        split_axis=0,
        concat_axis=0,
        tiled=True,
    ).reshape(devices * drop_count, point_count)
    total_drops = all_points.shape[0]
    readers = reader_dev.shape[1]
    target = (reader_dev * drop_count + reader_slot).reshape(-1)
    pick = (target[:, None] == jnp.arange(total_drops, dtype=jnp.int32)[None, :]).astype(
        jnp.float32
    )
    target_radius = jnp.dot(pick, all_points.astype(jnp.float32), precision=HIGH)
    target_point = separation.reshape(3, drop_count * readers)[:, :, None] + (
        target_radius[None] * target_normal[:, None, :]
    )
    target_point = jnp.transpose(
        target_point.reshape(3, drop_count, readers * point_count), (1, 2, 0)
    )
    target_square = jnp.sum(target_point * target_point, axis=2) + SOFTENING
    entry_table = jnp.concatenate(
        [
            jnp.transpose(separation, (1, 2, 0)),
            target_radius.reshape(drop_count, readers, point_count),
            target_square.reshape(drop_count, readers, point_count),
        ],
        axis=2,
    ).reshape(-1)
    cell_table = cell_tables(nlat, nlon, point_count)
    partial = near_field(entry_table, near_grid, cell_table, readers, point_count)
    partial, traction_grid, split_grid = lax.optimization_barrier(
        (partial, traction_grid, split_grid)
    )
    sums = jnp.sum(partial, axis=3)
    contribution = (
        sums[:, :3] + jnp.transpose(target_point, (0, 2, 1)) * sums[:, 3:]
    ) / (8.0 * math.pi)
    contribution = jnp.transpose(
        contribution.reshape(drop_count, 3, readers, point_count), (0, 2, 1, 3)
    ).reshape(drop_count * readers, 3 * point_count)
    destination = reader_dev.reshape(-1)
    capacity = 2
    onehot = (destination[:, None] == jnp.arange(devices, dtype=jnp.int32)[None, :]).astype(
        jnp.int32
    )
    rank = jnp.sum((jnp.cumsum(onehot, axis=0) - onehot) * onehot, axis=1)
    position = destination * capacity + rank
    place = (position[:, None] == jnp.arange(devices * capacity, dtype=jnp.int32)[None, :]).astype(
        jnp.float32
    )
    record = jnp.concatenate(
        [contribution, reader_slot.reshape(-1, 1).astype(jnp.float32)], axis=1
    )
    outgoing = jnp.dot(jnp.transpose(place), record, precision=HIGH)
    incoming = lax.all_to_all(
        outgoing.reshape(devices, capacity, record.shape[1]),
        ("row", "col"),
        split_axis=0,
        concat_axis=0,
        tiled=True,
    ).reshape(devices * capacity, record.shape[1])
    slot_pick = (
        incoming[:, -1:] == jnp.arange(drop_count, dtype=jnp.float32)[None, :]
    ).astype(jnp.float32)
    mine = jnp.dot(jnp.transpose(slot_pick), incoming[:, :-1], precision=HIGH)
    near_velocity = jnp.transpose(mine.reshape(drop_count, 3, point_count), (1, 0, 2))
    traction_coeffs = (
        analysis_legendre(analysis_fourier(traction_grid, fourier, quad_weight), legendre)
        * keep_mask
    )
    coef_grid = analysis_fourier(split_grid, fourier, quad_weight)
    own_grid = lax.dynamic_slice_in_dim(coef_grid, half_index * half_orders, half_orders, 3)
    split_traction = analysis_legendre(own_grid, own_legendre) * keep_half[None]
    return (traction_coeffs, split_traction, near_velocity.reshape(3, drop_count * point_count))


def point_table(degrees):
    legendre, fourier, _, _ = (np.asarray(t) for t in spectral_tables_np(degrees))
    lat = np.arange(degrees // 4, degrees, degrees // 2)
    lon = np.arange(0, 2 * degrees, degrees)
    orders = np.arange(2 * degrees) % degrees
    table = np.zeros((degrees, 2 * degrees, lat.size * lon.size))
    for i, j in enumerate(lat):
        for k, col in enumerate(lon):
            table[:, :, i * lon.size + k] = (
                legendre[orders, j, :].T.astype(np.float64) * fourier[:, col][None, :]
            )
    return jnp.asarray(table.reshape(degrees * 2 * degrees, -1), dtype=jnp.float32)


def cell_tables(nlat, nlon, point_count):
    theta = (np.arange(nlat) + 0.5) * (math.pi / nlat)
    longitude = np.arange(nlon) * (2.0 * math.pi / nlon)
    quad_weight = (np.sin(theta) * (math.pi / nlat) * (2.0 * math.pi / nlon)).astype(np.float32)
    normals = np.stack(
        [
            np.sin(theta)[:, None] * np.cos(longitude)[None, :],
            np.sin(theta)[:, None] * np.sin(longitude)[None, :],
            np.cos(theta)[:, None] * np.ones((1, nlon)),
        ],
        axis=0,
    ).astype(np.float32)
    points = normals[:, nlat // 4 :: nlat // 2, :: nlon // 2].reshape(3, point_count)
    facing = np.einsum("dp,djk->pjk", points.astype(np.float64), normals.astype(np.float64))
    weight = np.broadcast_to(quad_weight[None, :, None], (1, nlat, nlon))
    table = np.concatenate([normals, facing.astype(np.float32), weight], axis=0)
    return jnp.asarray(table, dtype=jnp.float32)


def near_kernel(points, t_ref, g_ref, c_ref, o_ref, s_ref):
    drop = pl.program_id(0)
    entries = o_ref.shape[2] // points
    width = 3 + 2 * points
    chunks = g_ref.shape[2] // 8
    r = g_ref[0, 0].astype(jnp.float32)
    s_ref[0] = r
    s_ref[1] = r * r
    s_ref[2] = r + r
    s_ref[3] = g_ref[0, 1].astype(jnp.float32) * r * r * c_ref[3 + points]

    def body(e, carry):
        base = (drop * entries + e) * width
        sx = t_ref[base]
        sy = t_ref[base + 1]
        sz = t_ref[base + 2]
        lift = [t_ref[base + 3 + k] for k in range(points)]
        tt = [t_ref[base + 3 + points + k] for k in range(points)]
        acc = [[jnp.zeros((8, 128), jnp.float32) for _ in range(4)] for _ in range(points)]
        for c in range(chunks):
            rows = pl.ds(c * 8, 8)
            nx = c_ref[0, rows, :]
            ny = c_ref[1, rows, :]
            nz = c_ref[2, rows, :]
            rr = s_ref[0, rows, :]
            r2 = s_ref[1, rows, :]
            twice = s_ref[2, rows, :]
            load = s_ref[3, rows, :]
            shared = sx * nx + sy * ny + sz * nz
            for k in range(points):
                along = shared + lift[k] * c_ref[3 + k, rows, :]
                soft = (tt[k] + r2) - twice * along
                inv = lax.rsqrt(soft)
                w = load * (inv * inv * inv)
                dn = along - rr
                h = w * ((soft + SOFTENING) - dn * rr)
                hx, hy, hz, sq = acc[k]
                acc[k] = [hx + h * nx, hy + h * ny, hz + h * nz, sq + w * dn]
        for k in range(points):
            row = pl.ds(e * points + k, 1)
            for comp in range(4):
                o_ref[0, comp, row, :] = jnp.sum(acc[k][comp], axis=0, keepdims=True)
        return carry

    lax.fori_loop(0, entries, body, 0)


def near_field(entry_table, near_grid, cell_table, readers, points):
    drops, fields, nlat, nlon = near_grid.shape
    targets = readers * points
    cells = drops * targets * nlat * nlon
    return pl.pallas_call(
        functools.partial(near_kernel, points),
        grid=(drops,),
        in_specs=[
            pl.BlockSpec(memory_space=pltpu.SMEM),
            pl.BlockSpec((1, fields, nlat, nlon), lambda s: (s, 0, 0, 0)),
            pl.BlockSpec(cell_table.shape, lambda s: (0, 0, 0)),
        ],
        out_specs=pl.BlockSpec((1, 4, targets, nlon), lambda s: (s, 0, 0, 0)),
        out_shape=jax.ShapeDtypeStruct((drops, 4, targets, nlon), jnp.float32),
        scratch_shapes=[pltpu.VMEM((4, nlat, nlon), jnp.float32)],
        cost_estimate=pl.CostEstimate(
            flops=24 * cells, transcendentals=cells, bytes_accessed=2 * drops * fields * nlat * nlon
        ),
    )(entry_table, near_grid, cell_table)


def solution(mesh):
    in_specs = (
        P(("row", "col"), None, None, None),
        P(("row", "col")),
        P(("row", "col"), None),
        P(("row", "col"), None, None, None),
        P(),
        P(None, ("row", "col"), None),
        P(("row", "col"), None),
        P(("row", "col"), None),
    )
    out_specs = (
        P(("row", "col"), None, None),
        P(("row", "col"), None, None),
        P(None, ("row", "col")),
    )
    return jax.shard_map(
        per_device, mesh=mesh, in_specs=in_specs, out_specs=out_specs, check_vma=False
    )
```

```python
import functools
import math

import jax
import jax.numpy as jnp
import numpy as np
from jax import lax
from jax.experimental import pallas as pl
from jax.experimental.pallas import tpu as pltpu
from jax.sharding import PartitionSpec as P

HIGH = lax.Precision.HIGHEST
SPECTRAL = lax.Precision.DEFAULT
SOFTENING = 0.04


def from_partner(block, axis, stride):
    count = lax.axis_size(axis)
    route = []
    for low in range(count):
        high = low | 1 << stride
        if high != low and high < count:
            route += [(low, high), (high, low)]
    return lax.ppermute(block, axis, route)


def spectral_tables(degrees):
    nlon = 2 * degrees
    theta_lat = (np.arange(degrees) + 0.5) * (math.pi / degrees)
    cosine = np.cos(theta_lat)
    sine_theta = np.sin(theta_lat)
    legendre = np.zeros((degrees, degrees, degrees))
    for order in range(degrees):
        log_total = 0.0
        for step_index in range(1, order + 1):
            log_total = log_total + math.log((2.0 * step_index + 1.0) / (2.0 * step_index))
        diag_value = np.exp(0.5 * log_total + order * np.log(sine_theta)) / math.sqrt(4.0 * math.pi)
        legendre[order, :, order] = diag_value
        prev_two = diag_value
        if order + 1 < degrees:
            prev_one = math.sqrt(2.0 * order + 3.0) * cosine * diag_value
            legendre[order, :, order + 1] = prev_one
            for level in range(order + 2, degrees):
                alpha_term = math.sqrt(
                    (4.0 * level * level - 1.0) / (level * level - order * order)
                )
                beta_term = math.sqrt(
                    ((level - 1.0) ** 2 - order * order) / (4.0 * (level - 1.0) ** 2 - 1.0)
                )
                current = alpha_term * (cosine * prev_one - beta_term * prev_two)
                legendre[order, :, level] = current
                prev_two = prev_one
                prev_one = current
    order_index = np.arange(degrees)
    lon_index = np.arange(nlon)
    phase_angle = order_index[:, None] * lon_index[None, :] % nlon * (2.0 * math.pi / nlon)
    fourier = np.concatenate([np.cos(phase_angle), np.sin(phase_angle)], axis=0)
    quad_weight = sine_theta * (math.pi / degrees) * (2.0 * math.pi / nlon)
    longitude = lon_index * (2.0 * math.pi / nlon)
    normals = np.stack(
        [
            sine_theta[:, None] * np.cos(longitude)[None, :],
            sine_theta[:, None] * np.sin(longitude)[None, :],
            cosine[:, None] * np.ones((1, nlon)),
        ],
        axis=0,
    )
    return (
        jnp.asarray(legendre, dtype=jnp.float32),
        jnp.asarray(fourier, dtype=jnp.float32),
        jnp.asarray(quad_weight, dtype=jnp.float32),
        jnp.asarray(normals, dtype=jnp.float32),
    )


def spectral_tables_np(degrees):
    nlon = 2 * degrees
    theta_lat = (np.arange(degrees) + 0.5) * (math.pi / degrees)
    cosine = np.cos(theta_lat)
    sine_theta = np.sin(theta_lat)
    legendre = np.zeros((degrees, degrees, degrees))
    for order in range(degrees):
        log_total = 0.0
        for step_index in range(1, order + 1):
            log_total = log_total + math.log((2.0 * step_index + 1.0) / (2.0 * step_index))
        diag_value = np.exp(0.5 * log_total + order * np.log(sine_theta)) / math.sqrt(4.0 * math.pi)
        legendre[order, :, order] = diag_value
        prev_two = diag_value
        if order + 1 < degrees:
            prev_one = math.sqrt(2.0 * order + 3.0) * cosine * diag_value
            legendre[order, :, order + 1] = prev_one
            for level in range(order + 2, degrees):
                alpha_term = math.sqrt(
                    (4.0 * level * level - 1.0) / (level * level - order * order)
                )
                beta_term = math.sqrt(
                    ((level - 1.0) ** 2 - order * order) / (4.0 * (level - 1.0) ** 2 - 1.0)
                )
                current = alpha_term * (cosine * prev_one - beta_term * prev_two)
                legendre[order, :, level] = current
                prev_two = prev_one
                prev_one = current
    order_index = np.arange(degrees)
    lon_index = np.arange(nlon)
    phase_angle = order_index[:, None] * lon_index[None, :] % nlon * (2.0 * math.pi / nlon)
    fourier = np.concatenate([np.cos(phase_angle), np.sin(phase_angle)], axis=0)
    quad_weight = sine_theta * (math.pi / degrees) * (2.0 * math.pi / nlon)
    longitude = lon_index * (2.0 * math.pi / nlon)
    normals = np.stack(
        [
            sine_theta[:, None] * np.cos(longitude)[None, :],
            sine_theta[:, None] * np.sin(longitude)[None, :],
            cosine[:, None] * np.ones((1, nlon)),
        ],
        axis=0,
    )
    return (
        legendre.astype(np.float32),
        fourier.astype(np.float32),
        quad_weight.astype(np.float32),
        normals.astype(np.float32),
    )


def legendre_synth(coeff, legendre):
    batch_size, degrees, _ = coeff.shape
    orders = legendre.shape[0]
    parted = coeff.reshape(batch_size, degrees, 2, orders)
    return jnp.einsum("mjl,nlcm->njcm", legendre, parted, precision=SPECTRAL)


def fourier_synth(partial_legendre, fourier_rows):
    batch_size, nlat, two, orders = partial_legendre.shape
    return jnp.einsum(
        "njw,wk->njk",
        partial_legendre.reshape(batch_size, nlat, two * orders),
        fourier_rows,
        precision=SPECTRAL,
    )


def analysis_fourier(traction_grid, fourier, quad_weight):
    batch_size, nlat, _ = traction_grid.shape
    projected = (
        jnp.einsum("bjk,wk->bjw", traction_grid, fourier, precision=SPECTRAL)
        * quad_weight[None, :, None]
    )
    return projected.reshape(batch_size, nlat, 2, fourier.shape[0] // 2)


def analysis_legendre(coef_grid, legendre):
    batch_size = coef_grid.shape[0]
    result = jnp.einsum("mjl,bjcm->blcm", legendre, coef_grid, precision=SPECTRAL)
    return result.reshape(batch_size, legendre.shape[2], 2 * legendre.shape[0])


def prepare(coeffs, keep_mask):
    degrees = coeffs.shape[2]
    degree_value = jnp.arange(degrees, dtype=jnp.float32)
    shape_part = coeffs[:, 0] * keep_mask
    curvature = (
        shape_part * (degree_value * (degree_value + 1.0) / (degrees * degrees))[None, :, None]
    )
    electric = 3.0 * coeffs[:, 1] * keep_mask
    viscous = 3.0 * coeffs[:, 2] * keep_mask * ((degree_value + 2.0) / degrees)[None, :, None]
    return jnp.stack([shape_part, curvature, electric, viscous], axis=1)


def traction(surface, material):
    radius = jnp.exp(surface[:, 0])
    traction_grid = (
        material[:, 0, None, None] * surface[:, 1]
        + 0.5 * surface[:, 2] * surface[:, 2]
        + 2.0 * material[:, 1, None, None] * surface[:, 3]
    )
    return (radius, traction_grid)


def per_device(
    coeffs, degree, material, split_coeffs, split_material, separation, reader_dev, reader_slot
):
    drop_count, _, degrees, coef_width = coeffs.shape
    legendre, fourier, quad_weight, normals = spectral_tables(degrees)
    nlat = legendre.shape[1]
    nlon = fourier.shape[1]
    degree_index = jnp.arange(degrees, dtype=jnp.int32)
    order_full = jnp.arange(coef_width, dtype=jnp.int32) % degrees
    order_mask = (degree_index[:, None] >= order_full[None, :]).astype(jnp.float32)
    keep_mask = order_mask[None] * (degree_index[None, :, None] <= degree[:, None, None]).astype(
        jnp.float32
    )
    prepared = prepare(coeffs, keep_mask)
    point_weight = point_table(degrees)
    point_surface = jnp.dot(
        prepared[:, 0].reshape(drop_count, degrees * coef_width),
        point_weight,
        precision=lax.Precision.HIGH,
    )
    own_points = jnp.exp(point_surface).astype(jnp.bfloat16)
    partial_legendre = legendre_synth(
        prepared.reshape(drop_count * 4, degrees, coef_width), legendre
    )
    surface = fourier_synth(partial_legendre, fourier).reshape(drop_count, 4, nlat, nlon)
    radius, traction_grid = traction(surface, material)
    split_count = split_coeffs.shape[0]
    half_width = split_coeffs.shape[3]
    half_orders = half_width // 2
    half_index = lax.axis_index("row") % 2
    pair_start = (
        lax.axis_index("row") // 2 * lax.axis_size("col") + lax.axis_index("col")
    ) * split_count
    own_material = lax.dynamic_slice_in_dim(split_material, pair_start, split_count, 0)
    own_order = half_index * half_orders + jnp.arange(half_width, dtype=jnp.int32) % half_orders
    keep_half = (degree_index[:, None] >= own_order[None, :]).astype(jnp.float32)
    own_legendre = lax.dynamic_slice_in_dim(legendre, half_index * half_orders, half_orders, 0)
    own_fourier = lax.dynamic_slice_in_dim(
        fourier.reshape(2, degrees, nlon), half_index * half_orders, half_orders, 1
    ).reshape(half_width, nlon)
    split_prepared = prepare(split_coeffs, keep_half[None])
    split_legendre = legendre_synth(
        split_prepared.reshape(split_count * 4, degrees, half_width), own_legendre
    )
    partial_surface = fourier_synth(split_legendre, own_fourier)
    split_surface = partial_surface + from_partner(
        partial_surface.astype(jnp.bfloat16), "row", 0
    ).astype(partial_surface.dtype)
    _, split_grid = traction(split_surface.reshape(split_count, 4, nlat, nlon), own_material)
    near_grid = jnp.stack([radius, traction_grid], axis=1).astype(jnp.bfloat16)
    point_count = 4
    target_normal = normals[:, nlat // 4 :: nlat // 2, :: nlon // 2].reshape(3, point_count)
    devices = lax.axis_size("row") * lax.axis_size("col")
    all_points = lax.all_to_all(
        jnp.broadcast_to(own_points.reshape(1, -1), (devices, drop_count * point_count)),
        ("row", "col"),
        split_axis=0,
        concat_axis=0,
        tiled=True,
    ).reshape(devices * drop_count, point_count)
    total_drops = all_points.shape[0]
    readers = reader_dev.shape[1]
    target = (reader_dev * drop_count + reader_slot).reshape(-1)
    pick = (target[:, None] == jnp.arange(total_drops, dtype=jnp.int32)[None, :]).astype(
        jnp.float32
    )
    target_radius = jnp.dot(pick, all_points.astype(jnp.float32), precision=HIGH)
    target_point = separation.reshape(3, drop_count * readers)[:, :, None] + (
        target_radius[None] * target_normal[:, None, :]
    )
    target_point = jnp.transpose(
        target_point.reshape(3, drop_count, readers * point_count), (1, 2, 0)
    )
    target_square = jnp.sum(target_point * target_point, axis=2) + SOFTENING
    entry_table = jnp.concatenate(
        [
            jnp.transpose(separation, (1, 2, 0)),
            target_radius.reshape(drop_count, readers, point_count),
            target_square.reshape(drop_count, readers, point_count),
        ],
        axis=2,
    ).reshape(-1)
    cell_table = cell_tables(nlat, nlon, point_count)
    partial = near_field(entry_table, near_grid, cell_table, readers, point_count)
    partial, traction_grid = lax.optimization_barrier((partial, traction_grid))
    sums = partial
    contribution = (
        sums[:, :3] + jnp.transpose(target_point, (0, 2, 1)) * sums[:, 3:]
    ) / (8.0 * math.pi)
    contribution = jnp.transpose(
        contribution.reshape(drop_count, 3, readers, point_count), (0, 2, 1, 3)
    ).reshape(drop_count * readers, 3 * point_count)
    destination = reader_dev.reshape(-1)
    capacity = 2
    onehot = (destination[:, None] == jnp.arange(devices, dtype=jnp.int32)[None, :]).astype(
        jnp.int32
    )
    rank = jnp.sum((jnp.cumsum(onehot, axis=0) - onehot) * onehot, axis=1)
    position = destination * capacity + rank
    place = (position[:, None] == jnp.arange(devices * capacity, dtype=jnp.int32)[None, :]).astype(
        jnp.float32
    )
    record = jnp.concatenate(
        [contribution, reader_slot.reshape(-1, 1).astype(jnp.float32)], axis=1
    )
    outgoing = jnp.dot(jnp.transpose(place), record, precision=HIGH)
    incoming = lax.all_to_all(
        outgoing.reshape(devices, capacity, record.shape[1]),
        ("row", "col"),
        split_axis=0,
        concat_axis=0,
        tiled=True,
    ).reshape(devices * capacity, record.shape[1])
    slot_pick = (
        incoming[:, -1:] == jnp.arange(drop_count, dtype=jnp.float32)[None, :]
    ).astype(jnp.float32)
    mine = jnp.dot(jnp.transpose(slot_pick), incoming[:, :-1], precision=HIGH)
    near_velocity = jnp.transpose(mine.reshape(drop_count, 3, point_count), (1, 0, 2))
    traction_coeffs = (
        analysis_legendre(analysis_fourier(traction_grid, fourier, quad_weight), legendre)
        * keep_mask
    )
    coef_grid = analysis_fourier(split_grid, fourier, quad_weight)
    own_grid = lax.dynamic_slice_in_dim(coef_grid, half_index * half_orders, half_orders, 3)
    split_traction = analysis_legendre(own_grid, own_legendre) * keep_half[None]
    return (traction_coeffs, split_traction, near_velocity.reshape(3, drop_count * point_count))


def point_table(degrees):
    legendre, fourier, _, _ = (np.asarray(t) for t in spectral_tables_np(degrees))
    lat = np.arange(degrees // 4, degrees, degrees // 2)
    lon = np.arange(0, 2 * degrees, degrees)
    orders = np.arange(2 * degrees) % degrees
    table = np.zeros((degrees, 2 * degrees, lat.size * lon.size))
    for i, j in enumerate(lat):
        for k, col in enumerate(lon):
            table[:, :, i * lon.size + k] = (
                legendre[orders, j, :].T.astype(np.float64) * fourier[:, col][None, :]
            )
    return jnp.asarray(table.reshape(degrees * 2 * degrees, -1), dtype=jnp.float32)


def cell_tables(nlat, nlon, point_count):
    theta = (np.arange(nlat) + 0.5) * (math.pi / nlat)
    longitude = np.arange(nlon) * (2.0 * math.pi / nlon)
    quad_weight = (np.sin(theta) * (math.pi / nlat) * (2.0 * math.pi / nlon)).astype(np.float32)
    normals = np.stack(
        [
            np.sin(theta)[:, None] * np.cos(longitude)[None, :],
            np.sin(theta)[:, None] * np.sin(longitude)[None, :],
            np.cos(theta)[:, None] * np.ones((1, nlon)),
        ],
        axis=0,
    ).astype(np.float32)
    points = normals[:, nlat // 4 :: nlat // 2, :: nlon // 2].reshape(3, point_count)
    facing = np.einsum("dp,djk->pjk", points.astype(np.float64), normals.astype(np.float64))
    weight = np.broadcast_to(quad_weight[None, :, None], (1, nlat, nlon))
    table = np.concatenate([normals, facing.astype(np.float32), weight], axis=0)
    return jnp.asarray(table, dtype=jnp.float32)


def near_kernel(points, t_ref, g_ref, c_ref, f_ref, s_ref, o_ref):
    drop = pl.program_id(0)
    entries = o_ref.shape[2] // points
    width = 3 + 2 * points
    chunks = g_ref.shape[2] // 8
    r = g_ref[0, 0].astype(jnp.float32)
    s_ref[0] = r
    s_ref[1] = r * r
    s_ref[2] = r + r
    s_ref[3] = g_ref[0, 1].astype(jnp.float32) * r * r * c_ref[3 + points]

    def body(e, carry):
        base = (drop * entries + e) * width
        sx = t_ref[base]
        sy = t_ref[base + 1]
        sz = t_ref[base + 2]
        lift = [t_ref[base + 3 + k] for k in range(points)]
        tt = [t_ref[base + 3 + points + k] for k in range(points)]
        acc = [[jnp.zeros((8, 128), jnp.float32) for _ in range(4)] for _ in range(points)]
        for c in range(chunks):
            rows = pl.ds(c * 8, 8)
            nx = c_ref[0, rows, :]
            ny = c_ref[1, rows, :]
            nz = c_ref[2, rows, :]
            rr = s_ref[0, rows, :]
            r2 = s_ref[1, rows, :]
            twice = s_ref[2, rows, :]
            load = s_ref[3, rows, :]
            shared = sx * nx + sy * ny + sz * nz
            for k in range(points):
                along = shared + lift[k] * c_ref[3 + k, rows, :]
                soft = (tt[k] + r2) - twice * along
                inv = lax.rsqrt(soft)
                w = load * (inv * inv * inv)
                dn = along - rr
                h = w * ((soft + SOFTENING) - dn * rr)
                hx, hy, hz, sq = acc[k]
                acc[k] = [hx + h * nx, hy + h * ny, hz + h * nz, sq + w * dn]
        for k in range(points):
            row = pl.ds(e * points + k, 1)
            for comp in range(4):
                o_ref[0, comp, row, :] = jnp.sum(acc[k][comp], axis=0, keepdims=True)
        return carry

    lax.fori_loop(0, entries, body, 0)
    rows = o_ref.shape[1] * o_ref.shape[2]
    f_ref[0] = jnp.sum(o_ref[0].reshape(rows, o_ref.shape[3]), axis=1, keepdims=True)


def near_field(entry_table, near_grid, cell_table, readers, points):
    drops, fields, nlat, nlon = near_grid.shape
    targets = readers * points
    cells = drops * targets * nlat * nlon
    return pl.pallas_call(
        functools.partial(near_kernel, points),
        grid=(drops,),
        in_specs=[
            pl.BlockSpec(memory_space=pltpu.SMEM),
            pl.BlockSpec((1, fields, nlat, nlon), lambda s: (s, 0, 0, 0)),
            pl.BlockSpec(cell_table.shape, lambda s: (0, 0, 0)),
        ],
        out_specs=pl.BlockSpec((1, 4 * targets, 1), lambda s: (s, 0, 0)),
        out_shape=jax.ShapeDtypeStruct((drops, 4 * targets, 1), jnp.float32),
        scratch_shapes=[
            pltpu.VMEM((4, nlat, nlon), jnp.float32),
            pltpu.VMEM((1, 4, targets, nlon), jnp.float32),
        ],
        cost_estimate=pl.CostEstimate(
            flops=24 * cells, transcendentals=cells, bytes_accessed=2 * drops * fields * nlat * nlon
        ),
    )(entry_table, near_grid, cell_table).reshape(drops, 4, targets)


def solution(mesh):
    in_specs = (
        P(("row", "col"), None, None, None),
        P(("row", "col")),
        P(("row", "col"), None),
        P(("row", "col"), None, None, None),
        P(),
        P(None, ("row", "col"), None),
        P(("row", "col"), None),
        P(("row", "col"), None),
    )
    out_specs = (
        P(("row", "col"), None, None),
        P(("row", "col"), None, None),
        P(None, ("row", "col")),
    )
    return jax.shard_map(
        per_device, mesh=mesh, in_specs=in_specs, out_specs=out_specs, check_vma=False
    )
```

```python
import functools
import math

import jax
import jax.numpy as jnp
import numpy as np
from jax import lax
from jax.experimental import pallas as pl
from jax.experimental.pallas import tpu as pltpu
from jax.sharding import PartitionSpec as P

HIGH = lax.Precision.HIGHEST
SPECTRAL = lax.Precision.DEFAULT
SOFTENING = 0.04


def from_partner(block, axis, stride):
    count = lax.axis_size(axis)
    route = []
    for low in range(count):
        high = low | 1 << stride
        if high != low and high < count:
            route += [(low, high), (high, low)]
    return lax.ppermute(block, axis, route)


def spectral_tables(degrees):
    nlon = 2 * degrees
    theta_lat = (np.arange(degrees) + 0.5) * (math.pi / degrees)
    cosine = np.cos(theta_lat)
    sine_theta = np.sin(theta_lat)
    legendre = np.zeros((degrees, degrees, degrees))
    for order in range(degrees):
        log_total = 0.0
        for step_index in range(1, order + 1):
            log_total = log_total + math.log((2.0 * step_index + 1.0) / (2.0 * step_index))
        diag_value = np.exp(0.5 * log_total + order * np.log(sine_theta)) / math.sqrt(4.0 * math.pi)
        legendre[order, :, order] = diag_value
        prev_two = diag_value
        if order + 1 < degrees:
            prev_one = math.sqrt(2.0 * order + 3.0) * cosine * diag_value
            legendre[order, :, order + 1] = prev_one
            for level in range(order + 2, degrees):
                alpha_term = math.sqrt(
                    (4.0 * level * level - 1.0) / (level * level - order * order)
                )
                beta_term = math.sqrt(
                    ((level - 1.0) ** 2 - order * order) / (4.0 * (level - 1.0) ** 2 - 1.0)
                )
                current = alpha_term * (cosine * prev_one - beta_term * prev_two)
                legendre[order, :, level] = current
                prev_two = prev_one
                prev_one = current
    order_index = np.arange(degrees)
    lon_index = np.arange(nlon)
    phase_angle = order_index[:, None] * lon_index[None, :] % nlon * (2.0 * math.pi / nlon)
    fourier = np.concatenate([np.cos(phase_angle), np.sin(phase_angle)], axis=0)
    quad_weight = sine_theta * (math.pi / degrees) * (2.0 * math.pi / nlon)
    longitude = lon_index * (2.0 * math.pi / nlon)
    normals = np.stack(
        [
            sine_theta[:, None] * np.cos(longitude)[None, :],
            sine_theta[:, None] * np.sin(longitude)[None, :],
            cosine[:, None] * np.ones((1, nlon)),
        ],
        axis=0,
    )
    return (
        jnp.asarray(legendre, dtype=jnp.float32),
        jnp.asarray(fourier, dtype=jnp.float32),
        jnp.asarray(quad_weight, dtype=jnp.float32),
        jnp.asarray(normals, dtype=jnp.float32),
    )


def spectral_tables_np(degrees):
    nlon = 2 * degrees
    theta_lat = (np.arange(degrees) + 0.5) * (math.pi / degrees)
    cosine = np.cos(theta_lat)
    sine_theta = np.sin(theta_lat)
    legendre = np.zeros((degrees, degrees, degrees))
    for order in range(degrees):
        log_total = 0.0
        for step_index in range(1, order + 1):
            log_total = log_total + math.log((2.0 * step_index + 1.0) / (2.0 * step_index))
        diag_value = np.exp(0.5 * log_total + order * np.log(sine_theta)) / math.sqrt(4.0 * math.pi)
        legendre[order, :, order] = diag_value
        prev_two = diag_value
        if order + 1 < degrees:
            prev_one = math.sqrt(2.0 * order + 3.0) * cosine * diag_value
            legendre[order, :, order + 1] = prev_one
            for level in range(order + 2, degrees):
                alpha_term = math.sqrt(
                    (4.0 * level * level - 1.0) / (level * level - order * order)
                )
                beta_term = math.sqrt(
                    ((level - 1.0) ** 2 - order * order) / (4.0 * (level - 1.0) ** 2 - 1.0)
                )
                current = alpha_term * (cosine * prev_one - beta_term * prev_two)
                legendre[order, :, level] = current
                prev_two = prev_one
                prev_one = current
    order_index = np.arange(degrees)
    lon_index = np.arange(nlon)
    phase_angle = order_index[:, None] * lon_index[None, :] % nlon * (2.0 * math.pi / nlon)
    fourier = np.concatenate([np.cos(phase_angle), np.sin(phase_angle)], axis=0)
    quad_weight = sine_theta * (math.pi / degrees) * (2.0 * math.pi / nlon)
    longitude = lon_index * (2.0 * math.pi / nlon)
    normals = np.stack(
        [
            sine_theta[:, None] * np.cos(longitude)[None, :],
            sine_theta[:, None] * np.sin(longitude)[None, :],
            cosine[:, None] * np.ones((1, nlon)),
        ],
        axis=0,
    )
    return (
        legendre.astype(np.float32),
        fourier.astype(np.float32),
        quad_weight.astype(np.float32),
        normals.astype(np.float32),
    )


def legendre_synth(coeff, legendre):
    batch_size, degrees, _ = coeff.shape
    orders = legendre.shape[0]
    parted = coeff.reshape(batch_size, degrees, 2, orders)
    return jnp.einsum("mjl,nlcm->njcm", legendre, parted, precision=SPECTRAL)


def fourier_synth(partial_legendre, fourier_rows):
    batch_size, nlat, two, orders = partial_legendre.shape
    return jnp.einsum(
        "njw,wk->njk",
        partial_legendre.reshape(batch_size, nlat, two * orders),
        fourier_rows,
        precision=SPECTRAL,
    )


def analysis_fourier(traction_grid, fourier, quad_weight):
    batch_size, nlat, _ = traction_grid.shape
    projected = (
        jnp.einsum("bjk,wk->bjw", traction_grid, fourier, precision=SPECTRAL)
        * quad_weight[None, :, None]
    )
    return projected.reshape(batch_size, nlat, 2, fourier.shape[0] // 2)


def analysis_legendre(coef_grid, legendre):
    batch_size = coef_grid.shape[0]
    result = jnp.einsum("mjl,bjcm->blcm", legendre, coef_grid, precision=SPECTRAL)
    return result.reshape(batch_size, legendre.shape[2], 2 * legendre.shape[0])


def prepare(coeffs, keep_mask):
    degrees = coeffs.shape[2]
    degree_value = jnp.arange(degrees, dtype=jnp.float32)
    shape_part = coeffs[:, 0] * keep_mask
    curvature = (
        shape_part * (degree_value * (degree_value + 1.0) / (degrees * degrees))[None, :, None]
    )
    electric = 3.0 * coeffs[:, 1] * keep_mask
    viscous = 3.0 * coeffs[:, 2] * keep_mask * ((degree_value + 2.0) / degrees)[None, :, None]
    return jnp.stack([shape_part, curvature, electric, viscous], axis=1)


def traction(surface, material):
    radius = jnp.exp(surface[:, 0])
    traction_grid = (
        material[:, 0, None, None] * surface[:, 1]
        + 0.5 * surface[:, 2] * surface[:, 2]
        + 2.0 * material[:, 1, None, None] * surface[:, 3]
    )
    return (radius, traction_grid)


def per_device(
    coeffs, degree, material, split_coeffs, split_material, separation, reader_dev, reader_slot
):
    drop_count, _, degrees, coef_width = coeffs.shape
    legendre, fourier, quad_weight, normals = spectral_tables(degrees)
    nlat = legendre.shape[1]
    nlon = fourier.shape[1]
    degree_index = jnp.arange(degrees, dtype=jnp.int32)
    order_full = jnp.arange(coef_width, dtype=jnp.int32) % degrees
    order_mask = (degree_index[:, None] >= order_full[None, :]).astype(jnp.float32)
    keep_mask = order_mask[None] * (degree_index[None, :, None] <= degree[:, None, None]).astype(
        jnp.float32
    )
    prepared = prepare(coeffs, keep_mask)
    point_weight = point_table(degrees)
    point_surface = jnp.dot(
        (coeffs[:, 0] * keep_mask).reshape(drop_count, degrees * coef_width),
        point_weight,
        precision=lax.Precision.HIGH,
    )
    own_points = jnp.exp(point_surface).astype(jnp.bfloat16)
    partial_legendre = legendre_synth(
        prepared.reshape(drop_count * 4, degrees, coef_width), legendre
    )
    surface = fourier_synth(partial_legendre, fourier).reshape(drop_count, 4, nlat, nlon)
    radius, traction_grid = traction(surface, material)
    split_count = split_coeffs.shape[0]
    half_width = split_coeffs.shape[3]
    half_orders = half_width // 2
    half_index = lax.axis_index("row") % 2
    pair_start = (
        lax.axis_index("row") // 2 * lax.axis_size("col") + lax.axis_index("col")
    ) * split_count
    own_material = lax.dynamic_slice_in_dim(split_material, pair_start, split_count, 0)
    own_order = half_index * half_orders + jnp.arange(half_width, dtype=jnp.int32) % half_orders
    keep_half = (degree_index[:, None] >= own_order[None, :]).astype(jnp.float32)
    own_legendre = lax.dynamic_slice_in_dim(legendre, half_index * half_orders, half_orders, 0)
    own_fourier = lax.dynamic_slice_in_dim(
        fourier.reshape(2, degrees, nlon), half_index * half_orders, half_orders, 1
    ).reshape(half_width, nlon)
    split_prepared = prepare(split_coeffs, keep_half[None])
    split_legendre = legendre_synth(
        split_prepared.reshape(split_count * 4, degrees, half_width), own_legendre
    )
    partial_surface = fourier_synth(split_legendre, own_fourier)
    split_surface = partial_surface + from_partner(
        partial_surface.astype(jnp.bfloat16), "row", 0
    ).astype(partial_surface.dtype)
    _, split_grid = traction(split_surface.reshape(split_count, 4, nlat, nlon), own_material)
    near_grid = jnp.stack([radius, traction_grid], axis=1).astype(jnp.bfloat16)
    point_count = 4
    target_normal = normals[:, nlat // 4 :: nlat // 2, :: nlon // 2].reshape(3, point_count)
    devices = lax.axis_size("row") * lax.axis_size("col")
    all_points = lax.all_to_all(
        jnp.broadcast_to(own_points.reshape(1, -1), (devices, drop_count * point_count)),
        ("row", "col"),
        split_axis=0,
        concat_axis=0,
        tiled=True,
    ).reshape(devices * drop_count, point_count)
    total_drops = all_points.shape[0]
    readers = reader_dev.shape[1]
    target = (reader_dev * drop_count + reader_slot).reshape(-1)
    pick = (target[:, None] == jnp.arange(total_drops, dtype=jnp.int32)[None, :]).astype(
        jnp.float32
    )
    target_radius = jnp.dot(pick, all_points.astype(jnp.float32), precision=HIGH)
    target_point = separation.reshape(3, drop_count * readers)[:, :, None] + (
        target_radius[None] * target_normal[:, None, :]
    )
    target_point = jnp.transpose(
        target_point.reshape(3, drop_count, readers * point_count), (1, 2, 0)
    )
    target_square = jnp.sum(target_point * target_point, axis=2) + SOFTENING
    entry_table = jnp.concatenate(
        [
            jnp.transpose(separation, (1, 2, 0)),
            target_radius.reshape(drop_count, readers, point_count),
            target_square.reshape(drop_count, readers, point_count),
        ],
        axis=2,
    ).reshape(-1)
    cell_table = cell_tables(nlat, nlon, point_count)
    partial = near_field(entry_table, near_grid, cell_table, readers, point_count)
    partial, traction_grid = lax.optimization_barrier((partial, traction_grid))
    sums = jnp.sum(partial, axis=3)
    contribution = (
        sums[:, :3] + jnp.transpose(target_point, (0, 2, 1)) * sums[:, 3:]
    ) / (8.0 * math.pi)
    contribution = jnp.transpose(
        contribution.reshape(drop_count, 3, readers, point_count), (0, 2, 1, 3)
    ).reshape(drop_count * readers, 3 * point_count)
    destination = reader_dev.reshape(-1)
    capacity = 2
    onehot = (destination[:, None] == jnp.arange(devices, dtype=jnp.int32)[None, :]).astype(
        jnp.int32
    )
    rank = jnp.sum((jnp.cumsum(onehot, axis=0) - onehot) * onehot, axis=1)
    position = destination * capacity + rank
    place = (position[:, None] == jnp.arange(devices * capacity, dtype=jnp.int32)[None, :]).astype(
        jnp.float32
    )
    record = jnp.concatenate(
        [contribution, reader_slot.reshape(-1, 1).astype(jnp.float32)], axis=1
    )
    outgoing = jnp.dot(jnp.transpose(place), record, precision=HIGH)
    incoming = lax.all_to_all(
        outgoing.reshape(devices, capacity, record.shape[1]),
        ("row", "col"),
        split_axis=0,
        concat_axis=0,
        tiled=True,
    ).reshape(devices * capacity, record.shape[1])
    slot_pick = (
        incoming[:, -1:] == jnp.arange(drop_count, dtype=jnp.float32)[None, :]
    ).astype(jnp.float32)
    mine = jnp.dot(jnp.transpose(slot_pick), incoming[:, :-1], precision=HIGH)
    near_velocity = jnp.transpose(mine.reshape(drop_count, 3, point_count), (1, 0, 2))
    traction_coeffs = (
        analysis_legendre(analysis_fourier(traction_grid, fourier, quad_weight), legendre)
        * keep_mask
    )
    coef_grid = analysis_fourier(split_grid, fourier, quad_weight)
    own_grid = lax.dynamic_slice_in_dim(coef_grid, half_index * half_orders, half_orders, 3)
    split_traction = analysis_legendre(own_grid, own_legendre) * keep_half[None]
    return (traction_coeffs, split_traction, near_velocity.reshape(3, drop_count * point_count))


def point_table(degrees):
    legendre, fourier, _, _ = (np.asarray(t) for t in spectral_tables_np(degrees))
    lat = np.arange(degrees // 4, degrees, degrees // 2)
    lon = np.arange(0, 2 * degrees, degrees)
    orders = np.arange(2 * degrees) % degrees
    table = np.zeros((degrees, 2 * degrees, lat.size * lon.size))
    for i, j in enumerate(lat):
        for k, col in enumerate(lon):
            table[:, :, i * lon.size + k] = (
                legendre[orders, j, :].T.astype(np.float64) * fourier[:, col][None, :]
            )
    return jnp.asarray(table.reshape(degrees * 2 * degrees, -1), dtype=jnp.float32)


def cell_tables(nlat, nlon, point_count):
    theta = (np.arange(nlat) + 0.5) * (math.pi / nlat)
    longitude = np.arange(nlon) * (2.0 * math.pi / nlon)
    quad_weight = (np.sin(theta) * (math.pi / nlat) * (2.0 * math.pi / nlon)).astype(np.float32)
    normals = np.stack(
        [
            np.sin(theta)[:, None] * np.cos(longitude)[None, :],
            np.sin(theta)[:, None] * np.sin(longitude)[None, :],
            np.cos(theta)[:, None] * np.ones((1, nlon)),
        ],
        axis=0,
    ).astype(np.float32)
    points = normals[:, nlat // 4 :: nlat // 2, :: nlon // 2].reshape(3, point_count)
    facing = np.einsum("dp,djk->pjk", points.astype(np.float64), normals.astype(np.float64))
    weight = np.broadcast_to(quad_weight[None, :, None], (1, nlat, nlon))
    table = np.concatenate([normals, facing.astype(np.float32), weight], axis=0)
    return jnp.asarray(table, dtype=jnp.float32)


def near_kernel(points, t_ref, g_ref, c_ref, o_ref, s_ref):
    drop = pl.program_id(0)
    entries = o_ref.shape[2] // points
    width = 3 + 2 * points
    chunks = g_ref.shape[2] // 8
    r = g_ref[0, 0].astype(jnp.float32)
    s_ref[0] = r
    s_ref[1] = r * r
    s_ref[2] = r + r
    s_ref[3] = g_ref[0, 1].astype(jnp.float32) * r * r * c_ref[3 + points]

    def body(e, carry):
        base = (drop * entries + e) * width
        sx = t_ref[base]
        sy = t_ref[base + 1]
        sz = t_ref[base + 2]
        lift = [t_ref[base + 3 + k] for k in range(points)]
        tt = [t_ref[base + 3 + points + k] for k in range(points)]
        acc = [[jnp.zeros((8, 128), jnp.float32) for _ in range(4)] for _ in range(points)]
        for c in range(chunks):
            rows = pl.ds(c * 8, 8)
            nx = c_ref[0, rows, :]
            ny = c_ref[1, rows, :]
            nz = c_ref[2, rows, :]
            rr = s_ref[0, rows, :]
            r2 = s_ref[1, rows, :]
            twice = s_ref[2, rows, :]
            load = s_ref[3, rows, :]
            shared = sx * nx + sy * ny + sz * nz
            for k in range(points):
                along = shared + lift[k] * c_ref[3 + k, rows, :]
                soft = (tt[k] + r2) - twice * along
                inv = lax.rsqrt(soft)
                w = load * (inv * inv * inv)
                dn = along - rr
                h = w * ((soft + SOFTENING) - dn * rr)
                hx, hy, hz, sq = acc[k]
                acc[k] = [hx + h * nx, hy + h * ny, hz + h * nz, sq + w * dn]
        for k in range(points):
            row = pl.ds(e * points + k, 1)
            for comp in range(4):
                o_ref[0, comp, row, :] = jnp.sum(acc[k][comp], axis=0, keepdims=True)
        return carry

    lax.fori_loop(0, entries, body, 0)


def near_field(entry_table, near_grid, cell_table, readers, points):
    drops, fields, nlat, nlon = near_grid.shape
    targets = readers * points
    cells = drops * targets * nlat * nlon
    return pl.pallas_call(
        functools.partial(near_kernel, points),
        grid=(drops,),
        in_specs=[
            pl.BlockSpec(memory_space=pltpu.SMEM),
            pl.BlockSpec((1, fields, nlat, nlon), lambda s: (s, 0, 0, 0)),
            pl.BlockSpec(cell_table.shape, lambda s: (0, 0, 0)),
        ],
        out_specs=pl.BlockSpec((1, 4, targets, nlon), lambda s: (s, 0, 0, 0)),
        out_shape=jax.ShapeDtypeStruct((drops, 4, targets, nlon), jnp.float32),
        scratch_shapes=[pltpu.VMEM((4, nlat, nlon), jnp.float32)],
        cost_estimate=pl.CostEstimate(
            flops=24 * cells, transcendentals=cells, bytes_accessed=2 * drops * fields * nlat * nlon
        ),
    )(entry_table, near_grid, cell_table)


def solution(mesh):
    in_specs = (
        P(("row", "col"), None, None, None),
        P(("row", "col")),
        P(("row", "col"), None),
        P(("row", "col"), None, None, None),
        P(),
        P(None, ("row", "col"), None),
        P(("row", "col"), None),
        P(("row", "col"), None),
    )
    out_specs = (
        P(("row", "col"), None, None),
        P(("row", "col"), None, None),
        P(None, ("row", "col")),
    )
    return jax.shard_map(
        per_device, mesh=mesh, in_specs=in_specs, out_specs=out_specs, check_vma=False
    )
```

```python
import functools
import math

import jax
import jax.numpy as jnp
import numpy as np
from jax import lax
from jax.experimental import pallas as pl
from jax.experimental.pallas import tpu as pltpu
from jax.sharding import PartitionSpec as P

HIGH = lax.Precision.HIGHEST
SPECTRAL = lax.Precision.DEFAULT
SOFTENING = 0.04


def from_partner(block, axis, stride):
    count = lax.axis_size(axis)
    route = []
    for low in range(count):
        high = low | 1 << stride
        if high != low and high < count:
            route += [(low, high), (high, low)]
    return lax.ppermute(block, axis, route)


def spectral_tables(degrees):
    nlon = 2 * degrees
    theta_lat = (np.arange(degrees) + 0.5) * (math.pi / degrees)
    cosine = np.cos(theta_lat)
    sine_theta = np.sin(theta_lat)
    legendre = np.zeros((degrees, degrees, degrees))
    for order in range(degrees):
        log_total = 0.0
        for step_index in range(1, order + 1):
            log_total = log_total + math.log((2.0 * step_index + 1.0) / (2.0 * step_index))
        diag_value = np.exp(0.5 * log_total + order * np.log(sine_theta)) / math.sqrt(4.0 * math.pi)
        legendre[order, :, order] = diag_value
        prev_two = diag_value
        if order + 1 < degrees:
            prev_one = math.sqrt(2.0 * order + 3.0) * cosine * diag_value
            legendre[order, :, order + 1] = prev_one
            for level in range(order + 2, degrees):
                alpha_term = math.sqrt(
                    (4.0 * level * level - 1.0) / (level * level - order * order)
                )
                beta_term = math.sqrt(
                    ((level - 1.0) ** 2 - order * order) / (4.0 * (level - 1.0) ** 2 - 1.0)
                )
                current = alpha_term * (cosine * prev_one - beta_term * prev_two)
                legendre[order, :, level] = current
                prev_two = prev_one
                prev_one = current
    order_index = np.arange(degrees)
    lon_index = np.arange(nlon)
    phase_angle = order_index[:, None] * lon_index[None, :] % nlon * (2.0 * math.pi / nlon)
    fourier = np.concatenate([np.cos(phase_angle), np.sin(phase_angle)], axis=0)
    quad_weight = sine_theta * (math.pi / degrees) * (2.0 * math.pi / nlon)
    longitude = lon_index * (2.0 * math.pi / nlon)
    normals = np.stack(
        [
            sine_theta[:, None] * np.cos(longitude)[None, :],
            sine_theta[:, None] * np.sin(longitude)[None, :],
            cosine[:, None] * np.ones((1, nlon)),
        ],
        axis=0,
    )
    return (
        jnp.asarray(legendre, dtype=jnp.float32),
        jnp.asarray(fourier, dtype=jnp.float32),
        jnp.asarray(quad_weight, dtype=jnp.float32),
        jnp.asarray(normals, dtype=jnp.float32),
    )


def spectral_tables_np(degrees):
    nlon = 2 * degrees
    theta_lat = (np.arange(degrees) + 0.5) * (math.pi / degrees)
    cosine = np.cos(theta_lat)
    sine_theta = np.sin(theta_lat)
    legendre = np.zeros((degrees, degrees, degrees))
    for order in range(degrees):
        log_total = 0.0
        for step_index in range(1, order + 1):
            log_total = log_total + math.log((2.0 * step_index + 1.0) / (2.0 * step_index))
        diag_value = np.exp(0.5 * log_total + order * np.log(sine_theta)) / math.sqrt(4.0 * math.pi)
        legendre[order, :, order] = diag_value
        prev_two = diag_value
        if order + 1 < degrees:
            prev_one = math.sqrt(2.0 * order + 3.0) * cosine * diag_value
            legendre[order, :, order + 1] = prev_one
            for level in range(order + 2, degrees):
                alpha_term = math.sqrt(
                    (4.0 * level * level - 1.0) / (level * level - order * order)
                )
                beta_term = math.sqrt(
                    ((level - 1.0) ** 2 - order * order) / (4.0 * (level - 1.0) ** 2 - 1.0)
                )
                current = alpha_term * (cosine * prev_one - beta_term * prev_two)
                legendre[order, :, level] = current
                prev_two = prev_one
                prev_one = current
    order_index = np.arange(degrees)
    lon_index = np.arange(nlon)
    phase_angle = order_index[:, None] * lon_index[None, :] % nlon * (2.0 * math.pi / nlon)
    fourier = np.concatenate([np.cos(phase_angle), np.sin(phase_angle)], axis=0)
    quad_weight = sine_theta * (math.pi / degrees) * (2.0 * math.pi / nlon)
    longitude = lon_index * (2.0 * math.pi / nlon)
    normals = np.stack(
        [
            sine_theta[:, None] * np.cos(longitude)[None, :],
            sine_theta[:, None] * np.sin(longitude)[None, :],
            cosine[:, None] * np.ones((1, nlon)),
        ],
        axis=0,
    )
    return (
        legendre.astype(np.float32),
        fourier.astype(np.float32),
        quad_weight.astype(np.float32),
        normals.astype(np.float32),
    )


def legendre_synth(coeff, legendre):
    batch_size, degrees, _ = coeff.shape
    orders = legendre.shape[0]
    parted = coeff.reshape(batch_size, degrees, 2, orders)
    return jnp.einsum("mjl,nlcm->njcm", legendre, parted, precision=SPECTRAL)


def fourier_synth(partial_legendre, fourier_rows):
    batch_size, nlat, two, orders = partial_legendre.shape
    return jnp.einsum(
        "njw,wk->njk",
        partial_legendre.reshape(batch_size, nlat, two * orders),
        fourier_rows,
        precision=SPECTRAL,
    )


def analysis_fourier(traction_grid, fourier, quad_weight):
    batch_size, nlat, _ = traction_grid.shape
    projected = (
        jnp.einsum("bjk,wk->bjw", traction_grid, fourier, precision=SPECTRAL)
        * quad_weight[None, :, None]
    )
    return projected.reshape(batch_size, nlat, 2, fourier.shape[0] // 2)


def analysis_legendre(coef_grid, legendre):
    batch_size = coef_grid.shape[0]
    result = jnp.einsum("mjl,bjcm->blcm", legendre, coef_grid, precision=SPECTRAL)
    return result.reshape(batch_size, legendre.shape[2], 2 * legendre.shape[0])


def prepare(coeffs, keep_mask):
    degrees = coeffs.shape[2]
    degree_value = jnp.arange(degrees, dtype=jnp.float32)
    shape_part = coeffs[:, 0] * keep_mask
    curvature = (
        shape_part * (degree_value * (degree_value + 1.0) / (degrees * degrees))[None, :, None]
    )
    electric = 3.0 * coeffs[:, 1] * keep_mask
    viscous = 3.0 * coeffs[:, 2] * keep_mask * ((degree_value + 2.0) / degrees)[None, :, None]
    return jnp.stack([shape_part, curvature, electric, viscous], axis=1)


def traction(surface, material):
    radius = jnp.exp(surface[:, 0])
    traction_grid = (
        material[:, 0, None, None] * surface[:, 1]
        + 0.5 * surface[:, 2] * surface[:, 2]
        + 2.0 * material[:, 1, None, None] * surface[:, 3]
    )
    return (radius, traction_grid)


def per_device(
    coeffs, degree, material, split_coeffs, split_material, separation, reader_dev, reader_slot
):
    drop_count, _, degrees, coef_width = coeffs.shape
    legendre, fourier, quad_weight, normals = spectral_tables(degrees)
    nlat = legendre.shape[1]
    nlon = fourier.shape[1]
    degree_index = jnp.arange(degrees, dtype=jnp.int32)
    order_full = jnp.arange(coef_width, dtype=jnp.int32) % degrees
    order_mask = (degree_index[:, None] >= order_full[None, :]).astype(jnp.float32)
    keep_mask = order_mask[None] * (degree_index[None, :, None] <= degree[:, None, None]).astype(
        jnp.float32
    )
    prepared = prepare(coeffs, keep_mask)
    point_weight = point_table(degrees)
    point_surface = jnp.dot(
        (coeffs[:, 0] * keep_mask).reshape(drop_count, degrees * coef_width),
        point_weight,
        precision=lax.Precision.HIGH,
    )
    own_points = jnp.exp(point_surface).astype(jnp.bfloat16)
    batched = jnp.einsum(
        "mjl,nlcm->mcnj",
        legendre,
        prepared.reshape(drop_count * 4, degrees, 2, degrees),
        precision=SPECTRAL,
    )
    surface = jnp.einsum(
        "mcnj,cmk->njk", batched, fourier.reshape(2, degrees, nlon), precision=SPECTRAL
    ).reshape(drop_count, 4, nlat, nlon)
    radius, traction_grid = traction(surface, material)
    split_count = split_coeffs.shape[0]
    half_width = split_coeffs.shape[3]
    half_orders = half_width // 2
    half_index = lax.axis_index("row") % 2
    pair_start = (
        lax.axis_index("row") // 2 * lax.axis_size("col") + lax.axis_index("col")
    ) * split_count
    own_material = lax.dynamic_slice_in_dim(split_material, pair_start, split_count, 0)
    own_order = half_index * half_orders + jnp.arange(half_width, dtype=jnp.int32) % half_orders
    keep_half = (degree_index[:, None] >= own_order[None, :]).astype(jnp.float32)
    own_legendre = lax.dynamic_slice_in_dim(legendre, half_index * half_orders, half_orders, 0)
    own_fourier = lax.dynamic_slice_in_dim(
        fourier.reshape(2, degrees, nlon), half_index * half_orders, half_orders, 1
    ).reshape(half_width, nlon)
    split_prepared = prepare(split_coeffs, keep_half[None])
    split_legendre = legendre_synth(
        split_prepared.reshape(split_count * 4, degrees, half_width), own_legendre
    )
    partial_surface = fourier_synth(split_legendre, own_fourier)
    split_surface = partial_surface + from_partner(
        partial_surface.astype(jnp.bfloat16), "row", 0
    ).astype(partial_surface.dtype)
    _, split_grid = traction(split_surface.reshape(split_count, 4, nlat, nlon), own_material)
    near_grid = jnp.stack([radius, traction_grid], axis=1).astype(jnp.bfloat16)
    point_count = 4
    target_normal = normals[:, nlat // 4 :: nlat // 2, :: nlon // 2].reshape(3, point_count)
    devices = lax.axis_size("row") * lax.axis_size("col")
    all_points = lax.all_to_all(
        jnp.broadcast_to(own_points.reshape(1, -1), (devices, drop_count * point_count)),
        ("row", "col"),
        split_axis=0,
        concat_axis=0,
        tiled=True,
    ).reshape(devices * drop_count, point_count)
    total_drops = all_points.shape[0]
    readers = reader_dev.shape[1]
    target = (reader_dev * drop_count + reader_slot).reshape(-1)
    pick = (target[:, None] == jnp.arange(total_drops, dtype=jnp.int32)[None, :]).astype(
        jnp.float32
    )
    target_radius = jnp.dot(pick, all_points.astype(jnp.float32), precision=HIGH)
    target_point = separation.reshape(3, drop_count * readers)[:, :, None] + (
        target_radius[None] * target_normal[:, None, :]
    )
    target_point = jnp.transpose(
        target_point.reshape(3, drop_count, readers * point_count), (1, 2, 0)
    )
    target_square = jnp.sum(target_point * target_point, axis=2) + SOFTENING
    entry_table = jnp.concatenate(
        [
            jnp.transpose(separation, (1, 2, 0)),
            target_radius.reshape(drop_count, readers, point_count),
            target_square.reshape(drop_count, readers, point_count),
        ],
        axis=2,
    ).reshape(-1)
    cell_table = cell_tables(nlat, nlon, point_count)
    partial = near_field(entry_table, near_grid, cell_table, readers, point_count)
    partial, traction_grid = lax.optimization_barrier((partial, traction_grid))
    sums = jnp.sum(partial, axis=3)
    contribution = (
        sums[:, :3] + jnp.transpose(target_point, (0, 2, 1)) * sums[:, 3:]
    ) / (8.0 * math.pi)
    contribution = jnp.transpose(
        contribution.reshape(drop_count, 3, readers, point_count), (0, 2, 1, 3)
    ).reshape(drop_count * readers, 3 * point_count)
    destination = reader_dev.reshape(-1)
    capacity = 2
    onehot = (destination[:, None] == jnp.arange(devices, dtype=jnp.int32)[None, :]).astype(
        jnp.int32
    )
    rank = jnp.sum((jnp.cumsum(onehot, axis=0) - onehot) * onehot, axis=1)
    position = destination * capacity + rank
    place = (position[:, None] == jnp.arange(devices * capacity, dtype=jnp.int32)[None, :]).astype(
        jnp.float32
    )
    record = jnp.concatenate(
        [contribution, reader_slot.reshape(-1, 1).astype(jnp.float32)], axis=1
    )
    outgoing = jnp.dot(jnp.transpose(place), record, precision=HIGH)
    incoming = lax.all_to_all(
        outgoing.reshape(devices, capacity, record.shape[1]),
        ("row", "col"),
        split_axis=0,
        concat_axis=0,
        tiled=True,
    ).reshape(devices * capacity, record.shape[1])
    slot_pick = (
        incoming[:, -1:] == jnp.arange(drop_count, dtype=jnp.float32)[None, :]
    ).astype(jnp.float32)
    mine = jnp.dot(jnp.transpose(slot_pick), incoming[:, :-1], precision=HIGH)
    near_velocity = jnp.transpose(mine.reshape(drop_count, 3, point_count), (1, 0, 2))
    traction_coeffs = (
        analysis_legendre(analysis_fourier(traction_grid, fourier, quad_weight), legendre)
        * keep_mask
    )
    coef_grid = analysis_fourier(split_grid, fourier, quad_weight)
    own_grid = lax.dynamic_slice_in_dim(coef_grid, half_index * half_orders, half_orders, 3)
    split_traction = analysis_legendre(own_grid, own_legendre) * keep_half[None]
    return (traction_coeffs, split_traction, near_velocity.reshape(3, drop_count * point_count))


def point_table(degrees):
    legendre, fourier, _, _ = (np.asarray(t) for t in spectral_tables_np(degrees))
    lat = np.arange(degrees // 4, degrees, degrees // 2)
    lon = np.arange(0, 2 * degrees, degrees)
    orders = np.arange(2 * degrees) % degrees
    table = np.zeros((degrees, 2 * degrees, lat.size * lon.size))
    for i, j in enumerate(lat):
        for k, col in enumerate(lon):
            table[:, :, i * lon.size + k] = (
                legendre[orders, j, :].T.astype(np.float64) * fourier[:, col][None, :]
            )
    return jnp.asarray(table.reshape(degrees * 2 * degrees, -1), dtype=jnp.float32)


def cell_tables(nlat, nlon, point_count):
    theta = (np.arange(nlat) + 0.5) * (math.pi / nlat)
    longitude = np.arange(nlon) * (2.0 * math.pi / nlon)
    quad_weight = (np.sin(theta) * (math.pi / nlat) * (2.0 * math.pi / nlon)).astype(np.float32)
    normals = np.stack(
        [
            np.sin(theta)[:, None] * np.cos(longitude)[None, :],
            np.sin(theta)[:, None] * np.sin(longitude)[None, :],
            np.cos(theta)[:, None] * np.ones((1, nlon)),
        ],
        axis=0,
    ).astype(np.float32)
    points = normals[:, nlat // 4 :: nlat // 2, :: nlon // 2].reshape(3, point_count)
    facing = np.einsum("dp,djk->pjk", points.astype(np.float64), normals.astype(np.float64))
    weight = np.broadcast_to(quad_weight[None, :, None], (1, nlat, nlon))
    table = np.concatenate([normals, facing.astype(np.float32), weight], axis=0)
    return jnp.asarray(table, dtype=jnp.float32)


def near_kernel(points, t_ref, g_ref, c_ref, o_ref, s_ref):
    drop = pl.program_id(0)
    entries = o_ref.shape[2] // points
    width = 3 + 2 * points
    chunks = g_ref.shape[2] // 8
    r = g_ref[0, 0].astype(jnp.float32)
    s_ref[0] = r
    s_ref[1] = r * r
    s_ref[2] = r + r
    s_ref[3] = g_ref[0, 1].astype(jnp.float32) * r * r * c_ref[3 + points]

    def body(e, carry):
        base = (drop * entries + e) * width
        sx = t_ref[base]
        sy = t_ref[base + 1]
        sz = t_ref[base + 2]
        lift = [t_ref[base + 3 + k] for k in range(points)]
        tt = [t_ref[base + 3 + points + k] for k in range(points)]
        acc = [[jnp.zeros((8, 128), jnp.float32) for _ in range(4)] for _ in range(points)]
        for c in range(chunks):
            rows = pl.ds(c * 8, 8)
            nx = c_ref[0, rows, :]
            ny = c_ref[1, rows, :]
            nz = c_ref[2, rows, :]
            rr = s_ref[0, rows, :]
            r2 = s_ref[1, rows, :]
            twice = s_ref[2, rows, :]
            load = s_ref[3, rows, :]
            shared = sx * nx + sy * ny + sz * nz
            for k in range(points):
                along = shared + lift[k] * c_ref[3 + k, rows, :]
                soft = (tt[k] + r2) - twice * along
                inv = lax.rsqrt(soft)
                w = load * (inv * inv * inv)
                dn = along - rr
                h = w * ((soft + SOFTENING) - dn * rr)
                hx, hy, hz, sq = acc[k]
                acc[k] = [hx + h * nx, hy + h * ny, hz + h * nz, sq + w * dn]
        for k in range(points):
            row = pl.ds(e * points + k, 1)
            for comp in range(4):
                o_ref[0, comp, row, :] = jnp.sum(acc[k][comp], axis=0, keepdims=True)
        return carry

    lax.fori_loop(0, entries, body, 0)


def near_field(entry_table, near_grid, cell_table, readers, points):
    drops, fields, nlat, nlon = near_grid.shape
    targets = readers * points
    cells = drops * targets * nlat * nlon
    return pl.pallas_call(
        functools.partial(near_kernel, points),
        grid=(drops,),
        in_specs=[
            pl.BlockSpec(memory_space=pltpu.SMEM),
            pl.BlockSpec((1, fields, nlat, nlon), lambda s: (s, 0, 0, 0)),
            pl.BlockSpec(cell_table.shape, lambda s: (0, 0, 0)),
        ],
        out_specs=pl.BlockSpec((1, 4, targets, nlon), lambda s: (s, 0, 0, 0)),
        out_shape=jax.ShapeDtypeStruct((drops, 4, targets, nlon), jnp.float32),
        scratch_shapes=[pltpu.VMEM((4, nlat, nlon), jnp.float32)],
        cost_estimate=pl.CostEstimate(
            flops=24 * cells, transcendentals=cells, bytes_accessed=2 * drops * fields * nlat * nlon
        ),
    )(entry_table, near_grid, cell_table)


def solution(mesh):
    in_specs = (
        P(("row", "col"), None, None, None),
        P(("row", "col")),
        P(("row", "col"), None),
        P(("row", "col"), None, None, None),
        P(),
        P(None, ("row", "col"), None),
        P(("row", "col"), None),
        P(("row", "col"), None),
    )
    out_specs = (
        P(("row", "col"), None, None),
        P(("row", "col"), None, None),
        P(None, ("row", "col")),
    )
    return jax.shard_map(
        per_device, mesh=mesh, in_specs=in_specs, out_specs=out_specs, check_vma=False
    )
```

```python
import functools
import math

import jax
import jax.numpy as jnp
import numpy as np
from jax import lax
from jax.experimental import pallas as pl
from jax.experimental.pallas import tpu as pltpu
from jax.sharding import PartitionSpec as P

HIGH = lax.Precision.HIGHEST
SPECTRAL = lax.Precision.DEFAULT
SOFTENING = 0.04


def from_partner(block, axis, stride):
    count = lax.axis_size(axis)
    route = []
    for low in range(count):
        high = low | 1 << stride
        if high != low and high < count:
            route += [(low, high), (high, low)]
    return lax.ppermute(block, axis, route)


def spectral_tables(degrees):
    nlon = 2 * degrees
    theta_lat = (np.arange(degrees) + 0.5) * (math.pi / degrees)
    cosine = np.cos(theta_lat)
    sine_theta = np.sin(theta_lat)
    legendre = np.zeros((degrees, degrees, degrees))
    for order in range(degrees):
        log_total = 0.0
        for step_index in range(1, order + 1):
            log_total = log_total + math.log((2.0 * step_index + 1.0) / (2.0 * step_index))
        diag_value = np.exp(0.5 * log_total + order * np.log(sine_theta)) / math.sqrt(4.0 * math.pi)
        legendre[order, :, order] = diag_value
        prev_two = diag_value
        if order + 1 < degrees:
            prev_one = math.sqrt(2.0 * order + 3.0) * cosine * diag_value
            legendre[order, :, order + 1] = prev_one
            for level in range(order + 2, degrees):
                alpha_term = math.sqrt(
                    (4.0 * level * level - 1.0) / (level * level - order * order)
                )
                beta_term = math.sqrt(
                    ((level - 1.0) ** 2 - order * order) / (4.0 * (level - 1.0) ** 2 - 1.0)
                )
                current = alpha_term * (cosine * prev_one - beta_term * prev_two)
                legendre[order, :, level] = current
                prev_two = prev_one
                prev_one = current
    order_index = np.arange(degrees)
    lon_index = np.arange(nlon)
    phase_angle = order_index[:, None] * lon_index[None, :] % nlon * (2.0 * math.pi / nlon)
    fourier = np.concatenate([np.cos(phase_angle), np.sin(phase_angle)], axis=0)
    quad_weight = sine_theta * (math.pi / degrees) * (2.0 * math.pi / nlon)
    longitude = lon_index * (2.0 * math.pi / nlon)
    normals = np.stack(
        [
            sine_theta[:, None] * np.cos(longitude)[None, :],
            sine_theta[:, None] * np.sin(longitude)[None, :],
            cosine[:, None] * np.ones((1, nlon)),
        ],
        axis=0,
    )
    return (
        jnp.asarray(legendre, dtype=jnp.float32),
        jnp.asarray(fourier, dtype=jnp.float32),
        jnp.asarray(quad_weight, dtype=jnp.float32),
        jnp.asarray(normals, dtype=jnp.float32),
    )


def spectral_tables_np(degrees):
    nlon = 2 * degrees
    theta_lat = (np.arange(degrees) + 0.5) * (math.pi / degrees)
    cosine = np.cos(theta_lat)
    sine_theta = np.sin(theta_lat)
    legendre = np.zeros((degrees, degrees, degrees))
    for order in range(degrees):
        log_total = 0.0
        for step_index in range(1, order + 1):
            log_total = log_total + math.log((2.0 * step_index + 1.0) / (2.0 * step_index))
        diag_value = np.exp(0.5 * log_total + order * np.log(sine_theta)) / math.sqrt(4.0 * math.pi)
        legendre[order, :, order] = diag_value
        prev_two = diag_value
        if order + 1 < degrees:
            prev_one = math.sqrt(2.0 * order + 3.0) * cosine * diag_value
            legendre[order, :, order + 1] = prev_one
            for level in range(order + 2, degrees):
                alpha_term = math.sqrt(
                    (4.0 * level * level - 1.0) / (level * level - order * order)
                )
                beta_term = math.sqrt(
                    ((level - 1.0) ** 2 - order * order) / (4.0 * (level - 1.0) ** 2 - 1.0)
                )
                current = alpha_term * (cosine * prev_one - beta_term * prev_two)
                legendre[order, :, level] = current
                prev_two = prev_one
                prev_one = current
    order_index = np.arange(degrees)
    lon_index = np.arange(nlon)
    phase_angle = order_index[:, None] * lon_index[None, :] % nlon * (2.0 * math.pi / nlon)
    fourier = np.concatenate([np.cos(phase_angle), np.sin(phase_angle)], axis=0)
    quad_weight = sine_theta * (math.pi / degrees) * (2.0 * math.pi / nlon)
    longitude = lon_index * (2.0 * math.pi / nlon)
    normals = np.stack(
        [
            sine_theta[:, None] * np.cos(longitude)[None, :],
            sine_theta[:, None] * np.sin(longitude)[None, :],
            cosine[:, None] * np.ones((1, nlon)),
        ],
        axis=0,
    )
    return (
        legendre.astype(np.float32),
        fourier.astype(np.float32),
        quad_weight.astype(np.float32),
        normals.astype(np.float32),
    )


def legendre_synth(coeff, legendre):
    batch_size, degrees, _ = coeff.shape
    orders = legendre.shape[0]
    parted = coeff.reshape(batch_size, degrees, 2, orders)
    return jnp.einsum("mjl,nlcm->njcm", legendre, parted, precision=SPECTRAL)


def fourier_synth(partial_legendre, fourier_rows):
    batch_size, nlat, two, orders = partial_legendre.shape
    return jnp.einsum(
        "njw,wk->njk",
        partial_legendre.reshape(batch_size, nlat, two * orders),
        fourier_rows,
        precision=SPECTRAL,
    )


def analysis_fourier(traction_grid, fourier, quad_weight):
    batch_size, nlat, _ = traction_grid.shape
    projected = (
        jnp.einsum("bjk,wk->bjw", traction_grid, fourier, precision=SPECTRAL)
        * quad_weight[None, :, None]
    )
    return projected.reshape(batch_size, nlat, 2, fourier.shape[0] // 2)


def analysis_legendre(coef_grid, legendre):
    batch_size = coef_grid.shape[0]
    result = jnp.einsum("mjl,bjcm->blcm", legendre, coef_grid, precision=SPECTRAL)
    return result.reshape(batch_size, legendre.shape[2], 2 * legendre.shape[0])


def prepare(coeffs, keep_mask):
    degrees = coeffs.shape[2]
    degree_value = jnp.arange(degrees, dtype=jnp.float32)
    shape_part = coeffs[:, 0] * keep_mask
    curvature = (
        shape_part * (degree_value * (degree_value + 1.0) / (degrees * degrees))[None, :, None]
    )
    electric = 3.0 * coeffs[:, 1] * keep_mask
    viscous = 3.0 * coeffs[:, 2] * keep_mask * ((degree_value + 2.0) / degrees)[None, :, None]
    return jnp.stack([shape_part, curvature, electric, viscous], axis=1)


def traction(surface, material):
    radius = jnp.exp(surface[:, 0])
    traction_grid = (
        material[:, 0, None, None] * surface[:, 1]
        + 0.5 * surface[:, 2] * surface[:, 2]
        + 2.0 * material[:, 1, None, None] * surface[:, 3]
    )
    return (radius, traction_grid)


def per_device(
    coeffs, degree, material, split_coeffs, split_material, separation, reader_dev, reader_slot
):
    drop_count, _, degrees, coef_width = coeffs.shape
    legendre, fourier, quad_weight, normals = spectral_tables(degrees)
    nlat = legendre.shape[1]
    nlon = fourier.shape[1]
    degree_index = jnp.arange(degrees, dtype=jnp.int32)
    order_full = jnp.arange(coef_width, dtype=jnp.int32) % degrees
    order_mask = (degree_index[:, None] >= order_full[None, :]).astype(jnp.float32)
    keep_mask = order_mask[None] * (degree_index[None, :, None] <= degree[:, None, None]).astype(
        jnp.float32
    )
    prepared = prepare(coeffs, keep_mask)
    point_weight = point_table(degrees)
    point_surface = jnp.dot(
        (coeffs[:, 0] * keep_mask).reshape(drop_count, degrees * coef_width),
        point_weight,
        precision=lax.Precision.HIGH,
    )
    own_points = jnp.exp(point_surface).astype(jnp.bfloat16)
    batched = jnp.einsum(
        "mjl,nlcm->mcnj",
        legendre,
        prepared.reshape(drop_count * 4, degrees, 2, degrees),
        precision=SPECTRAL,
    )
    surface = jnp.einsum(
        "mcnj,cmk->njk", batched, fourier.reshape(2, degrees, nlon), precision=SPECTRAL
    ).reshape(drop_count, 4, nlat, nlon)
    radius, traction_grid = traction(surface, material)
    split_count = split_coeffs.shape[0]
    half_width = split_coeffs.shape[3]
    half_orders = half_width // 2
    half_index = lax.axis_index("row") % 2
    pair_start = (
        lax.axis_index("row") // 2 * lax.axis_size("col") + lax.axis_index("col")
    ) * split_count
    own_material = lax.dynamic_slice_in_dim(split_material, pair_start, split_count, 0)
    own_order = half_index * half_orders + jnp.arange(half_width, dtype=jnp.int32) % half_orders
    keep_half = (degree_index[:, None] >= own_order[None, :]).astype(jnp.float32)
    own_legendre = lax.dynamic_slice_in_dim(legendre, half_index * half_orders, half_orders, 0)
    own_fourier = lax.dynamic_slice_in_dim(
        fourier.reshape(2, degrees, nlon), half_index * half_orders, half_orders, 1
    ).reshape(half_width, nlon)
    split_prepared = prepare(split_coeffs, keep_half[None])
    split_legendre = legendre_synth(
        split_prepared.reshape(split_count * 4, degrees, half_width), own_legendre
    )
    partial_surface = fourier_synth(split_legendre, own_fourier)
    split_surface = partial_surface + from_partner(
        partial_surface.astype(jnp.bfloat16), "row", 0
    ).astype(partial_surface.dtype)
    _, split_grid = traction(split_surface.reshape(split_count, 4, nlat, nlon), own_material)
    near_grid = jnp.stack([radius, traction_grid], axis=1).astype(jnp.bfloat16)
    point_count = 4
    target_normal = normals[:, nlat // 4 :: nlat // 2, :: nlon // 2].reshape(3, point_count)
    devices = lax.axis_size("row") * lax.axis_size("col")
    all_points = lax.all_to_all(
        jnp.broadcast_to(own_points.reshape(1, -1), (devices, drop_count * point_count)),
        ("row", "col"),
        split_axis=0,
        concat_axis=0,
        tiled=True,
    ).reshape(devices * drop_count, point_count)
    total_drops = all_points.shape[0]
    readers = reader_dev.shape[1]
    target = (reader_dev * drop_count + reader_slot).reshape(-1)
    pick = (target[:, None] == jnp.arange(total_drops, dtype=jnp.int32)[None, :]).astype(
        jnp.float32
    )
    target_radius = jnp.dot(pick, all_points.astype(jnp.float32), precision=HIGH)
    target_point = separation.reshape(3, drop_count * readers)[:, :, None] + (
        target_radius[None] * target_normal[:, None, :]
    )
    target_point = jnp.transpose(
        target_point.reshape(3, drop_count, readers * point_count), (1, 2, 0)
    )
    target_square = jnp.sum(target_point * target_point, axis=2) + SOFTENING
    entry_table = jnp.concatenate(
        [
            jnp.transpose(separation, (1, 2, 0)),
            target_radius.reshape(drop_count, readers, point_count),
            target_square.reshape(drop_count, readers, point_count),
        ],
        axis=2,
    ).reshape(-1)
    cell_table = cell_tables(nlat, nlon, point_count)
    partial = near_field(entry_table, near_grid, cell_table, readers, point_count)
    partial, traction_grid = lax.optimization_barrier((partial, traction_grid))
    sums = partial
    contribution = (
        sums[:, :3] + jnp.transpose(target_point, (0, 2, 1)) * sums[:, 3:]
    ) / (8.0 * math.pi)
    contribution = jnp.transpose(
        contribution.reshape(drop_count, 3, readers, point_count), (0, 2, 1, 3)
    ).reshape(drop_count * readers, 3 * point_count)
    destination = reader_dev.reshape(-1)
    capacity = 2
    onehot = (destination[:, None] == jnp.arange(devices, dtype=jnp.int32)[None, :]).astype(
        jnp.int32
    )
    rank = jnp.sum((jnp.cumsum(onehot, axis=0) - onehot) * onehot, axis=1)
    position = destination * capacity + rank
    place = (position[:, None] == jnp.arange(devices * capacity, dtype=jnp.int32)[None, :]).astype(
        jnp.float32
    )
    record = jnp.concatenate(
        [contribution, reader_slot.reshape(-1, 1).astype(jnp.float32)], axis=1
    )
    outgoing = jnp.dot(jnp.transpose(place), record, precision=HIGH)
    incoming = lax.all_to_all(
        outgoing.reshape(devices, capacity, record.shape[1]),
        ("row", "col"),
        split_axis=0,
        concat_axis=0,
        tiled=True,
    ).reshape(devices * capacity, record.shape[1])
    slot_pick = (
        incoming[:, -1:] == jnp.arange(drop_count, dtype=jnp.float32)[None, :]
    ).astype(jnp.float32)
    mine = jnp.dot(jnp.transpose(slot_pick), incoming[:, :-1], precision=HIGH)
    near_velocity = jnp.transpose(mine.reshape(drop_count, 3, point_count), (1, 0, 2))
    traction_coeffs = (
        analysis_legendre(analysis_fourier(traction_grid, fourier, quad_weight), legendre)
        * keep_mask
    )
    coef_grid = analysis_fourier(split_grid, fourier, quad_weight)
    own_grid = lax.dynamic_slice_in_dim(coef_grid, half_index * half_orders, half_orders, 3)
    split_traction = analysis_legendre(own_grid, own_legendre) * keep_half[None]
    return (traction_coeffs, split_traction, near_velocity.reshape(3, drop_count * point_count))


def point_table(degrees):
    legendre, fourier, _, _ = (np.asarray(t) for t in spectral_tables_np(degrees))
    lat = np.arange(degrees // 4, degrees, degrees // 2)
    lon = np.arange(0, 2 * degrees, degrees)
    orders = np.arange(2 * degrees) % degrees
    table = np.zeros((degrees, 2 * degrees, lat.size * lon.size))
    for i, j in enumerate(lat):
        for k, col in enumerate(lon):
            table[:, :, i * lon.size + k] = (
                legendre[orders, j, :].T.astype(np.float64) * fourier[:, col][None, :]
            )
    return jnp.asarray(table.reshape(degrees * 2 * degrees, -1), dtype=jnp.float32)


def cell_tables(nlat, nlon, point_count):
    theta = (np.arange(nlat) + 0.5) * (math.pi / nlat)
    longitude = np.arange(nlon) * (2.0 * math.pi / nlon)
    quad_weight = (np.sin(theta) * (math.pi / nlat) * (2.0 * math.pi / nlon)).astype(np.float32)
    normals = np.stack(
        [
            np.sin(theta)[:, None] * np.cos(longitude)[None, :],
            np.sin(theta)[:, None] * np.sin(longitude)[None, :],
            np.cos(theta)[:, None] * np.ones((1, nlon)),
        ],
        axis=0,
    ).astype(np.float32)
    points = normals[:, nlat // 4 :: nlat // 2, :: nlon // 2].reshape(3, point_count)
    facing = np.einsum("dp,djk->pjk", points.astype(np.float64), normals.astype(np.float64))
    weight = np.broadcast_to(quad_weight[None, :, None], (1, nlat, nlon))
    table = np.concatenate([normals, facing.astype(np.float32), weight], axis=0)
    return jnp.asarray(table, dtype=jnp.float32)


def near_kernel(points, t_ref, g_ref, c_ref, f_ref, s_ref, o_ref):
    drop = pl.program_id(0)
    entries = o_ref.shape[2] // points
    width = 3 + 2 * points
    chunks = g_ref.shape[2] // 8
    r = g_ref[0, 0].astype(jnp.float32)
    s_ref[0] = r
    s_ref[1] = r * r
    s_ref[2] = r + r
    s_ref[3] = g_ref[0, 1].astype(jnp.float32) * r * r * c_ref[3 + points]

    def body(e, carry):
        base = (drop * entries + e) * width
        sx = t_ref[base]
        sy = t_ref[base + 1]
        sz = t_ref[base + 2]
        lift = [t_ref[base + 3 + k] for k in range(points)]
        tt = [t_ref[base + 3 + points + k] for k in range(points)]
        acc = [[jnp.zeros((8, 128), jnp.float32) for _ in range(4)] for _ in range(points)]
        for c in range(chunks):
            rows = pl.ds(c * 8, 8)
            nx = c_ref[0, rows, :]
            ny = c_ref[1, rows, :]
            nz = c_ref[2, rows, :]
            rr = s_ref[0, rows, :]
            r2 = s_ref[1, rows, :]
            twice = s_ref[2, rows, :]
            load = s_ref[3, rows, :]
            shared = sx * nx + sy * ny + sz * nz
            for k in range(points):
                along = shared + lift[k] * c_ref[3 + k, rows, :]
                soft = (tt[k] + r2) - twice * along
                inv = lax.rsqrt(soft)
                w = load * (inv * inv * inv)
                dn = along - rr
                h = w * ((soft + SOFTENING) - dn * rr)
                hx, hy, hz, sq = acc[k]
                acc[k] = [hx + h * nx, hy + h * ny, hz + h * nz, sq + w * dn]
        for k in range(points):
            row = pl.ds(e * points + k, 1)
            for comp in range(4):
                o_ref[0, comp, row, :] = jnp.sum(acc[k][comp], axis=0, keepdims=True)
        return carry

    lax.fori_loop(0, entries, body, 0)
    rows = o_ref.shape[1] * o_ref.shape[2]
    table = o_ref[0].reshape(rows, o_ref.shape[3])
    ones = jnp.ones((8, o_ref.shape[3]), jnp.float32)
    totals = lax.dot_general(
        ones, table, (((1,), (1,)), ((), ())), precision=HIGH, preferred_element_type=jnp.float32
    )
    f_ref[0] = totals[0:1, :]


def near_field(entry_table, near_grid, cell_table, readers, points):
    drops, fields, nlat, nlon = near_grid.shape
    targets = readers * points
    cells = drops * targets * nlat * nlon
    return pl.pallas_call(
        functools.partial(near_kernel, points),
        grid=(drops,),
        in_specs=[
            pl.BlockSpec(memory_space=pltpu.SMEM),
            pl.BlockSpec((1, fields, nlat, nlon), lambda s: (s, 0, 0, 0)),
            pl.BlockSpec(cell_table.shape, lambda s: (0, 0, 0)),
        ],
        out_specs=pl.BlockSpec((1, 1, 4 * targets), lambda s: (s, 0, 0)),
        out_shape=jax.ShapeDtypeStruct((drops, 1, 4 * targets), jnp.float32),
        scratch_shapes=[
            pltpu.VMEM((4, nlat, nlon), jnp.float32),
            pltpu.VMEM((1, 4, targets, nlon), jnp.float32),
        ],
        cost_estimate=pl.CostEstimate(
            flops=24 * cells, transcendentals=cells, bytes_accessed=2 * drops * fields * nlat * nlon
        ),
    )(entry_table, near_grid, cell_table).reshape(drops, 4, targets)


def solution(mesh):
    in_specs = (
        P(("row", "col"), None, None, None),
        P(("row", "col")),
        P(("row", "col"), None),
        P(("row", "col"), None, None, None),
        P(),
        P(None, ("row", "col"), None),
        P(("row", "col"), None),
        P(("row", "col"), None),
    )
    out_specs = (
        P(("row", "col"), None, None),
        P(("row", "col"), None, None),
        P(None, ("row", "col")),
    )
    return jax.shard_map(
        per_device, mesh=mesh, in_specs=in_specs, out_specs=out_specs, check_vma=False
    )
```

```python
import functools
import math

import jax
import jax.numpy as jnp
import numpy as np
from jax import lax
from jax.experimental import pallas as pl
from jax.experimental.pallas import tpu as pltpu
from jax.sharding import PartitionSpec as P

SPECTRAL = lax.Precision.DEFAULT
SOFTENING = 0.04


def from_partner(block, axis, stride):
    count = lax.axis_size(axis)
    route = []
    for low in range(count):
        high = low | 1 << stride
        if high != low and high < count:
            route += [(low, high), (high, low)]
    return lax.ppermute(block, axis, route)


def spectral_tables(degrees):
    nlon = 2 * degrees
    theta_lat = (np.arange(degrees) + 0.5) * (math.pi / degrees)
    cosine = np.cos(theta_lat)
    sine_theta = np.sin(theta_lat)
    legendre = np.zeros((degrees, degrees, degrees))
    for order in range(degrees):
        log_total = 0.0
        for step_index in range(1, order + 1):
            log_total = log_total + math.log((2.0 * step_index + 1.0) / (2.0 * step_index))
        diag_value = np.exp(0.5 * log_total + order * np.log(sine_theta)) / math.sqrt(4.0 * math.pi)
        legendre[order, :, order] = diag_value
        prev_two = diag_value
        if order + 1 < degrees:
            prev_one = math.sqrt(2.0 * order + 3.0) * cosine * diag_value
            legendre[order, :, order + 1] = prev_one
            for level in range(order + 2, degrees):
                alpha_term = math.sqrt(
                    (4.0 * level * level - 1.0) / (level * level - order * order)
                )
                beta_term = math.sqrt(
                    ((level - 1.0) ** 2 - order * order) / (4.0 * (level - 1.0) ** 2 - 1.0)
                )
                current = alpha_term * (cosine * prev_one - beta_term * prev_two)
                legendre[order, :, level] = current
                prev_two = prev_one
                prev_one = current
    order_index = np.arange(degrees)
    lon_index = np.arange(nlon)
    phase_angle = order_index[:, None] * lon_index[None, :] % nlon * (2.0 * math.pi / nlon)
    fourier = np.concatenate([np.cos(phase_angle), np.sin(phase_angle)], axis=0)
    quad_weight = sine_theta * (math.pi / degrees) * (2.0 * math.pi / nlon)
    longitude = lon_index * (2.0 * math.pi / nlon)
    normals = np.stack(
        [
            sine_theta[:, None] * np.cos(longitude)[None, :],
            sine_theta[:, None] * np.sin(longitude)[None, :],
            cosine[:, None] * np.ones((1, nlon)),
        ],
        axis=0,
    )
    return (
        jnp.asarray(legendre, dtype=jnp.float32),
        jnp.asarray(fourier, dtype=jnp.float32),
        jnp.asarray(quad_weight, dtype=jnp.float32),
        jnp.asarray(normals, dtype=jnp.float32),
    )


def spectral_tables_np(degrees):
    nlon = 2 * degrees
    theta_lat = (np.arange(degrees) + 0.5) * (math.pi / degrees)
    cosine = np.cos(theta_lat)
    sine_theta = np.sin(theta_lat)
    legendre = np.zeros((degrees, degrees, degrees))
    for order in range(degrees):
        log_total = 0.0
        for step_index in range(1, order + 1):
            log_total = log_total + math.log((2.0 * step_index + 1.0) / (2.0 * step_index))
        diag_value = np.exp(0.5 * log_total + order * np.log(sine_theta)) / math.sqrt(4.0 * math.pi)
        legendre[order, :, order] = diag_value
        prev_two = diag_value
        if order + 1 < degrees:
            prev_one = math.sqrt(2.0 * order + 3.0) * cosine * diag_value
            legendre[order, :, order + 1] = prev_one
            for level in range(order + 2, degrees):
                alpha_term = math.sqrt(
                    (4.0 * level * level - 1.0) / (level * level - order * order)
                )
                beta_term = math.sqrt(
                    ((level - 1.0) ** 2 - order * order) / (4.0 * (level - 1.0) ** 2 - 1.0)
                )
                current = alpha_term * (cosine * prev_one - beta_term * prev_two)
                legendre[order, :, level] = current
                prev_two = prev_one
                prev_one = current
    order_index = np.arange(degrees)
    lon_index = np.arange(nlon)
    phase_angle = order_index[:, None] * lon_index[None, :] % nlon * (2.0 * math.pi / nlon)
    fourier = np.concatenate([np.cos(phase_angle), np.sin(phase_angle)], axis=0)
    quad_weight = sine_theta * (math.pi / degrees) * (2.0 * math.pi / nlon)
    longitude = lon_index * (2.0 * math.pi / nlon)
    normals = np.stack(
        [
            sine_theta[:, None] * np.cos(longitude)[None, :],
            sine_theta[:, None] * np.sin(longitude)[None, :],
            cosine[:, None] * np.ones((1, nlon)),
        ],
        axis=0,
    )
    return (
        legendre.astype(np.float32),
        fourier.astype(np.float32),
        quad_weight.astype(np.float32),
        normals.astype(np.float32),
    )


def legendre_synth(coeff, legendre):
    batch_size, degrees, _ = coeff.shape
    orders = legendre.shape[0]
    parted = coeff.reshape(batch_size, degrees, 2, orders)
    return jnp.einsum("mjl,nlcm->njcm", legendre, parted, precision=SPECTRAL)


def fourier_synth(partial_legendre, fourier_rows):
    batch_size, nlat, two, orders = partial_legendre.shape
    return jnp.einsum(
        "njw,wk->njk",
        partial_legendre.reshape(batch_size, nlat, two * orders),
        fourier_rows,
        precision=SPECTRAL,
    )


def analysis_fourier(traction_grid, fourier, quad_weight):
    batch_size, nlat, _ = traction_grid.shape
    projected = (
        jnp.einsum("bjk,wk->bjw", traction_grid, fourier, precision=SPECTRAL)
        * quad_weight[None, :, None]
    )
    return projected.reshape(batch_size, nlat, 2, fourier.shape[0] // 2)


def analysis_legendre(coef_grid, legendre):
    batch_size = coef_grid.shape[0]
    result = jnp.einsum("mjl,bjcm->blcm", legendre, coef_grid, precision=SPECTRAL)
    return result.reshape(batch_size, legendre.shape[2], 2 * legendre.shape[0])


def prepare(coeffs, keep_mask):
    degrees = coeffs.shape[2]
    degree_value = jnp.arange(degrees, dtype=jnp.float32)
    shape_part = coeffs[:, 0] * keep_mask
    curvature = (
        shape_part * (degree_value * (degree_value + 1.0) / (degrees * degrees))[None, :, None]
    )
    electric = 3.0 * coeffs[:, 1] * keep_mask
    viscous = 3.0 * coeffs[:, 2] * keep_mask * ((degree_value + 2.0) / degrees)[None, :, None]
    return jnp.stack([shape_part, curvature, electric, viscous], axis=1)


def traction(surface, material):
    radius = jnp.exp(surface[:, 0])
    traction_grid = (
        material[:, 0, None, None] * surface[:, 1]
        + 0.5 * surface[:, 2] * surface[:, 2]
        + 2.0 * material[:, 1, None, None] * surface[:, 3]
    )
    return (radius, traction_grid)


def per_device(
    coeffs, degree, material, split_coeffs, split_material, separation, reader_dev, reader_slot
):
    drop_count, _, degrees, coef_width = coeffs.shape
    legendre, fourier, quad_weight, normals = spectral_tables(degrees)
    nlat = legendre.shape[1]
    nlon = fourier.shape[1]
    degree_index = jnp.arange(degrees, dtype=jnp.int32)
    order_full = jnp.arange(coef_width, dtype=jnp.int32) % degrees
    order_mask = (degree_index[:, None] >= order_full[None, :]).astype(jnp.float32)
    keep_mask = order_mask[None] * (degree_index[None, :, None] <= degree[:, None, None]).astype(
        jnp.float32
    )
    prepared = prepare(coeffs, keep_mask)
    point_weight = point_table(degrees)
    point_surface = jnp.dot(
        (coeffs[:, 0] * keep_mask).reshape(drop_count, degrees * coef_width),
        point_weight,
        precision=lax.Precision.DEFAULT,
    )
    own_points = jnp.exp(point_surface).astype(jnp.bfloat16)
    batched = jnp.einsum(
        "mjl,nlcm->mcnj",
        legendre,
        prepared.reshape(drop_count * 4, degrees, 2, degrees),
        precision=SPECTRAL,
    )
    surface = jnp.einsum(
        "mcnj,cmk->njk", batched, fourier.reshape(2, degrees, nlon), precision=SPECTRAL
    ).reshape(drop_count, 4, nlat, nlon)
    radius, traction_grid = traction(surface, material)
    split_count = split_coeffs.shape[0]
    half_width = split_coeffs.shape[3]
    half_orders = half_width // 2
    half_index = lax.axis_index("row") % 2
    pair_start = (
        lax.axis_index("row") // 2 * lax.axis_size("col") + lax.axis_index("col")
    ) * split_count
    own_material = lax.dynamic_slice_in_dim(split_material, pair_start, split_count, 0)
    own_order = half_index * half_orders + jnp.arange(half_width, dtype=jnp.int32) % half_orders
    keep_half = (degree_index[:, None] >= own_order[None, :]).astype(jnp.float32)
    own_legendre = lax.dynamic_slice_in_dim(legendre, half_index * half_orders, half_orders, 0)
    own_fourier = lax.dynamic_slice_in_dim(
        fourier.reshape(2, degrees, nlon), half_index * half_orders, half_orders, 1
    ).reshape(half_width, nlon)
    split_prepared = prepare(split_coeffs, keep_half[None])
    split_legendre = legendre_synth(
        split_prepared.reshape(split_count * 4, degrees, half_width), own_legendre
    )
    partial_surface = fourier_synth(split_legendre, own_fourier)
    split_surface = partial_surface + from_partner(
        partial_surface.astype(jnp.bfloat16), "row", 0
    ).astype(partial_surface.dtype)
    _, split_grid = traction(split_surface.reshape(split_count, 4, nlat, nlon), own_material)
    near_grid = jnp.stack([radius, traction_grid], axis=1).astype(jnp.bfloat16)
    point_count = 4
    target_normal = normals[:, nlat // 4 :: nlat // 2, :: nlon // 2].reshape(3, point_count)
    devices = lax.axis_size("row") * lax.axis_size("col")
    all_points = lax.all_to_all(
        jnp.broadcast_to(own_points.reshape(1, -1), (devices, drop_count * point_count)),
        ("row", "col"),
        split_axis=0,
        concat_axis=0,
        tiled=True,
    ).reshape(devices * drop_count, point_count)
    total_drops = all_points.shape[0]
    readers = reader_dev.shape[1]
    target = (reader_dev * drop_count + reader_slot).reshape(-1)
    pick = (target[:, None] == jnp.arange(total_drops, dtype=jnp.int32)[None, :]).astype(
        jnp.float32
    )
    target_radius = jnp.dot(
        pick, all_points.astype(jnp.float32), precision=lax.Precision.DEFAULT
    )
    target_point = separation.reshape(3, drop_count * readers)[:, :, None] + (
        target_radius[None] * target_normal[:, None, :]
    )
    target_point = jnp.transpose(
        target_point.reshape(3, drop_count, readers * point_count), (1, 2, 0)
    )
    target_square = jnp.sum(target_point * target_point, axis=2) + SOFTENING
    entry_table = jnp.concatenate(
        [
            jnp.transpose(separation, (1, 2, 0)),
            target_radius.reshape(drop_count, readers, point_count),
            target_square.reshape(drop_count, readers, point_count),
        ],
        axis=2,
    ).reshape(-1)
    cell_table = cell_tables(nlat, nlon, point_count)
    partial = near_field(entry_table, near_grid, cell_table, readers, point_count)
    partial, traction_grid = lax.optimization_barrier((partial, traction_grid))
    sums = jnp.sum(partial, axis=3)
    contribution = (
        sums[:, :3] + jnp.transpose(target_point, (0, 2, 1)) * sums[:, 3:]
    ) / (8.0 * math.pi)
    contribution = jnp.transpose(
        contribution.reshape(drop_count, 3, readers, point_count), (0, 2, 1, 3)
    ).reshape(drop_count * readers, 3 * point_count)
    destination = reader_dev.reshape(-1)
    capacity = 2
    onehot = (destination[:, None] == jnp.arange(devices, dtype=jnp.int32)[None, :]).astype(
        jnp.int32
    )
    rank = jnp.sum((jnp.cumsum(onehot, axis=0) - onehot) * onehot, axis=1)
    position = destination * capacity + rank
    place = (position[:, None] == jnp.arange(devices * capacity, dtype=jnp.int32)[None, :]).astype(
        jnp.float32
    )
    record = jnp.concatenate(
        [contribution, reader_slot.reshape(-1, 1).astype(jnp.float32)], axis=1
    )
    outgoing = jnp.dot(jnp.transpose(place), record, precision=lax.Precision.HIGH)
    incoming = lax.all_to_all(
        outgoing.reshape(devices, capacity, record.shape[1]),
        ("row", "col"),
        split_axis=0,
        concat_axis=0,
        tiled=True,
    ).reshape(devices * capacity, record.shape[1])
    slot_pick = (
        incoming[:, -1:] == jnp.arange(drop_count, dtype=jnp.float32)[None, :]
    ).astype(jnp.float32)
    mine = jnp.dot(
        jnp.transpose(slot_pick), incoming[:, :-1], precision=lax.Precision.HIGH
    )
    near_velocity = jnp.transpose(mine.reshape(drop_count, 3, point_count), (1, 0, 2))
    traction_coeffs = (
        analysis_legendre(analysis_fourier(traction_grid, fourier, quad_weight), legendre)
        * keep_mask
    )
    coef_grid = analysis_fourier(split_grid, fourier, quad_weight)
    own_grid = lax.dynamic_slice_in_dim(coef_grid, half_index * half_orders, half_orders, 3)
    split_traction = analysis_legendre(own_grid, own_legendre) * keep_half[None]
    return (traction_coeffs, split_traction, near_velocity.reshape(3, drop_count * point_count))


def point_table(degrees):
    legendre, fourier, _, _ = (np.asarray(t) for t in spectral_tables_np(degrees))
    lat = np.arange(degrees // 4, degrees, degrees // 2)
    lon = np.arange(0, 2 * degrees, degrees)
    orders = np.arange(2 * degrees) % degrees
    table = np.zeros((degrees, 2 * degrees, lat.size * lon.size))
    for i, j in enumerate(lat):
        for k, col in enumerate(lon):
            table[:, :, i * lon.size + k] = (
                legendre[orders, j, :].T.astype(np.float64) * fourier[:, col][None, :]
            )
    return jnp.asarray(table.reshape(degrees * 2 * degrees, -1), dtype=jnp.float32)


def cell_tables(nlat, nlon, point_count):
    theta = (np.arange(nlat) + 0.5) * (math.pi / nlat)
    longitude = np.arange(nlon) * (2.0 * math.pi / nlon)
    quad_weight = (np.sin(theta) * (math.pi / nlat) * (2.0 * math.pi / nlon)).astype(np.float32)
    normals = np.stack(
        [
            np.sin(theta)[:, None] * np.cos(longitude)[None, :],
            np.sin(theta)[:, None] * np.sin(longitude)[None, :],
            np.cos(theta)[:, None] * np.ones((1, nlon)),
        ],
        axis=0,
    ).astype(np.float32)
    points = normals[:, nlat // 4 :: nlat // 2, :: nlon // 2].reshape(3, point_count)
    facing = np.einsum("dp,djk->pjk", points.astype(np.float64), normals.astype(np.float64))
    weight = np.broadcast_to(quad_weight[None, :, None], (1, nlat, nlon))
    table = np.concatenate([normals, facing.astype(np.float32), weight], axis=0)
    return jnp.asarray(table, dtype=jnp.float32)


def near_kernel(points, t_ref, g_ref, c_ref, o_ref, s_ref):
    drop = pl.program_id(0)
    entries = o_ref.shape[2] // points
    width = 3 + 2 * points
    chunks = g_ref.shape[2] // 8
    r = g_ref[0, 0].astype(jnp.float32)
    s_ref[0] = r
    s_ref[1] = r * r
    s_ref[2] = r + r
    s_ref[3] = g_ref[0, 1].astype(jnp.float32) * r * r * c_ref[3 + points]

    def body(e, carry):
        base = (drop * entries + e) * width
        sx = t_ref[base]
        sy = t_ref[base + 1]
        sz = t_ref[base + 2]
        lift = [t_ref[base + 3 + k] for k in range(points)]
        tt = [t_ref[base + 3 + points + k] for k in range(points)]
        acc = [[jnp.zeros((8, 128), jnp.float32) for _ in range(4)] for _ in range(points)]
        for c in range(chunks):
            rows = pl.ds(c * 8, 8)
            nx = c_ref[0, rows, :]
            ny = c_ref[1, rows, :]
            nz = c_ref[2, rows, :]
            rr = s_ref[0, rows, :]
            r2 = s_ref[1, rows, :]
            twice = s_ref[2, rows, :]
            load = s_ref[3, rows, :]
            shared = sx * nx + sy * ny + sz * nz
            for k in range(points):
                along = shared + lift[k] * c_ref[3 + k, rows, :]
                soft = (tt[k] + r2) - twice * along
                inv = lax.rsqrt(soft)
                w = load * (inv * inv * inv)
                dn = along - rr
                h = w * ((soft + SOFTENING) - dn * rr)
                hx, hy, hz, sq = acc[k]
                acc[k] = [hx + h * nx, hy + h * ny, hz + h * nz, sq + w * dn]
        for k in range(points):
            row = pl.ds(e * points + k, 1)
            for comp in range(4):
                o_ref[0, comp, row, :] = jnp.sum(acc[k][comp], axis=0, keepdims=True)
        return carry

    lax.fori_loop(0, entries, body, 0)


def near_field(entry_table, near_grid, cell_table, readers, points):
    drops, fields, nlat, nlon = near_grid.shape
    targets = readers * points
    cells = drops * targets * nlat * nlon
    return pl.pallas_call(
        functools.partial(near_kernel, points),
        grid=(drops,),
        in_specs=[
            pl.BlockSpec(memory_space=pltpu.SMEM),
            pl.BlockSpec((1, fields, nlat, nlon), lambda s: (s, 0, 0, 0)),
            pl.BlockSpec(cell_table.shape, lambda s: (0, 0, 0)),
        ],
        out_specs=pl.BlockSpec((1, 4, targets, nlon), lambda s: (s, 0, 0, 0)),
        out_shape=jax.ShapeDtypeStruct((drops, 4, targets, nlon), jnp.float32),
        scratch_shapes=[pltpu.VMEM((4, nlat, nlon), jnp.float32)],
        cost_estimate=pl.CostEstimate(
            flops=24 * cells, transcendentals=cells, bytes_accessed=2 * drops * fields * nlat * nlon
        ),
    )(entry_table, near_grid, cell_table)


def solution(mesh):
    in_specs = (
        P(("row", "col"), None, None, None),
        P(("row", "col")),
        P(("row", "col"), None),
        P(("row", "col"), None, None, None),
        P(),
        P(None, ("row", "col"), None),
        P(("row", "col"), None),
        P(("row", "col"), None),
    )
    out_specs = (
        P(("row", "col"), None, None),
        P(("row", "col"), None, None),
        P(None, ("row", "col")),
    )
    return jax.shard_map(
        per_device, mesh=mesh, in_specs=in_specs, out_specs=out_specs, check_vma=False
    )
```

```python
import functools
import math

import jax
import jax.numpy as jnp
import numpy as np
from jax import lax
from jax.experimental import pallas as pl
from jax.experimental.pallas import tpu as pltpu
from jax.sharding import PartitionSpec as P

SPECTRAL = lax.Precision.DEFAULT
SOFTENING = 0.04


def from_partner(block, axis, stride):
    count = lax.axis_size(axis)
    route = []
    for low in range(count):
        high = low | 1 << stride
        if high != low and high < count:
            route += [(low, high), (high, low)]
    return lax.ppermute(block, axis, route)


def spectral_tables(degrees):
    nlon = 2 * degrees
    theta_lat = (np.arange(degrees) + 0.5) * (math.pi / degrees)
    cosine = np.cos(theta_lat)
    sine_theta = np.sin(theta_lat)
    legendre = np.zeros((degrees, degrees, degrees))
    for order in range(degrees):
        log_total = 0.0
        for step_index in range(1, order + 1):
            log_total = log_total + math.log((2.0 * step_index + 1.0) / (2.0 * step_index))
        diag_value = np.exp(0.5 * log_total + order * np.log(sine_theta)) / math.sqrt(4.0 * math.pi)
        legendre[order, :, order] = diag_value
        prev_two = diag_value
        if order + 1 < degrees:
            prev_one = math.sqrt(2.0 * order + 3.0) * cosine * diag_value
            legendre[order, :, order + 1] = prev_one
            for level in range(order + 2, degrees):
                alpha_term = math.sqrt(
                    (4.0 * level * level - 1.0) / (level * level - order * order)
                )
                beta_term = math.sqrt(
                    ((level - 1.0) ** 2 - order * order) / (4.0 * (level - 1.0) ** 2 - 1.0)
                )
                current = alpha_term * (cosine * prev_one - beta_term * prev_two)
                legendre[order, :, level] = current
                prev_two = prev_one
                prev_one = current
    order_index = np.arange(degrees)
    lon_index = np.arange(nlon)
    phase_angle = order_index[:, None] * lon_index[None, :] % nlon * (2.0 * math.pi / nlon)
    fourier = np.concatenate([np.cos(phase_angle), np.sin(phase_angle)], axis=0)
    quad_weight = sine_theta * (math.pi / degrees) * (2.0 * math.pi / nlon)
    longitude = lon_index * (2.0 * math.pi / nlon)
    normals = np.stack(
        [
            sine_theta[:, None] * np.cos(longitude)[None, :],
            sine_theta[:, None] * np.sin(longitude)[None, :],
            cosine[:, None] * np.ones((1, nlon)),
        ],
        axis=0,
    )
    return (
        jnp.asarray(legendre, dtype=jnp.float32),
        jnp.asarray(fourier, dtype=jnp.float32),
        jnp.asarray(quad_weight, dtype=jnp.float32),
        jnp.asarray(normals, dtype=jnp.float32),
    )


def spectral_tables_np(degrees):
    nlon = 2 * degrees
    theta_lat = (np.arange(degrees) + 0.5) * (math.pi / degrees)
    cosine = np.cos(theta_lat)
    sine_theta = np.sin(theta_lat)
    legendre = np.zeros((degrees, degrees, degrees))
    for order in range(degrees):
        log_total = 0.0
        for step_index in range(1, order + 1):
            log_total = log_total + math.log((2.0 * step_index + 1.0) / (2.0 * step_index))
        diag_value = np.exp(0.5 * log_total + order * np.log(sine_theta)) / math.sqrt(4.0 * math.pi)
        legendre[order, :, order] = diag_value
        prev_two = diag_value
        if order + 1 < degrees:
            prev_one = math.sqrt(2.0 * order + 3.0) * cosine * diag_value
            legendre[order, :, order + 1] = prev_one
            for level in range(order + 2, degrees):
                alpha_term = math.sqrt(
                    (4.0 * level * level - 1.0) / (level * level - order * order)
                )
                beta_term = math.sqrt(
                    ((level - 1.0) ** 2 - order * order) / (4.0 * (level - 1.0) ** 2 - 1.0)
                )
                current = alpha_term * (cosine * prev_one - beta_term * prev_two)
                legendre[order, :, level] = current
                prev_two = prev_one
                prev_one = current
    order_index = np.arange(degrees)
    lon_index = np.arange(nlon)
    phase_angle = order_index[:, None] * lon_index[None, :] % nlon * (2.0 * math.pi / nlon)
    fourier = np.concatenate([np.cos(phase_angle), np.sin(phase_angle)], axis=0)
    quad_weight = sine_theta * (math.pi / degrees) * (2.0 * math.pi / nlon)
    longitude = lon_index * (2.0 * math.pi / nlon)
    normals = np.stack(
        [
            sine_theta[:, None] * np.cos(longitude)[None, :],
            sine_theta[:, None] * np.sin(longitude)[None, :],
            cosine[:, None] * np.ones((1, nlon)),
        ],
        axis=0,
    )
    return (
        legendre.astype(np.float32),
        fourier.astype(np.float32),
        quad_weight.astype(np.float32),
        normals.astype(np.float32),
    )


def legendre_synth(coeff, legendre):
    batch_size, degrees, _ = coeff.shape
    orders = legendre.shape[0]
    parted = coeff.reshape(batch_size, degrees, 2, orders)
    return jnp.einsum("mjl,nlcm->njcm", legendre, parted, precision=SPECTRAL)


def fourier_synth(partial_legendre, fourier_rows):
    batch_size, nlat, two, orders = partial_legendre.shape
    return jnp.einsum(
        "njw,wk->njk",
        partial_legendre.reshape(batch_size, nlat, two * orders),
        fourier_rows,
        precision=SPECTRAL,
    )


def analysis_fourier(traction_grid, fourier, quad_weight):
    batch_size, nlat, _ = traction_grid.shape
    projected = (
        jnp.einsum("bjk,wk->bjw", traction_grid, fourier, precision=SPECTRAL)
        * quad_weight[None, :, None]
    )
    return projected.reshape(batch_size, nlat, 2, fourier.shape[0] // 2)


def analysis_legendre(coef_grid, legendre):
    batch_size = coef_grid.shape[0]
    result = jnp.einsum("mjl,bjcm->blcm", legendre, coef_grid, precision=SPECTRAL)
    return result.reshape(batch_size, legendre.shape[2], 2 * legendre.shape[0])


def prepare(coeffs, keep_mask):
    degrees = coeffs.shape[2]
    degree_value = jnp.arange(degrees, dtype=jnp.float32)
    shape_part = coeffs[:, 0] * keep_mask
    curvature = (
        shape_part * (degree_value * (degree_value + 1.0) / (degrees * degrees))[None, :, None]
    )
    electric = 3.0 * coeffs[:, 1] * keep_mask
    viscous = 3.0 * coeffs[:, 2] * keep_mask * ((degree_value + 2.0) / degrees)[None, :, None]
    return jnp.stack([shape_part, curvature, electric, viscous], axis=1)


def traction(surface, material):
    radius = jnp.exp(surface[:, 0])
    traction_grid = (
        material[:, 0, None, None] * surface[:, 1]
        + 0.5 * surface[:, 2] * surface[:, 2]
        + 2.0 * material[:, 1, None, None] * surface[:, 3]
    )
    return (radius, traction_grid)


def per_device(
    coeffs, degree, material, split_coeffs, split_material, separation, reader_dev, reader_slot
):
    drop_count, fields, degrees, coef_width = coeffs.shape
    legendre, fourier, quad_weight, normals = spectral_tables(degrees)
    nlat = legendre.shape[1]
    nlon = fourier.shape[1]
    degree_index = jnp.arange(degrees, dtype=jnp.int32)
    order_full = jnp.arange(coef_width, dtype=jnp.int32) % degrees
    order_mask = (degree_index[:, None] >= order_full[None, :]).astype(jnp.float32)
    keep_mask = order_mask[None] * (degree_index[None, :, None] <= degree[:, None, None]).astype(
        jnp.float32
    )
    prepared = prepare(coeffs, keep_mask)
    point_weight = point_table(degrees)
    point_weight = jnp.concatenate(
        [point_weight, jnp.zeros(((fields - 1) * point_weight.shape[0], point_weight.shape[1]))]
    )
    point_surface = jnp.dot(
        (coeffs * keep_mask[:, None]).reshape(drop_count, fields * degrees * coef_width),
        point_weight,
        precision=lax.Precision.DEFAULT,
    )
    own_points = jnp.exp(point_surface).astype(jnp.bfloat16)
    batched = jnp.einsum(
        "mjl,nlcm->mcnj",
        legendre,
        prepared.reshape(drop_count * 4, degrees, 2, degrees),
        precision=SPECTRAL,
    )
    surface = jnp.einsum(
        "mcnj,cmk->njk", batched, fourier.reshape(2, degrees, nlon), precision=SPECTRAL
    ).reshape(drop_count, 4, nlat, nlon)
    radius, traction_grid = traction(surface, material)
    split_count = split_coeffs.shape[0]
    half_width = split_coeffs.shape[3]
    half_orders = half_width // 2
    half_index = lax.axis_index("row") % 2
    pair_start = (
        lax.axis_index("row") // 2 * lax.axis_size("col") + lax.axis_index("col")
    ) * split_count
    own_material = lax.dynamic_slice_in_dim(split_material, pair_start, split_count, 0)
    own_order = half_index * half_orders + jnp.arange(half_width, dtype=jnp.int32) % half_orders
    keep_half = (degree_index[:, None] >= own_order[None, :]).astype(jnp.float32)
    own_legendre = lax.dynamic_slice_in_dim(legendre, half_index * half_orders, half_orders, 0)
    own_fourier = lax.dynamic_slice_in_dim(
        fourier.reshape(2, degrees, nlon), half_index * half_orders, half_orders, 1
    ).reshape(half_width, nlon)
    split_prepared = prepare(split_coeffs, keep_half[None])
    split_legendre = legendre_synth(
        split_prepared.reshape(split_count * 4, degrees, half_width), own_legendre
    )
    partial_surface = fourier_synth(split_legendre, own_fourier)
    split_surface = partial_surface + from_partner(
        partial_surface.astype(jnp.bfloat16), "row", 0
    ).astype(partial_surface.dtype)
    _, split_grid = traction(split_surface.reshape(split_count, 4, nlat, nlon), own_material)
    near_grid = jnp.stack([radius, traction_grid], axis=1).astype(jnp.bfloat16)
    point_count = 4
    target_normal = normals[:, nlat // 4 :: nlat // 2, :: nlon // 2].reshape(3, point_count)
    devices = lax.axis_size("row") * lax.axis_size("col")
    all_points = lax.all_to_all(
        jnp.broadcast_to(own_points.reshape(1, -1), (devices, drop_count * point_count)),
        ("row", "col"),
        split_axis=0,
        concat_axis=0,
        tiled=True,
    ).reshape(devices * drop_count, point_count)
    total_drops = all_points.shape[0]
    readers = reader_dev.shape[1]
    target = (reader_dev * drop_count + reader_slot).reshape(-1)
    pick = (target[:, None] == jnp.arange(total_drops, dtype=jnp.int32)[None, :]).astype(
        jnp.float32
    )
    target_radius = jnp.dot(
        pick, all_points.astype(jnp.float32), precision=lax.Precision.DEFAULT
    )
    target_point = separation.reshape(3, drop_count * readers)[:, :, None] + (
        target_radius[None] * target_normal[:, None, :]
    )
    target_point = jnp.transpose(
        target_point.reshape(3, drop_count, readers * point_count), (1, 2, 0)
    )
    target_square = jnp.sum(target_point * target_point, axis=2) + SOFTENING
    entry_table = jnp.concatenate(
        [
            jnp.transpose(separation, (1, 2, 0)),
            target_radius.reshape(drop_count, readers, point_count),
            target_square.reshape(drop_count, readers, point_count),
        ],
        axis=2,
    ).reshape(-1)
    cell_table = cell_tables(nlat, nlon, point_count)
    partial = near_field(entry_table, near_grid, cell_table, readers, point_count)
    partial, traction_grid = lax.optimization_barrier((partial, traction_grid))
    sums = jnp.sum(partial, axis=3)
    contribution = (
        sums[:, :3] + jnp.transpose(target_point, (0, 2, 1)) * sums[:, 3:]
    ) / (8.0 * math.pi)
    contribution = jnp.transpose(
        contribution.reshape(drop_count, 3, readers, point_count), (0, 2, 1, 3)
    ).reshape(drop_count * readers, 3 * point_count)
    destination = reader_dev.reshape(-1)
    capacity = 2
    onehot = (destination[:, None] == jnp.arange(devices, dtype=jnp.int32)[None, :]).astype(
        jnp.int32
    )
    rank = jnp.sum((jnp.cumsum(onehot, axis=0) - onehot) * onehot, axis=1)
    position = destination * capacity + rank
    place = (position[:, None] == jnp.arange(devices * capacity, dtype=jnp.int32)[None, :]).astype(
        jnp.float32
    )
    record = jnp.concatenate(
        [contribution, reader_slot.reshape(-1, 1).astype(jnp.float32)], axis=1
    )
    outgoing = jnp.dot(jnp.transpose(place), record, precision=lax.Precision.HIGH)
    incoming = lax.all_to_all(
        outgoing.reshape(devices, capacity, record.shape[1]),
        ("row", "col"),
        split_axis=0,
        concat_axis=0,
        tiled=True,
    ).reshape(devices * capacity, record.shape[1])
    slot_pick = (
        incoming[:, -1:] == jnp.arange(drop_count, dtype=jnp.float32)[None, :]
    ).astype(jnp.float32)
    mine = jnp.dot(
        jnp.transpose(slot_pick), incoming[:, :-1], precision=lax.Precision.HIGH
    )
    near_velocity = jnp.transpose(mine.reshape(drop_count, 3, point_count), (1, 0, 2))
    traction_coeffs = (
        analysis_legendre(analysis_fourier(traction_grid, fourier, quad_weight), legendre)
        * keep_mask
    )
    coef_grid = analysis_fourier(split_grid, fourier, quad_weight)
    own_grid = lax.dynamic_slice_in_dim(coef_grid, half_index * half_orders, half_orders, 3)
    split_traction = analysis_legendre(own_grid, own_legendre) * keep_half[None]
    return (traction_coeffs, split_traction, near_velocity.reshape(3, drop_count * point_count))


def point_table(degrees):
    legendre, fourier, _, _ = (np.asarray(t) for t in spectral_tables_np(degrees))
    lat = np.arange(degrees // 4, degrees, degrees // 2)
    lon = np.arange(0, 2 * degrees, degrees)
    orders = np.arange(2 * degrees) % degrees
    table = np.zeros((degrees, 2 * degrees, lat.size * lon.size))
    for i, j in enumerate(lat):
        for k, col in enumerate(lon):
            table[:, :, i * lon.size + k] = (
                legendre[orders, j, :].T.astype(np.float64) * fourier[:, col][None, :]
            )
    return jnp.asarray(table.reshape(degrees * 2 * degrees, -1), dtype=jnp.float32)


def cell_tables(nlat, nlon, point_count):
    theta = (np.arange(nlat) + 0.5) * (math.pi / nlat)
    longitude = np.arange(nlon) * (2.0 * math.pi / nlon)
    quad_weight = (np.sin(theta) * (math.pi / nlat) * (2.0 * math.pi / nlon)).astype(np.float32)
    normals = np.stack(
        [
            np.sin(theta)[:, None] * np.cos(longitude)[None, :],
            np.sin(theta)[:, None] * np.sin(longitude)[None, :],
            np.cos(theta)[:, None] * np.ones((1, nlon)),
        ],
        axis=0,
    ).astype(np.float32)
    points = normals[:, nlat // 4 :: nlat // 2, :: nlon // 2].reshape(3, point_count)
    facing = np.einsum("dp,djk->pjk", points.astype(np.float64), normals.astype(np.float64))
    weight = np.broadcast_to(quad_weight[None, :, None], (1, nlat, nlon))
    table = np.concatenate([normals, facing.astype(np.float32), weight], axis=0)
    return jnp.asarray(table, dtype=jnp.float32)


def near_kernel(points, t_ref, g_ref, c_ref, o_ref, s_ref):
    drop = pl.program_id(0)
    entries = o_ref.shape[2] // points
    width = 3 + 2 * points
    chunks = g_ref.shape[2] // 8
    r = g_ref[0, 0].astype(jnp.float32)
    s_ref[0] = r
    s_ref[1] = r * r
    s_ref[2] = r + r
    s_ref[3] = g_ref[0, 1].astype(jnp.float32) * r * r * c_ref[3 + points]

    def body(e, carry):
        base = (drop * entries + e) * width
        sx = t_ref[base]
        sy = t_ref[base + 1]
        sz = t_ref[base + 2]
        lift = [t_ref[base + 3 + k] for k in range(points)]
        tt = [t_ref[base + 3 + points + k] for k in range(points)]
        acc = [[jnp.zeros((8, 128), jnp.float32) for _ in range(4)] for _ in range(points)]
        for c in range(chunks):
            rows = pl.ds(c * 8, 8)
            nx = c_ref[0, rows, :]
            ny = c_ref[1, rows, :]
            nz = c_ref[2, rows, :]
            rr = s_ref[0, rows, :]
            r2 = s_ref[1, rows, :]
            twice = s_ref[2, rows, :]
            load = s_ref[3, rows, :]
            shared = sx * nx + sy * ny + sz * nz
            for k in range(points):
                along = shared + lift[k] * c_ref[3 + k, rows, :]
                soft = (tt[k] + r2) - twice * along
                inv = lax.rsqrt(soft)
                w = load * (inv * inv * inv)
                dn = along - rr
                h = w * ((soft + SOFTENING) - dn * rr)
                hx, hy, hz, sq = acc[k]
                acc[k] = [hx + h * nx, hy + h * ny, hz + h * nz, sq + w * dn]
        for k in range(points):
            row = pl.ds(e * points + k, 1)
            for comp in range(4):
                o_ref[0, comp, row, :] = jnp.sum(acc[k][comp], axis=0, keepdims=True)
        return carry

    lax.fori_loop(0, entries, body, 0)


def near_field(entry_table, near_grid, cell_table, readers, points):
    drops, fields, nlat, nlon = near_grid.shape
    targets = readers * points
    cells = drops * targets * nlat * nlon
    return pl.pallas_call(
        functools.partial(near_kernel, points),
        grid=(drops,),
        in_specs=[
            pl.BlockSpec(memory_space=pltpu.SMEM),
            pl.BlockSpec((1, fields, nlat, nlon), lambda s: (s, 0, 0, 0)),
            pl.BlockSpec(cell_table.shape, lambda s: (0, 0, 0)),
        ],
        out_specs=pl.BlockSpec((1, 4, targets, nlon), lambda s: (s, 0, 0, 0)),
        out_shape=jax.ShapeDtypeStruct((drops, 4, targets, nlon), jnp.float32),
        scratch_shapes=[pltpu.VMEM((4, nlat, nlon), jnp.float32)],
        cost_estimate=pl.CostEstimate(
            flops=24 * cells, transcendentals=cells, bytes_accessed=2 * drops * fields * nlat * nlon
        ),
    )(entry_table, near_grid, cell_table)


def solution(mesh):
    in_specs = (
        P(("row", "col"), None, None, None),
        P(("row", "col")),
        P(("row", "col"), None),
        P(("row", "col"), None, None, None),
        P(),
        P(None, ("row", "col"), None),
        P(("row", "col"), None),
        P(("row", "col"), None),
    )
    out_specs = (
        P(("row", "col"), None, None),
        P(("row", "col"), None, None),
        P(None, ("row", "col")),
    )
    return jax.shard_map(
        per_device, mesh=mesh, in_specs=in_specs, out_specs=out_specs, check_vma=False
    )
```
